512 devices in a mesh: req: 64 (over z, x, core), tp: 8 (over y).
Axes of the slice: x: 4, y: 8, z: 8, core: 2. Of those that a mesh axis runs over, the one named last changes fastest.
Arguments:
- gate_in: bfloat16 [2, 4096, 4096], P(None, 'req', 'tp'), may hold values from -6 to 6
- mix_in: bfloat16 [2, 4096, 4096], P(None, 'req', 'tp'), may hold values from -6 to 6
- keys_in: bfloat16 [2, 4096, 256], P(None, 'req'), may hold values from -6 to 6
- step_in: bfloat16 [2, 4096, 64], P(None, 'req', 'tp'), may hold values from -6 to 6
- resid_in: bfloat16 [2, 4096, 2048], P(None, 'req', 'tp'), may hold values from -12 to 12
- kernel_mix: float32 [2, 4, 4096], P(None, None, 'tp'), may hold values from -3 to 3
- kernel_keys: float32 [2, 4, 256], replicated, may hold values from -3 to 3
- step_bias: float32 [2, 64], P(None, 'tp'), may hold values from -4 to 0
- decay_rate: float32 [2, 64], P(None, 'tp'), may hold values from 0.02 to 2
- skip_gain: float32 [2, 64], P(None, 'tp'), may hold values from 0.5 to 1.5
- norm_gain: float32 [2, 4096], P(None, 'tp'), may hold values from 0.5 to 1.5
- final_gain: float32 [2, 2048], replicated, may hold values from 0.5 to 1.5
- out_weight: bfloat16 [2, 4096, 2048], P(None, 'tp', 'req'), may hold values from -0.09375 to 0.09375
- head_weight: bfloat16 [2, 25600, 2048], P(None, 'req'), may hold values from -8 to 8
- history_mix: bfloat16 [2, 192, 3, 4096], P(None, 'req', None, 'tp'), may hold values from -6 to 6
- history_keys: bfloat16 [2, 192, 3, 256], P(None, 'req'), may hold values from -6 to 6
- start_state: bfloat16 [2, 192, 4096, 128], P(None, 'req', 'tp'), may hold values from -0.59765625 to 0.59765625
- lengths: int32 [64, 3], P('req'), may hold values from 1 to 32, 64 in all within a row
- continued: int32 [64, 3], P('req'), may hold values 0 or 1
- targets: int32 [4096], P('req'), may hold values from 0 to 25599
- score_flag: int32 [4096], P('req'), may hold values 0 or 1
Outputs:
- logprobs: float32 [2, 4096], P(None, ('req', 'tp'))
The draws below stay inside these ranges and needn't reach their ends.
Inputs may be any that keep to these rules, and one draw needn't show every extreme that they name: The 3 lengths of a row fill its 64 slots exactly.
All inputs are finite; a program needn't handle non-finite values. No bound on the sum of `continued` or of `score_flag` on one device may be relied on, other than what follows from the above.
Results may differ from the reference program's by a relative error of at most 0.00075.
Values may be sent and summed in bfloat16 or wider, within the bound.
No kernel may reach another device: no remote copies, remote signals or barrier semaphores. Data moves between devices by JAX's collectives and lax.ppermute only.
A program may use at most 64 MiB of HBM per device.

```python
import math
import jax
import jax.numpy as jnp
import numpy as np
from jax import lax

D = 2048
INNER = 4096
HEADS = 64
STATE = 128
VOCAB = 25600
CONV = 4
MODELS = 2
TOK_DEV = 64
REQ_DEV = 3
TOKENS = 4096
REQS = 192
N_REQ = 64


def common_signs(key):
    picks = jax.random.randint(jax.random.fold_in(key, 7), (D,), 0, 2)
    return jnp.where(picks == 1, 1.0, -1.0).astype(jnp.float32)


def draw_resid_in(key, part):
    signs = common_signs(key)
    base = jnp.clip(jax.random.normal(jax.random.fold_in(key, 1), (MODELS, TOKENS, D), jnp.float32), -6.0, 6.0)
    chosen = jax.random.randint(jax.random.fold_in(key, 2), (MODELS, TOKENS, 1), 0, 16) == 0
    aligned = 8.0 * signs[None, None, :] + 0.3 * base
    return jnp.where(chosen, aligned, base).astype(jnp.bfloat16)


def draw_head_weight(key, part):
    signs = common_signs(key)
    base = 0.07 * jnp.clip(jax.random.normal(jax.random.fold_in(key, 1), (MODELS, VOCAB, D), jnp.float32), -6.0, 6.0)
    level = 150.0
    stride = VOCAB // 8
    offset_row = jax.random.randint(jax.random.fold_in(key, 3), (), 0, stride)
    rows = jnp.arange(VOCAB, dtype=jnp.int32)
    strong = rows % stride == offset_row
    rank = (rows // stride).astype(jnp.float32)
    amplitude = (level + 2.0 * rank) / D
    aligned = amplitude[None, :, None] * signs[None, None, :] + 0.3 * base
    return jnp.where(strong[None, :, None], aligned, base).astype(jnp.bfloat16)


def place_ends(values, key, low, largest):
    spot = [jax.random.randint(jax.random.fold_in(key, axis), (), 0, length) for axis, length in enumerate(values.shape)]
    main_axis = values.shape.index(max(values.shape))
    neighbour = spot[:main_axis] + [(spot[main_axis] + 1) % values.shape[main_axis]] + spot[main_axis + 1:]
    return values.at[tuple(spot)].set(low).at[tuple(neighbour)].set(largest)


def steps_of(rng, dims, shards, low, high):
    loudness = 1.0
    for position, shards_of in shards:
        draws = jax.random.uniform(jax.random.fold_in(jax.random.fold_in(rng, 6), position), (shards_of,), jnp.float32, low / len(shards), high / len(shards))
        loudness = loudness * jnp.repeat(jnp.exp(draws), dims[position] // shards_of).reshape((-1,) + (1,) * (len(dims) - 1 - position))
    return loudness


def rank_table(number_of, skew):
    loads = [(1 << 20) // math.isqrt(grade ** skew) + 1 for grade in range(1, number_of + 1)]
    width = 1 + sum(loads) // (1 << 30)
    return np.cumsum(np.array([max(1, weight // width) for weight in loads]))


def ranked_ids(own_key, shape, count, slope):
    grid = rank_table(count, slope)
    ticket = jax.random.randint(jax.random.fold_in(own_key, 1), shape, 0, int(grid[count - 1]))
    rank = jnp.searchsorted(jnp.asarray(grid, jnp.int32), ticket, side="right")
    return jax.random.permutation(jax.random.fold_in(own_key, 2), count)[rank].astype(jnp.int32)


def split_up(count, total, most, lean):
    portions = [(1 << 20) // math.isqrt(grade ** lean) + 1 for grade in range(2, count + 1)]
    surplus, counts = total - most - (count - 1), [1] * (count - 1)
    while surplus > 0:
        movable = [i for i in range(count - 1) if counts[i] < most]
        whole, left = sum([portions[i] for i in movable]), surplus
        for i in movable:
            addition = min(most - counts[i], max(1, left * portions[i] // whole), surplus)
            counts[i] = counts[i] + addition
            surplus = surplus - addition
    return np.array([most] + counts)


def uneven(stream_key, amount, total, bound, lean):
    if amount == 2:
        one = jax.random.randint(stream_key, (), max(1, total - bound), min(bound, total - 1) + 1)
        return jnp.stack([one, total - one])
    sizes = jnp.asarray(split_up(amount, total, bound, lean), jnp.int32)
    pairs = (amount - 1) // 2
    source_of, taker = sizes[1:1 + 2 * pairs:2], sizes[2:2 + 2 * pairs:2]
    slack = jnp.minimum(source_of - 1, bound - taker)
    moved = jax.random.randint(jax.random.fold_in(stream_key, 1), (pairs,), 0, 1 << 20) % (slack + 1)
    sizes = sizes.at[1:1 + 2 * pairs:2].set(source_of - moved).at[2:2 + 2 * pairs:2].set(taker + moved)
    return sizes[jax.random.permutation(jax.random.fold_in(stream_key, 2), amount)]


def noise(key, dims, scale, most, shards=(), kind=jnp.bfloat16):
    entries = scale * jax.random.normal(key, dims, jnp.float32)
    if shards:
        entries = entries * steps_of(key, dims, shards, -0.22, 0.18)
    return jnp.clip(entries, -most, most).astype(kind)


def setup_inputs(seed: int = 0) -> dict:
    streams_of = jax.random.split(jax.random.key(seed), 22)
    gate_in = noise(streams_of[0], (MODELS, TOKENS, INNER), 1.0, 6.0, ((1, 64), (2, 8)))
    mix_in = noise(streams_of[1], (MODELS, TOKENS, INNER), 1.0, 6.0, ((1, 64), (2, 8)))
    keys_in = noise(streams_of[2], (MODELS, TOKENS, 2 * STATE), 1.0, 6.0, ((1, 64),))
    step_in = noise(streams_of[3], (MODELS, TOKENS, HEADS), 1.0, 6.0, ((1, 64), (2, 8)))
    resid_in = draw_resid_in(jax.random.fold_in(streams_of[21], 71), 0)
    kernel_mix = noise(streams_of[5], (MODELS, CONV, INNER), CONV ** -0.5, 3.0, ((2, 8),), jnp.float32)
    kernel_keys = noise(streams_of[6], (MODELS, CONV, 2 * STATE), CONV ** -0.5, 3.0, (), jnp.float32)
    step_bias = jnp.clip(-4.0 + 4.0 * jax.random.uniform(streams_of[7], (MODELS, HEADS), jnp.float32) ** steps_of(streams_of[7], (MODELS, HEADS), ((1, 8),), -0.2, 0.2), -4.0, 0.0)
    decay_rate = jnp.clip(jnp.exp(math.log(2.0) - 4.6051702 * jax.random.uniform(streams_of[8], (MODELS, HEADS), jnp.float32) ** steps_of(streams_of[8], (MODELS, HEADS), ((1, 8),), -0.2, 0.2)), 0.02, 2.0)
    skip_gain = jnp.clip(0.5 + 1.0 * jax.random.uniform(streams_of[9], (MODELS, HEADS), jnp.float32) ** steps_of(streams_of[9], (MODELS, HEADS), ((1, 8),), -0.2, 0.2), 0.5, 1.5)
    norm_gain = jnp.clip(1.0 + 0.1 * jax.random.normal(streams_of[10], (MODELS, INNER), jnp.float32), 0.5, 1.5)
    final_gain = jnp.clip(1.0 + 0.1 * jax.random.normal(streams_of[11], (MODELS, D), jnp.float32), 0.5, 1.5)
    out_weight = noise(streams_of[12], (MODELS, INNER, D), INNER ** -0.5, 0.09375, ((1, 8), (2, 64)))
    head_weight = draw_head_weight(jax.random.fold_in(streams_of[21], 71), 0)
    history_mix = noise(streams_of[14], (MODELS, REQS, CONV - 1, INNER), 1.0, 6.0, ((1, 64), (3, 8)))
    history_keys = noise(streams_of[15], (MODELS, REQS, CONV - 1, 2 * STATE), 1.0, 6.0, ((1, 64),))
    start_state = noise(streams_of[16], (MODELS, REQS, INNER, STATE), 0.1, 0.59765625, ((1, 64), (2, 8)))
    lengths = jax.vmap(lambda own: uneven(own, REQ_DEV, TOK_DEV, TOK_DEV // 2, 2))(jax.random.split(streams_of[17], N_REQ)).reshape((N_REQ, REQ_DEV)).astype(jnp.int32)
    continued = place_ends((jax.random.randint(streams_of[18], (N_REQ, REQ_DEV), 0, 2) < 1).astype(jnp.int32), jax.random.fold_in(streams_of[18], 1), 0, 1)
    targets = place_ends(ranked_ids(streams_of[19], (TOKENS,), VOCAB, 2), jax.random.fold_in(streams_of[19], 3), 0, VOCAB - 1).astype(jnp.int32)
    score_flag = place_ends((jax.random.randint(streams_of[20], (TOKENS,), 0, 4) < 3).astype(jnp.int32), jax.random.fold_in(streams_of[20], 1), 0, 1)
    return {"gate_in": gate_in, "mix_in": mix_in, "keys_in": keys_in, "step_in": step_in, "resid_in": resid_in, "kernel_mix": kernel_mix, "kernel_keys": kernel_keys, "step_bias": step_bias, "decay_rate": decay_rate, "skip_gain": skip_gain, "norm_gain": norm_gain, "final_gain": final_gain, "out_weight": out_weight, "head_weight": head_weight, "history_mix": history_mix, "history_keys": history_keys, "start_state": start_state, "lengths": lengths, "continued": continued, "targets": targets, "score_flag": score_flag}


EPSILON = 1e-05
PRECISE = lax.Precision.HIGHEST

def request_layout(lengths, step_count):
    lengths = lengths.astype(jnp.int32)
    starts = (jnp.cumsum(lengths) - lengths).astype(jnp.int32)
    time_index = jnp.arange(step_count, dtype=jnp.int32)
    segment = lax.optimization_barrier(jnp.sum((time_index[:, None] >= starts[None, 1:]).astype(jnp.int32), axis=1)).astype(jnp.int32)
    member = segment[:, None] == jnp.arange(lengths.shape[0], dtype=jnp.int32)[None, :]
    first_step = lax.optimization_barrier(jnp.sum(jnp.where(member, starts[None, :], 0), axis=1)).astype(jnp.int32)
    return (starts, segment, member, time_index - first_step)

def causal_conv(stream, kernel, history, member, offset):
    tap_count = kernel.shape[0]
    history_len = tap_count - 1
    current = stream.astype(jnp.float32)
    member_bf = member.astype(jnp.bfloat16)
    slot_values = [jnp.dot(member_bf, history[:, slot_index, :], preferred_element_type=jnp.float32) for slot_index in range(history_len)]
    output = kernel[history_len][None, :] * current
    for lag_steps in range(1, tap_count):
        shifted = jnp.concatenate([jnp.zeros((lag_steps, current.shape[1]), current.dtype), current[:-lag_steps]], axis=0)
        earlier = jnp.zeros_like(current)
        for slot_index in range(history_len):
            earlier = earlier + jnp.where((offset - lag_steps == slot_index - history_len)[:, None], slot_values[slot_index], 0.0)
        output = output + kernel[history_len - lag_steps][None, :] * jnp.where((offset >= lag_steps)[:, None], shifted, earlier)
    return jax.nn.silu(output)

def mixer_block(gate_rows, mix_rows, keys_rows, step_raw, kernel_mix, kernel_keys, step_bias, decay_rate, skip_gain, history_mix, history_keys, start_state, lengths, continued):
    step_count = gate_rows.shape[0]
    head_count = step_raw.shape[1]
    inner_width = mix_rows.shape[1]
    head_size = inner_width // head_count
    states = start_state.shape[2]
    starts, segment, member, offset = request_layout(lengths, step_count)
    keep_state = continued.astype(jnp.bfloat16)
    mixed = causal_conv(mix_rows, kernel_mix, history_mix * keep_state[:, None, None], member, offset)
    projected = causal_conv(keys_rows, kernel_keys, history_keys * keep_state[:, None, None], member, offset)
    inject = projected[:, :states]
    readout = projected[:, states:]
    step_size = jax.nn.softplus(step_raw.astype(jnp.float32) + step_bias[None, :])
    log_decay = -step_size * decay_rate[None, :]
    running = jnp.cumsum(log_decay, axis=0)
    time_index = jnp.arange(step_count, dtype=jnp.int32)
    causal = (segment[:, None] == segment[None, :]) & (time_index[:, None] >= time_index[None, :])
    spread = jnp.minimum(running[:, None, :] - running[None, :, :], 0.0)
    transfer = jnp.where(causal[:, :, None], jnp.exp(spread), 0.0)
    intersection = jnp.dot(readout, inject.T, precision=PRECISE)
    kernel_full = transfer * intersection[:, :, None]
    values = mixed.reshape(step_count, head_count, head_size)
    output = jnp.einsum('tsh,shp->thp', kernel_full, step_size[:, :, None] * values, precision=PRECISE)
    before = jnp.take(running - log_decay, starts, axis=0)
    member_float = member.astype(jnp.float32)
    entry_level = jnp.dot(member_float, before, precision=PRECISE)
    carried = jnp.exp(jnp.minimum(running - entry_level, 0.0))
    initial = start_state.astype(jnp.float32) * keep_state.astype(jnp.float32)[:, None, None]
    readings = jnp.einsum('tn,rcn->trc', readout, initial, precision=PRECISE)
    chosen = lax.optimization_barrier(jnp.sum(member_float[:, :, None] * readings, axis=1)).reshape(step_count, head_count, head_size)
    output = output + carried[:, :, None] * chosen + skip_gain[None, :, None] * values
    return output.reshape(step_count, inner_width) * jax.nn.silu(gate_rows.astype(jnp.float32))

def reference(gate_in, mix_in, keys_in, step_in, resid_in, kernel_mix, kernel_keys, step_bias, decay_rate, skip_gain, norm_gain, final_gain, out_weight, head_weight, history_mix, history_keys, start_state, lengths, continued, targets, score_flag):

    def per_block(array):
        return jnp.swapaxes(array.reshape((MODELS, N_REQ, TOK_DEV) + array.shape[2:]), 0, 1)

    def per_request(array):
        return jnp.swapaxes(array.reshape((MODELS, N_REQ, REQ_DEV) + array.shape[2:]), 0, 1)

    def score_block(block_args):
        gate_rows, mix_rows, keys_rows, step_rows, resid_rows, length_row, continued_row, state_mix, state_keys, state_ssm, target_row, flag_row = block_args
        results = []
        for model_index in range(MODELS):
            gated = mixer_block(gate_rows[model_index], mix_rows[model_index], keys_rows[model_index], step_rows[model_index], kernel_mix[model_index], kernel_keys[model_index], step_bias[model_index], decay_rate[model_index], skip_gain[model_index], state_mix[model_index], state_keys[model_index], state_ssm[model_index], length_row, continued_row)
            squares = lax.optimization_barrier(jnp.sum(gated * gated, axis=1))
            normed = (gated * lax.rsqrt(squares / INNER + EPSILON)[:, None] * norm_gain[model_index][None, :]).astype(jnp.bfloat16)
            update = jnp.dot(normed, out_weight[model_index], preferred_element_type=jnp.float32)
            hidden = (resid_rows[model_index].astype(jnp.float32) + update).astype(jnp.bfloat16)
            hidden_float = hidden.astype(jnp.float32)
            final_squares = lax.optimization_barrier(jnp.sum(hidden_float * hidden_float, axis=1))
            final_rows = (hidden_float * lax.rsqrt(final_squares / D + EPSILON)[:, None] * final_gain[model_index][None, :]).astype(jnp.bfloat16)
            logits = jnp.dot(final_rows, head_weight[model_index].T, preferred_element_type=jnp.float32)
            peak_logit = lax.optimization_barrier(jnp.max(logits, axis=1))
            normalizer = peak_logit + jnp.log(lax.optimization_barrier(jnp.sum(jnp.exp(logits - peak_logit[:, None]), axis=1)))
            picked = jnp.take_along_axis(logits, target_row[:, None].astype(jnp.int32), axis=1)[:, 0]
            results.append((picked - normalizer) * flag_row.astype(jnp.float32))
        return jnp.stack(results)
    block_inputs = (per_block(gate_in), per_block(mix_in), per_block(keys_in), per_block(step_in), per_block(resid_in), lengths, continued, per_request(history_mix), per_request(history_keys), per_request(start_state), targets.reshape(N_REQ, TOK_DEV), score_flag.reshape(N_REQ, TOK_DEV))
    scored = lax.map(score_block, block_inputs)
    return jnp.swapaxes(scored, 0, 1).reshape(MODELS, TOKENS)
```

```python
import jax
import jax.numpy as jnp
from jax import lax
from jax.sharding import PartitionSpec as P

EPSILON = 1e-05
PRECISE = lax.Precision.HIGHEST


def merged_2(part, axis, combine):
    gathered = jax.tree.map(lambda a: lax.all_gather(a, axis), part)

    def take(source):
        return jax.tree.map(lambda a: lax.dynamic_index_in_dim(a, source, 0, False), gathered)

    return lax.fori_loop(
        1, lax.axis_size(axis), lambda source, state: combine(state, take(source)), take(0)
    )


def request_layout(lengths, step_count):
    starts = jnp.cumsum(lengths) - lengths
    time_index = jnp.arange(step_count, dtype=jnp.int32)
    segment = jnp.sum((time_index[:, None] >= starts[None, 1:]).astype(jnp.int32), axis=1)
    member = segment[:, None] == jnp.arange(lengths.shape[0], dtype=jnp.int32)[None, :]
    first_step = jnp.sum(jnp.where(member, starts[None, :], 0), axis=1)
    return (starts, segment, member, time_index - first_step)


def causal_conv(stream, kernel, history, member, offset):
    tap_count = kernel.shape[0]
    history_len = tap_count - 1
    current = stream.astype(jnp.float32)
    member_bf = member.astype(jnp.bfloat16)
    slot_values = [
        jnp.dot(member_bf, history[:, slot_index, :], preferred_element_type=jnp.float32)
        for slot_index in range(history_len)
    ]
    output = kernel[history_len][None, :] * current
    for lag_steps in range(1, tap_count):
        shifted = jnp.concatenate(
            [jnp.zeros((lag_steps, current.shape[1]), current.dtype), current[:-lag_steps]], axis=0
        )
        earlier = jnp.zeros_like(current)
        for slot_index in range(history_len):
            earlier = earlier + jnp.where(
                (offset - lag_steps == slot_index - history_len)[:, None],
                slot_values[slot_index],
                0.0,
            )
        output = output + kernel[history_len - lag_steps][None, :] * jnp.where(
            (offset >= lag_steps)[:, None], shifted, earlier
        )
    return jax.nn.silu(output)


def mixer_block(
    gate_rows,
    mix_rows,
    keys_rows,
    step_raw,
    kernel_mix,
    kernel_keys,
    step_bias,
    decay_rate,
    skip_gain,
    history_mix,
    history_keys,
    start_state,
    lengths,
    continued,
):
    step_count = gate_rows.shape[0]
    head_count = step_raw.shape[1]
    inner_width = mix_rows.shape[1]
    head_size = inner_width // head_count
    states = start_state.shape[2]
    starts, segment, member, offset = request_layout(lengths, step_count)
    keep_state = continued.astype(jnp.bfloat16)
    mixed = causal_conv(
        mix_rows, kernel_mix, history_mix * keep_state[:, None, None], member, offset
    )
    projected = causal_conv(
        keys_rows, kernel_keys, history_keys * keep_state[:, None, None], member, offset
    )
    inject = projected[:, :states]
    readout = projected[:, states:]
    step_size = jax.nn.softplus(step_raw.astype(jnp.float32) + step_bias[None, :])
    log_decay = -step_size * decay_rate[None, :]
    running = jnp.cumsum(log_decay, axis=0)
    time_index = jnp.arange(step_count, dtype=jnp.int32)
    causal = (segment[:, None] == segment[None, :]) & (time_index[:, None] >= time_index[None, :])
    spread = jnp.minimum(running[:, None, :] - running[None, :, :], 0.0)
    transfer = jnp.where(causal[:, :, None], jnp.exp(spread), 0.0)
    intersection = jnp.dot(readout, inject.T, precision=PRECISE)
    kernel_full = transfer * intersection[:, :, None]
    values = mixed.reshape(step_count, head_count, head_size)
    output = jnp.einsum(
        "tsh,shp->thp", kernel_full, step_size[:, :, None] * values, precision=PRECISE
    )
    before = jnp.take(running - log_decay, starts, axis=0)
    member_float = member.astype(jnp.float32)
    entry_level = jnp.dot(member_float, before, precision=PRECISE)
    carried = jnp.exp(jnp.minimum(running - entry_level, 0.0))
    initial = start_state.astype(jnp.float32) * keep_state.astype(jnp.float32)[:, None, None]
    readings = jnp.einsum("tn,rcn->trc", readout, initial, precision=PRECISE)
    chosen = jnp.sum(member_float[:, :, None] * readings, axis=1).reshape(
        step_count, head_count, head_size
    )
    output = output + carried[:, :, None] * chosen + skip_gain[None, :, None] * values
    return output.reshape(step_count, inner_width) * jax.nn.silu(gate_rows.astype(jnp.float32))


def head_scores(head_weight, vocab_start, rows_hidden, rows_target):
    logits = jnp.einsum(
        "mnd,mvd->mnv", rows_hidden, head_weight, preferred_element_type=jnp.float32
    )
    peak_logit = jnp.max(logits, axis=2)
    spread = jnp.sum(jnp.exp(logits - peak_logit[:, :, None]), axis=2)
    local_id = rows_target - vocab_start
    matches = jnp.arange(head_weight.shape[1], dtype=jnp.int32)[None, :] == local_id[:, None]
    picked = jnp.sum(jnp.where(matches[None, :, :], logits, 0.0), axis=2)
    return jnp.stack([peak_logit, spread, picked])


STATS_BY_ALL_TO_ALL = True
DIGIT = 256


def local(
    gate_in,
    mix_in,
    keys_in,
    step_in,
    resid_in,
    kernel_mix,
    kernel_keys,
    step_bias,
    decay_rate,
    skip_gain,
    norm_gain,
    final_gain,
    out_weight,
    head_weight,
    history_mix,
    history_keys,
    start_state,
    lengths,
    continued,
    targets,
    score_flag,
):
    groups = lax.axis_size("tp")
    shards = lax.axis_size("req")
    lane_index = lax.axis_index("tp")
    shard_index = lax.axis_index("req")
    models = gate_in.shape[0]
    step_count = gate_in.shape[1]
    row_count = step_count // groups
    gated = jnp.stack(
        [
            mixer_block(
                gate_in[model_index],
                mix_in[model_index],
                keys_in[model_index],
                step_in[model_index],
                kernel_mix[model_index],
                kernel_keys[model_index],
                step_bias[model_index],
                decay_rate[model_index],
                skip_gain[model_index],
                history_mix[model_index],
                history_keys[model_index],
                start_state[model_index],
                lengths[0],
                continued[0],
            )
            for model_index in range(models)
        ]
    )
    squares = lax.psum(jnp.sum(gated * gated, axis=2), "tp")
    inner_width = gated.shape[2] * groups
    normed = (
        gated * lax.rsqrt(squares / inner_width + EPSILON)[:, :, None] * norm_gain[:, None, :]
    ).astype(jnp.bfloat16)
    partial_out = jnp.einsum(
        "mtc,mcd->mtd",
        normed,
        lax.all_gather(out_weight, "req", axis=2, tiled=True),
        preferred_element_type=jnp.float32,
    )
    update = lax.psum_scatter(partial_out, "tp", scatter_dimension=1, tiled=True)
    resid_rows = lax.all_to_all(resid_in, "tp", split_axis=1, concat_axis=2, tiled=True)
    hidden = (resid_rows.astype(jnp.float32) + update).astype(jnp.bfloat16)
    full_width = hidden.shape[2]
    hidden_float = hidden.astype(jnp.float32)
    final_squares = jnp.sum(hidden_float * hidden_float, axis=2)
    final_rows = (
        hidden_float
        * lax.rsqrt(final_squares / full_width + EPSILON)[:, :, None]
        * final_gain[:, None, :]
    ).astype(jnp.bfloat16)
    own_target = lax.dynamic_slice_in_dim(targets, lane_index * row_count, row_count, 0)
    high_digit = (own_target // DIGIT).astype(jnp.bfloat16)
    low_digit = (own_target % DIGIT).astype(jnp.bfloat16)
    target_row = jnp.zeros((1, full_width), jnp.bfloat16)
    target_row = target_row.at[0, :row_count].set(high_digit)
    target_row = target_row.at[0, row_count : 2 * row_count].set(low_digit)
    packet = jnp.concatenate([final_rows.reshape(models * row_count, full_width), target_row], axis=0)
    every = lax.all_gather(packet, "req", axis=0, tiled=False)
    every_rows = (
        every[:, : models * row_count]
        .reshape(shards, models, row_count, full_width)
        .transpose(1, 0, 2, 3)
        .reshape(models, shards * row_count, full_width)
    )
    every_target = (
        every[:, models * row_count, :row_count].astype(jnp.int32) * DIGIT
        + every[:, models * row_count, row_count : 2 * row_count].astype(jnp.int32)
    ).reshape(shards * row_count)
    vocab_part = head_weight.shape[1]
    statistics = head_scores(head_weight, shard_index * vocab_part, every_rows, every_target)
    if STATS_BY_ALL_TO_ALL:
        received = lax.all_to_all(
            statistics.reshape(3, models, shards, row_count), "req", split_axis=2, concat_axis=2, tiled=True
        )
    else:
        gathered = lax.all_gather(statistics, "req", axis=2, tiled=False)
        received = lax.dynamic_slice_in_dim(
            gathered.reshape(3, models, shards, shards, row_count), shard_index, 1, 3
        ).reshape(3, models, shards, row_count)
    peak_each, spread_each, picked_each = received[0], received[1], received[2]
    peak_logit = jnp.max(peak_each, axis=1)
    spread = jnp.sum(spread_each * jnp.exp(peak_each - peak_logit[:, None, :]), axis=1)
    picked = jnp.sum(picked_each, axis=1)
    scored_rows = lax.dynamic_slice_in_dim(score_flag, lane_index * row_count, row_count, 0).astype(
        jnp.float32
    )
    return (picked - (peak_logit + jnp.log(spread))) * scored_rows[None, :]


def solution(mesh):
    placed = (
        P(None, "req", "tp"),
        P(None, "req", "tp"),
        P(None, "req", None),
        P(None, "req", "tp"),
        P(None, "req", "tp"),
        P(None, None, "tp"),
        P(),
        P(None, "tp"),
        P(None, "tp"),
        P(None, "tp"),
        P(None, "tp"),
        P(),
        P(None, "tp", "req"),
        P(None, "req", None),
        P(None, "req", None, "tp"),
        P(None, "req", None, None),
        P(None, "req", "tp", None),
        P("req", None),
        P("req", None),
        P("req"),
        P("req"),
    )
    return jax.shard_map(
        local, mesh=mesh, in_specs=placed, out_specs=P(None, ("req", "tp")), check_vma=False
    )
```

```python
import jax
import jax.numpy as jnp
from jax import lax
from jax.sharding import PartitionSpec as P

EPSILON = 1e-05
PRECISE = lax.Precision.HIGHEST


def merged_2(part, axis, combine):
    gathered = jax.tree.map(lambda a: lax.all_gather(a, axis), part)

    def take(source):
        return jax.tree.map(lambda a: lax.dynamic_index_in_dim(a, source, 0, False), gathered)

    return lax.fori_loop(
        1, lax.axis_size(axis), lambda source, state: combine(state, take(source)), take(0)
    )


def request_layout(lengths, step_count):
    starts = jnp.cumsum(lengths) - lengths
    time_index = jnp.arange(step_count, dtype=jnp.int32)
    segment = jnp.sum((time_index[:, None] >= starts[None, 1:]).astype(jnp.int32), axis=1)
    member = segment[:, None] == jnp.arange(lengths.shape[0], dtype=jnp.int32)[None, :]
    first_step = jnp.sum(jnp.where(member, starts[None, :], 0), axis=1)
    return (starts, segment, member, time_index - first_step)


def causal_conv(stream, kernel, history, member, offset):
    tap_count = kernel.shape[0]
    history_len = tap_count - 1
    current = stream.astype(jnp.float32)
    member_bf = member.astype(jnp.bfloat16)
    slot_values = [
        jnp.dot(member_bf, history[:, slot_index, :], preferred_element_type=jnp.float32)
        for slot_index in range(history_len)
    ]
    output = kernel[history_len][None, :] * current
    for lag_steps in range(1, tap_count):
        shifted = jnp.concatenate(
            [jnp.zeros((lag_steps, current.shape[1]), current.dtype), current[:-lag_steps]], axis=0
        )
        earlier = jnp.zeros_like(current)
        for slot_index in range(history_len):
            earlier = earlier + jnp.where(
                (offset - lag_steps == slot_index - history_len)[:, None],
                slot_values[slot_index],
                0.0,
            )
        output = output + kernel[history_len - lag_steps][None, :] * jnp.where(
            (offset >= lag_steps)[:, None], shifted, earlier
        )
    return jax.nn.silu(output)


def mixer_block(
    gate_rows,
    mix_rows,
    keys_rows,
    step_raw,
    kernel_mix,
    kernel_keys,
    step_bias,
    decay_rate,
    skip_gain,
    history_mix,
    history_keys,
    start_state,
    lengths,
    continued,
):
    step_count = gate_rows.shape[0]
    head_count = step_raw.shape[1]
    inner_width = mix_rows.shape[1]
    head_size = inner_width // head_count
    states = start_state.shape[2]
    starts, segment, member, offset = request_layout(lengths, step_count)
    keep_state = continued.astype(jnp.bfloat16)
    mixed = causal_conv(
        mix_rows, kernel_mix, history_mix * keep_state[:, None, None], member, offset
    )
    projected = causal_conv(
        keys_rows, kernel_keys, history_keys * keep_state[:, None, None], member, offset
    )
    inject = projected[:, :states]
    readout = projected[:, states:]
    step_size = jax.nn.softplus(step_raw.astype(jnp.float32) + step_bias[None, :])
    log_decay = -step_size * decay_rate[None, :]
    running = jnp.cumsum(log_decay, axis=0)
    time_index = jnp.arange(step_count, dtype=jnp.int32)
    causal = (segment[:, None] == segment[None, :]) & (time_index[:, None] >= time_index[None, :])
    spread = jnp.minimum(running[:, None, :] - running[None, :, :], 0.0)
    transfer = jnp.where(causal[:, :, None], jnp.exp(spread), 0.0)
    intersection = jnp.dot(readout, inject.T, precision=PRECISE)
    kernel_full = transfer * intersection[:, :, None]
    values = mixed.reshape(step_count, head_count, head_size)
    output = jnp.einsum(
        "tsh,shp->thp", kernel_full, step_size[:, :, None] * values, precision=PRECISE
    )
    before = jnp.take(running - log_decay, starts, axis=0)
    member_float = member.astype(jnp.float32)
    entry_level = jnp.dot(member_float, before, precision=PRECISE)
    carried = jnp.exp(jnp.minimum(running - entry_level, 0.0))
    initial = start_state.astype(jnp.float32) * keep_state.astype(jnp.float32)[:, None, None]
    readings = jnp.einsum("tn,rcn->trc", readout, initial, precision=PRECISE)
    chosen = jnp.sum(member_float[:, :, None] * readings, axis=1).reshape(
        step_count, head_count, head_size
    )
    output = output + carried[:, :, None] * chosen + skip_gain[None, :, None] * values
    return output.reshape(step_count, inner_width) * jax.nn.silu(gate_rows.astype(jnp.float32))


def head_scores(head_weight, vocab_start, rows_hidden, rows_target):
    logits = jnp.einsum(
        "mnd,mvd->mnv", rows_hidden, head_weight, preferred_element_type=jnp.float32
    )
    peak_logit = jnp.max(logits, axis=2)
    local_id = rows_target - vocab_start
    matches = jnp.arange(head_weight.shape[1], dtype=jnp.int32)[None, :] == local_id[:, None]
    picked = jnp.sum(jnp.where(matches[None, :, :], logits, 0.0), axis=2)
    return logits, peak_logit, picked


def ring_gather(block, perm_of, count):
    got = {0: block}
    forward = block
    backward = block
    for step in range(1, count // 2 + 1):
        forward = lax.ppermute(forward, "req", perm_of(1))
        got[-step % count] = forward
        if step < count - step:
            backward = lax.ppermute(backward, "req", perm_of(-1))
            got[step] = backward
    return jnp.stack([got[k] for k in range(count)])


DIGIT = 256
CORES = 2
ROWS_X = 4


def local(
    gate_in,
    mix_in,
    keys_in,
    step_in,
    resid_in,
    kernel_mix,
    kernel_keys,
    step_bias,
    decay_rate,
    skip_gain,
    norm_gain,
    final_gain,
    out_weight,
    head_weight,
    history_mix,
    history_keys,
    start_state,
    lengths,
    continued,
    targets,
    score_flag,
):
    groups = lax.axis_size("tp")
    shards = lax.axis_size("req")
    lane_index = lax.axis_index("tp")
    shard_index = lax.axis_index("req")
    models = gate_in.shape[0]
    step_count = gate_in.shape[1]
    row_count = step_count // groups
    chips_z = shards // (ROWS_X * CORES)
    core_index = shard_index % CORES
    x_index = (shard_index // CORES) % ROWS_X
    z_index = shard_index // (CORES * ROWS_X)
    vocab_part = head_weight.shape[1]
    partner_weight = lax.ppermute(
        head_weight, "req", [(i, i ^ 1) for i in range(shards)]
    )
    gated = jnp.stack(
        [
            mixer_block(
                gate_in[model_index],
                mix_in[model_index],
                keys_in[model_index],
                step_in[model_index],
                kernel_mix[model_index],
                kernel_keys[model_index],
                step_bias[model_index],
                decay_rate[model_index],
                skip_gain[model_index],
                history_mix[model_index],
                history_keys[model_index],
                start_state[model_index],
                lengths[0],
                continued[0],
            )
            for model_index in range(models)
        ]
    )
    squares = lax.psum(jnp.sum(gated * gated, axis=2), "tp")
    inner_width = gated.shape[2] * groups
    normed = (
        gated * lax.rsqrt(squares / inner_width + EPSILON)[:, :, None] * norm_gain[:, None, :]
    ).astype(jnp.bfloat16)
    partial_out = jnp.einsum(
        "mtc,mcd->mtd",
        normed,
        lax.all_gather(out_weight, "req", axis=2, tiled=True),
        preferred_element_type=jnp.float32,
    )
    part_width = resid_in.shape[2]
    partial_out = lax.dynamic_update_slice_in_dim(
        partial_out,
        lax.dynamic_slice_in_dim(partial_out, lane_index * part_width, part_width, 2)
        + resid_in.astype(jnp.float32),
        lane_index * part_width,
        2,
    )
    hidden = lax.psum_scatter(partial_out, "tp", scatter_dimension=1, tiled=True).astype(
        jnp.bfloat16
    )
    full_width = hidden.shape[2]
    hidden_float = hidden.astype(jnp.float32)
    final_squares = jnp.sum(hidden_float * hidden_float, axis=2)
    final_rows = (
        hidden_float
        * lax.rsqrt(final_squares / full_width + EPSILON)[:, :, None]
        * final_gain[:, None, :]
    ).astype(jnp.bfloat16)
    own_target = lax.dynamic_slice_in_dim(targets, lane_index * row_count, row_count, 0)
    high_digit = (own_target // DIGIT).astype(jnp.bfloat16)
    low_digit = (own_target % DIGIT).astype(jnp.bfloat16)
    target_row = jnp.zeros((1, full_width), jnp.bfloat16)
    target_row = target_row.at[0, :row_count].set(high_digit)
    target_row = target_row.at[0, row_count : 2 * row_count].set(low_digit)
    packet = jnp.concatenate([final_rows.reshape(models * row_count, full_width), target_row], axis=0)

    def along_z(shift):
        return [(i, (i + shift * CORES * ROWS_X) % shards) for i in range(shards)]

    def along_x(shift):
        return [
            (i, (i // (CORES * ROWS_X)) * CORES * ROWS_X
             + (((i // CORES) % ROWS_X + shift) % ROWS_X) * CORES + i % CORES)
            for i in range(shards)
        ]

    every = ring_gather(ring_gather(packet, along_z, chips_z), along_x, ROWS_X)
    peers = ROWS_X * chips_z
    every = every.reshape(peers, models * row_count + 1, full_width)
    every_rows = (
        every[:, : models * row_count]
        .reshape(peers, models, row_count, full_width)
        .transpose(1, 0, 2, 3)
        .reshape(models, peers * row_count, full_width)
    )
    every_target = (
        every[:, models * row_count, :row_count].astype(jnp.int32) * DIGIT
        + every[:, models * row_count, row_count : 2 * row_count].astype(jnp.int32)
    ).reshape(peers * row_count)
    own_logits, own_peak, own_picked = head_scores(
        head_weight, shard_index * vocab_part, every_rows, every_target
    )
    other_logits, other_peak, other_picked = head_scores(
        partner_weight, (shard_index ^ 1) * vocab_part, every_rows, every_target
    )
    peak_logit = jnp.maximum(own_peak, other_peak)
    spread = jnp.sum(jnp.exp(own_logits - peak_logit[:, :, None]), axis=2) + jnp.sum(
        jnp.exp(other_logits - peak_logit[:, :, None]), axis=2
    )
    statistics = jnp.stack([peak_logit, spread, own_picked + other_picked])
    statistics = statistics.reshape(3, models, ROWS_X, chips_z, row_count).transpose(0, 1, 3, 2, 4)
    statistics = jnp.roll(jnp.roll(statistics, z_index, axis=2), x_index, axis=3)
    neutral = jnp.stack(
        [
            jnp.full_like(statistics[0], -1e30),
            jnp.zeros_like(statistics[1]),
            jnp.zeros_like(statistics[2]),
        ]
    )
    send = jnp.stack(
        [jnp.where(core_index == c, statistics, neutral) for c in range(CORES)], axis=4
    ).reshape(3, models, shards, row_count)
    received = lax.all_to_all(send, "req", split_axis=2, concat_axis=2, tiled=True)
    peak_each, spread_each, picked_each = received[0], received[1], received[2]
    peak_logit = jnp.max(peak_each, axis=1)
    spread = jnp.sum(spread_each * jnp.exp(peak_each - peak_logit[:, None, :]), axis=1)
    picked = jnp.sum(picked_each, axis=1)
    scored_rows = lax.dynamic_slice_in_dim(score_flag, lane_index * row_count, row_count, 0).astype(
        jnp.float32
    )
    return (picked - (peak_logit + jnp.log(spread))) * scored_rows[None, :]


def solution(mesh):
    placed = (
        P(None, "req", "tp"),
        P(None, "req", "tp"),
        P(None, "req", None),
        P(None, "req", "tp"),
        P(None, "req", "tp"),
        P(None, None, "tp"),
        P(),
        P(None, "tp"),
        P(None, "tp"),
        P(None, "tp"),
        P(None, "tp"),
        P(),
        P(None, "tp", "req"),
        P(None, "req", None),
        P(None, "req", None, "tp"),
        P(None, "req", None, None),
        P(None, "req", "tp", None),
        P("req", None),
        P("req", None),
        P("req"),
        P("req"),
    )
    return jax.shard_map(
        local, mesh=mesh, in_specs=placed, out_specs=P(None, ("req", "tp")), check_vma=False
    )
```

```python
import jax
import jax.numpy as jnp
from jax import lax
from jax.sharding import PartitionSpec as P

EPSILON = 1e-05
PRECISE = lax.Precision.HIGHEST


def merged_2(part, axis, combine):
    gathered = jax.tree.map(lambda a: lax.all_gather(a, axis), part)

    def take(source):
        return jax.tree.map(lambda a: lax.dynamic_index_in_dim(a, source, 0, False), gathered)

    return lax.fori_loop(
        1, lax.axis_size(axis), lambda source, state: combine(state, take(source)), take(0)
    )


def request_layout(lengths, step_count):
    starts = jnp.cumsum(lengths) - lengths
    time_index = jnp.arange(step_count, dtype=jnp.int32)
    segment = jnp.sum((time_index[:, None] >= starts[None, 1:]).astype(jnp.int32), axis=1)
    member = segment[:, None] == jnp.arange(lengths.shape[0], dtype=jnp.int32)[None, :]
    first_step = jnp.sum(jnp.where(member, starts[None, :], 0), axis=1)
    return (starts, segment, member, time_index - first_step)


def causal_conv(stream, kernel, history, member, offset):
    tap_count = kernel.shape[0]
    history_len = tap_count - 1
    current = stream.astype(jnp.float32)
    member_bf = member.astype(jnp.bfloat16)
    slot_values = [
        jnp.dot(member_bf, history[:, slot_index, :], preferred_element_type=jnp.float32)
        for slot_index in range(history_len)
    ]
    output = kernel[history_len][None, :] * current
    for lag_steps in range(1, tap_count):
        shifted = jnp.concatenate(
            [jnp.zeros((lag_steps, current.shape[1]), current.dtype), current[:-lag_steps]], axis=0
        )
        earlier = jnp.zeros_like(current)
        for slot_index in range(history_len):
            earlier = earlier + jnp.where(
                (offset - lag_steps == slot_index - history_len)[:, None],
                slot_values[slot_index],
                0.0,
            )
        output = output + kernel[history_len - lag_steps][None, :] * jnp.where(
            (offset >= lag_steps)[:, None], shifted, earlier
        )
    return jax.nn.silu(output)


def mixer_block(
    gate_rows,
    mix_rows,
    keys_rows,
    step_raw,
    kernel_mix,
    kernel_keys,
    step_bias,
    decay_rate,
    skip_gain,
    history_mix,
    history_keys,
    start_state,
    lengths,
    continued,
):
    step_count = gate_rows.shape[0]
    head_count = step_raw.shape[1]
    inner_width = mix_rows.shape[1]
    head_size = inner_width // head_count
    states = start_state.shape[2]
    starts, segment, member, offset = request_layout(lengths, step_count)
    keep_state = continued.astype(jnp.bfloat16)
    mixed = causal_conv(
        mix_rows, kernel_mix, history_mix * keep_state[:, None, None], member, offset
    )
    projected = causal_conv(
        keys_rows, kernel_keys, history_keys * keep_state[:, None, None], member, offset
    )
    inject = projected[:, :states]
    readout = projected[:, states:]
    step_size = jax.nn.softplus(step_raw.astype(jnp.float32) + step_bias[None, :])
    log_decay = -step_size * decay_rate[None, :]
    running = jnp.cumsum(log_decay, axis=0)
    time_index = jnp.arange(step_count, dtype=jnp.int32)
    causal = (segment[:, None] == segment[None, :]) & (time_index[:, None] >= time_index[None, :])
    spread = jnp.minimum(running[:, None, :] - running[None, :, :], 0.0)
    transfer = jnp.where(causal[:, :, None], jnp.exp(spread), 0.0)
    intersection = jnp.dot(readout, inject.T, precision=PRECISE)
    kernel_full = transfer * intersection[:, :, None]
    values = mixed.reshape(step_count, head_count, head_size)
    output = jnp.einsum(
        "tsh,shp->thp", kernel_full, step_size[:, :, None] * values, precision=PRECISE
    )
    before = jnp.take(running - log_decay, starts, axis=0)
    member_float = member.astype(jnp.float32)
    entry_level = jnp.dot(member_float, before, precision=PRECISE)
    carried = jnp.exp(jnp.minimum(running - entry_level, 0.0))
    initial = start_state.astype(jnp.float32) * keep_state.astype(jnp.float32)[:, None, None]
    readings = jnp.einsum("tn,rcn->trc", readout, initial, precision=PRECISE)
    chosen = jnp.sum(member_float[:, :, None] * readings, axis=1).reshape(
        step_count, head_count, head_size
    )
    output = output + carried[:, :, None] * chosen + skip_gain[None, :, None] * values
    return output.reshape(step_count, inner_width) * jax.nn.silu(gate_rows.astype(jnp.float32))


def head_scores(head_weight, vocab_start, rows_hidden, rows_target):
    logits = jnp.einsum(
        "mnd,mvd->mnv", rows_hidden, head_weight, preferred_element_type=jnp.float32
    )
    peak_logit = jnp.max(logits, axis=2)
    local_id = rows_target - vocab_start
    matches = jnp.arange(head_weight.shape[1], dtype=jnp.int32)[None, :] == local_id[:, None]
    picked = jnp.sum(jnp.where(matches[None, :, :], logits, 0.0), axis=2)
    return logits, peak_logit, picked


def ring_gather(block, perm_of, count):
    got = {0: block}
    forward = block
    backward = block
    for step in range(1, count // 2 + 1):
        forward = lax.ppermute(forward, "req", perm_of(1))
        got[-step % count] = forward
        if step < count - step:
            backward = lax.ppermute(backward, "req", perm_of(-1))
            got[step] = backward
    return jnp.stack([got[k] for k in range(count)])


DIGIT = 256
CORES = 2
ROWS_X = 4


def local(
    gate_in,
    mix_in,
    keys_in,
    step_in,
    resid_in,
    kernel_mix,
    kernel_keys,
    step_bias,
    decay_rate,
    skip_gain,
    norm_gain,
    final_gain,
    out_weight,
    head_weight,
    history_mix,
    history_keys,
    start_state,
    lengths,
    continued,
    targets,
    score_flag,
):
    groups = lax.axis_size("tp")
    shards = lax.axis_size("req")
    lane_index = lax.axis_index("tp")
    shard_index = lax.axis_index("req")
    models = gate_in.shape[0]
    step_count = gate_in.shape[1]
    row_count = step_count // groups
    chips_z = shards // (ROWS_X * CORES)
    core_index = shard_index % CORES
    x_index = (shard_index // CORES) % ROWS_X
    z_index = shard_index // (CORES * ROWS_X)
    def along_z(shift):
        return [(i, (i + shift * CORES * ROWS_X) % shards) for i in range(shards)]

    def along_x(shift):
        return [
            (i, (i // (CORES * ROWS_X)) * CORES * ROWS_X
             + (((i // CORES) % ROWS_X + shift) % ROWS_X) * CORES + i % CORES)
            for i in range(shards)
        ]

    def along_core(shift):
        return [(i, i ^ 1) for i in range(shards)]

    vocab_part = head_weight.shape[1]
    partner_weight = lax.ppermute(
        head_weight, "req", [(i, i ^ 1) for i in range(shards)]
    )
    gated = jnp.stack(
        [
            mixer_block(
                gate_in[model_index],
                mix_in[model_index],
                keys_in[model_index],
                step_in[model_index],
                kernel_mix[model_index],
                kernel_keys[model_index],
                step_bias[model_index],
                decay_rate[model_index],
                skip_gain[model_index],
                history_mix[model_index],
                history_keys[model_index],
                start_state[model_index],
                lengths[0],
                continued[0],
            )
            for model_index in range(models)
        ]
    )
    squares = lax.psum(jnp.sum(gated * gated, axis=2), "tp")
    inner_width = gated.shape[2] * groups
    normed = (
        gated * lax.rsqrt(squares / inner_width + EPSILON)[:, :, None] * norm_gain[:, None, :]
    ).astype(jnp.bfloat16)
    first_weight = lax.all_gather(out_weight[0], "req", axis=1, tiled=True)
    ring_weight = ring_gather(
        ring_gather(ring_gather(out_weight[1], along_core, CORES), along_z, chips_z),
        along_x,
        ROWS_X,
    )
    ring_weight = jnp.roll(
        jnp.roll(jnp.roll(ring_weight.transpose(1, 0, 2, 3, 4), z_index, axis=0), x_index, axis=1),
        core_index,
        axis=2,
    )
    second_weight = ring_weight.transpose(3, 0, 1, 2, 4).reshape(
        out_weight.shape[1], shards * out_weight.shape[2]
    )
    partial_out = jnp.stack(
        [
            jnp.dot(normed[0], first_weight, preferred_element_type=jnp.float32),
            jnp.dot(normed[1], second_weight, preferred_element_type=jnp.float32),
        ]
    )
    part_width = resid_in.shape[2]
    partial_out = lax.dynamic_update_slice_in_dim(
        partial_out,
        lax.dynamic_slice_in_dim(partial_out, lane_index * part_width, part_width, 2)
        + resid_in.astype(jnp.float32),
        lane_index * part_width,
        2,
    )
    hidden = lax.psum_scatter(partial_out, "tp", scatter_dimension=1, tiled=True).astype(
        jnp.bfloat16
    )
    full_width = hidden.shape[2]
    hidden_float = hidden.astype(jnp.float32)
    final_squares = jnp.sum(hidden_float * hidden_float, axis=2)
    final_rows = (
        hidden_float
        * lax.rsqrt(final_squares / full_width + EPSILON)[:, :, None]
        * final_gain[:, None, :]
    ).astype(jnp.bfloat16)
    own_target = lax.dynamic_slice_in_dim(targets, lane_index * row_count, row_count, 0)
    high_digit = (own_target // DIGIT).astype(jnp.bfloat16)
    low_digit = (own_target % DIGIT).astype(jnp.bfloat16)
    target_row = jnp.zeros((1, full_width), jnp.bfloat16)
    target_row = target_row.at[0, :row_count].set(high_digit)
    target_row = target_row.at[0, row_count : 2 * row_count].set(low_digit)
    packet = jnp.concatenate([final_rows.reshape(models * row_count, full_width), target_row], axis=0)

    every = ring_gather(ring_gather(packet, along_z, chips_z), along_x, ROWS_X)
    peers = ROWS_X * chips_z
    every = every.reshape(peers, models * row_count + 1, full_width)
    every_rows = (
        every[:, : models * row_count]
        .reshape(peers, models, row_count, full_width)
        .transpose(1, 0, 2, 3)
        .reshape(models, peers * row_count, full_width)
    )
    every_target = (
        every[:, models * row_count, :row_count].astype(jnp.int32) * DIGIT
        + every[:, models * row_count, row_count : 2 * row_count].astype(jnp.int32)
    ).reshape(peers * row_count)
    own_logits, own_peak, own_picked = head_scores(
        head_weight, shard_index * vocab_part, every_rows, every_target
    )
    other_logits, other_peak, other_picked = head_scores(
        partner_weight, (shard_index ^ 1) * vocab_part, every_rows, every_target
    )
    peak_logit = jnp.maximum(own_peak, other_peak)
    spread = jnp.sum(jnp.exp(own_logits - peak_logit[:, :, None]), axis=2) + jnp.sum(
        jnp.exp(other_logits - peak_logit[:, :, None]), axis=2
    )
    statistics = jnp.stack([peak_logit, spread, own_picked + other_picked])
    statistics = statistics.reshape(3, models, ROWS_X, chips_z, row_count).transpose(0, 1, 3, 2, 4)
    statistics = jnp.roll(jnp.roll(statistics, z_index, axis=2), x_index, axis=3)
    neutral = jnp.stack(
        [
            jnp.full_like(statistics[0], -1e30),
            jnp.zeros_like(statistics[1]),
            jnp.zeros_like(statistics[2]),
        ]
    )
    send = jnp.stack(
        [jnp.where(core_index == c, statistics, neutral) for c in range(CORES)], axis=4
    ).reshape(3, models, shards, row_count)
    received = lax.all_to_all(send, "req", split_axis=2, concat_axis=2, tiled=True)
    peak_each, spread_each, picked_each = received[0], received[1], received[2]
    peak_logit = jnp.max(peak_each, axis=1)
    spread = jnp.sum(spread_each * jnp.exp(peak_each - peak_logit[:, None, :]), axis=1)
    picked = jnp.sum(picked_each, axis=1)
    scored_rows = lax.dynamic_slice_in_dim(score_flag, lane_index * row_count, row_count, 0).astype(
        jnp.float32
    )
    return (picked - (peak_logit + jnp.log(spread))) * scored_rows[None, :]


def solution(mesh):
    placed = (
        P(None, "req", "tp"),
        P(None, "req", "tp"),
        P(None, "req", None),
        P(None, "req", "tp"),
        P(None, "req", "tp"),
        P(None, None, "tp"),
        P(),
        P(None, "tp"),
        P(None, "tp"),
        P(None, "tp"),
        P(None, "tp"),
        P(),
        P(None, "tp", "req"),
        P(None, "req", None),
        P(None, "req", None, "tp"),
        P(None, "req", None, None),
        P(None, "req", "tp", None),
        P("req", None),
        P("req", None),
        P("req"),
        P("req"),
    )
    return jax.shard_map(
        local, mesh=mesh, in_specs=placed, out_specs=P(None, ("req", "tp")), check_vma=False
    )
```

```python
import jax
import jax.numpy as jnp
from jax import lax
from jax.sharding import PartitionSpec as P

EPSILON = 1e-05
PRECISE = lax.Precision.HIGHEST


def merged_2(part, axis, combine):
    gathered = jax.tree.map(lambda a: lax.all_gather(a, axis), part)

    def take(source):
        return jax.tree.map(lambda a: lax.dynamic_index_in_dim(a, source, 0, False), gathered)

    return lax.fori_loop(
        1, lax.axis_size(axis), lambda source, state: combine(state, take(source)), take(0)
    )


def request_layout(lengths, step_count):
    starts = jnp.cumsum(lengths) - lengths
    time_index = jnp.arange(step_count, dtype=jnp.int32)
    segment = jnp.sum((time_index[:, None] >= starts[None, 1:]).astype(jnp.int32), axis=1)
    member = segment[:, None] == jnp.arange(lengths.shape[0], dtype=jnp.int32)[None, :]
    first_step = jnp.sum(jnp.where(member, starts[None, :], 0), axis=1)
    return (starts, segment, member, time_index - first_step)


def causal_conv(stream, kernel, history, member, offset):
    tap_count = kernel.shape[0]
    history_len = tap_count - 1
    current = stream.astype(jnp.float32)
    member_bf = member.astype(jnp.bfloat16)
    slot_values = [
        jnp.dot(member_bf, history[:, slot_index, :], preferred_element_type=jnp.float32)
        for slot_index in range(history_len)
    ]
    output = kernel[history_len][None, :] * current
    for lag_steps in range(1, tap_count):
        shifted = jnp.concatenate(
            [jnp.zeros((lag_steps, current.shape[1]), current.dtype), current[:-lag_steps]], axis=0
        )
        earlier = jnp.zeros_like(current)
        for slot_index in range(history_len):
            earlier = earlier + jnp.where(
                (offset - lag_steps == slot_index - history_len)[:, None],
                slot_values[slot_index],
                0.0,
            )
        output = output + kernel[history_len - lag_steps][None, :] * jnp.where(
            (offset >= lag_steps)[:, None], shifted, earlier
        )
    return jax.nn.silu(output)


def mixer_block(
    gate_rows,
    mix_rows,
    keys_rows,
    step_raw,
    kernel_mix,
    kernel_keys,
    step_bias,
    decay_rate,
    skip_gain,
    history_mix,
    history_keys,
    start_state,
    lengths,
    continued,
):
    step_count = gate_rows.shape[0]
    head_count = step_raw.shape[1]
    inner_width = mix_rows.shape[1]
    head_size = inner_width // head_count
    states = start_state.shape[2]
    starts, segment, member, offset = request_layout(lengths, step_count)
    keep_state = continued.astype(jnp.bfloat16)
    mixed = causal_conv(
        mix_rows, kernel_mix, history_mix * keep_state[:, None, None], member, offset
    )
    projected = causal_conv(
        keys_rows, kernel_keys, history_keys * keep_state[:, None, None], member, offset
    )
    inject = projected[:, :states]
    readout = projected[:, states:]
    step_size = jax.nn.softplus(step_raw.astype(jnp.float32) + step_bias[None, :])
    log_decay = -step_size * decay_rate[None, :]
    running = jnp.cumsum(log_decay, axis=0)
    time_index = jnp.arange(step_count, dtype=jnp.int32)
    causal = (segment[:, None] == segment[None, :]) & (time_index[:, None] >= time_index[None, :])
    spread = jnp.minimum(running[:, None, :] - running[None, :, :], 0.0)
    transfer = jnp.where(causal[:, :, None], jnp.exp(spread), 0.0)
    intersection = jnp.dot(readout, inject.T, precision=PRECISE)
    kernel_full = transfer * intersection[:, :, None]
    values = mixed.reshape(step_count, head_count, head_size)
    output = jnp.einsum(
        "tsh,shp->thp", kernel_full, step_size[:, :, None] * values, precision=PRECISE
    )
    before = jnp.take(running - log_decay, starts, axis=0)
    member_float = member.astype(jnp.float32)
    entry_level = jnp.dot(member_float, before, precision=PRECISE)
    carried = jnp.exp(jnp.minimum(running - entry_level, 0.0))
    initial = start_state.astype(jnp.float32) * keep_state.astype(jnp.float32)[:, None, None]
    readings = jnp.einsum("tn,rcn->trc", readout, initial, precision=PRECISE)
    chosen = jnp.sum(member_float[:, :, None] * readings, axis=1).reshape(
        step_count, head_count, head_size
    )
    output = output + carried[:, :, None] * chosen + skip_gain[None, :, None] * values
    return output.reshape(step_count, inner_width) * jax.nn.silu(gate_rows.astype(jnp.float32))


def head_scores(head_weight, vocab_start, rows_hidden, rows_target):
    logits = jnp.einsum(
        "mnd,mvd->mnv", rows_hidden, head_weight, preferred_element_type=jnp.float32
    )
    peak_logit = jnp.max(logits, axis=2)
    local_id = rows_target - vocab_start
    matches = jnp.arange(head_weight.shape[1], dtype=jnp.int32)[None, :] == local_id[:, None]
    picked = jnp.sum(jnp.where(matches[None, :, :], logits, 0.0), axis=2)
    return logits, peak_logit, picked


def ring_gather(block, perm_of, count):
    got = {0: block}
    forward = block
    backward = block
    for step in range(1, count // 2 + 1):
        forward = lax.ppermute(forward, "req", perm_of(1))
        got[-step % count] = forward
        if step < count - step:
            backward = lax.ppermute(backward, "req", perm_of(-1))
            got[step] = backward
    return jnp.stack([got[k] for k in range(count)])


DIGIT = 256
SQUARE_COLUMNS = 128
CORES = 2
ROWS_X = 4


def local(
    gate_in,
    mix_in,
    keys_in,
    step_in,
    resid_in,
    kernel_mix,
    kernel_keys,
    step_bias,
    decay_rate,
    skip_gain,
    norm_gain,
    final_gain,
    out_weight,
    head_weight,
    history_mix,
    history_keys,
    start_state,
    lengths,
    continued,
    targets,
    score_flag,
):
    groups = lax.axis_size("tp")
    shards = lax.axis_size("req")
    lane_index = lax.axis_index("tp")
    shard_index = lax.axis_index("req")
    models = gate_in.shape[0]
    step_count = gate_in.shape[1]
    row_count = step_count // groups
    chips_z = shards // (ROWS_X * CORES)
    core_index = shard_index % CORES
    x_index = (shard_index // CORES) % ROWS_X
    z_index = shard_index // (CORES * ROWS_X)
    def along_z(shift):
        return [(i, (i + shift * CORES * ROWS_X) % shards) for i in range(shards)]

    def along_x(shift):
        return [
            (i, (i // (CORES * ROWS_X)) * CORES * ROWS_X
             + (((i // CORES) % ROWS_X + shift) % ROWS_X) * CORES + i % CORES)
            for i in range(shards)
        ]

    def along_core(shift):
        return [(i, i ^ 1) for i in range(shards)]

    vocab_part = head_weight.shape[1]
    partner_weight = lax.ppermute(
        head_weight, "req", [(i, i ^ 1) for i in range(shards)]
    )
    gated = jnp.stack(
        [
            mixer_block(
                gate_in[model_index],
                mix_in[model_index],
                keys_in[model_index],
                step_in[model_index],
                kernel_mix[model_index],
                kernel_keys[model_index],
                step_bias[model_index],
                decay_rate[model_index],
                skip_gain[model_index],
                history_mix[model_index],
                history_keys[model_index],
                start_state[model_index],
                lengths[0],
                continued[0],
            )
            for model_index in range(models)
        ]
    )
    inner_width = gated.shape[2] * groups
    squares = jnp.sum(gated * gated, axis=2)
    unscaled = (gated * norm_gain[:, None, :]).astype(jnp.bfloat16)
    ring_weight = ring_gather(
        ring_gather(ring_gather(out_weight, along_core, CORES), along_z, chips_z),
        along_x,
        ROWS_X,
    )
    ring_weight = jnp.roll(
        jnp.roll(jnp.roll(ring_weight.transpose(1, 0, 2, 3, 4, 5), z_index, axis=0), x_index, axis=1),
        core_index,
        axis=2,
    )
    full_weight = ring_weight.transpose(3, 4, 0, 1, 2, 5).reshape(
        models, out_weight.shape[1], shards * out_weight.shape[2]
    )
    partial_out = jnp.einsum(
        "mtc,mcd->mtd", unscaled, full_weight, preferred_element_type=jnp.float32
    )
    extra = jnp.zeros(squares.shape + (SQUARE_COLUMNS,), jnp.float32).at[:, :, 0].set(squares)
    reduced = lax.psum_scatter(
        jnp.concatenate([partial_out, extra], axis=2), "tp", scatter_dimension=1, tiled=True
    )
    full_width = partial_out.shape[2]
    update = reduced[:, :, :full_width]
    scale = lax.rsqrt(reduced[:, :, full_width] / inner_width + EPSILON)
    resid_rows = lax.all_to_all(resid_in, "tp", split_axis=1, concat_axis=2, tiled=True)
    hidden = (resid_rows.astype(jnp.float32) + update * scale[:, :, None]).astype(jnp.bfloat16)
    full_width = hidden.shape[2]
    hidden_float = hidden.astype(jnp.float32)
    final_squares = jnp.sum(hidden_float * hidden_float, axis=2)
    final_rows = (
        hidden_float
        * lax.rsqrt(final_squares / full_width + EPSILON)[:, :, None]
        * final_gain[:, None, :]
    ).astype(jnp.bfloat16)
    own_target = lax.dynamic_slice_in_dim(targets, lane_index * row_count, row_count, 0)
    high_digit = (own_target // DIGIT).astype(jnp.bfloat16)
    low_digit = (own_target % DIGIT).astype(jnp.bfloat16)
    target_row = jnp.zeros((1, full_width), jnp.bfloat16)
    target_row = target_row.at[0, :row_count].set(high_digit)
    target_row = target_row.at[0, row_count : 2 * row_count].set(low_digit)
    packet = jnp.concatenate([final_rows.reshape(models * row_count, full_width), target_row], axis=0)

    every = ring_gather(ring_gather(packet, along_z, chips_z), along_x, ROWS_X)
    peers = ROWS_X * chips_z
    every = every.reshape(peers, models * row_count + 1, full_width)
    every_rows = (
        every[:, : models * row_count]
        .reshape(peers, models, row_count, full_width)
        .transpose(1, 0, 2, 3)
        .reshape(models, peers * row_count, full_width)
    )
    every_target = (
        every[:, models * row_count, :row_count].astype(jnp.int32) * DIGIT
        + every[:, models * row_count, row_count : 2 * row_count].astype(jnp.int32)
    ).reshape(peers * row_count)
    own_logits, own_peak, own_picked = head_scores(
        head_weight, shard_index * vocab_part, every_rows, every_target
    )
    other_logits, other_peak, other_picked = head_scores(
        partner_weight, (shard_index ^ 1) * vocab_part, every_rows, every_target
    )
    peak_logit = jnp.maximum(own_peak, other_peak)
    spread = jnp.sum(jnp.exp(own_logits - peak_logit[:, :, None]), axis=2) + jnp.sum(
        jnp.exp(other_logits - peak_logit[:, :, None]), axis=2
    )
    statistics = jnp.stack([peak_logit, spread, own_picked + other_picked])
    statistics = statistics.reshape(3, models, ROWS_X, chips_z, row_count).transpose(0, 1, 3, 2, 4)
    statistics = jnp.roll(jnp.roll(statistics, z_index, axis=2), x_index, axis=3)
    neutral = jnp.stack(
        [
            jnp.full_like(statistics[0], -1e30),
            jnp.zeros_like(statistics[1]),
            jnp.zeros_like(statistics[2]),
        ]
    )
    send = jnp.stack(
        [jnp.where(core_index == c, statistics, neutral) for c in range(CORES)], axis=4
    ).reshape(3, models, shards, row_count)
    received = lax.all_to_all(send, "req", split_axis=2, concat_axis=2, tiled=True)
    peak_each, spread_each, picked_each = received[0], received[1], received[2]
    peak_logit = jnp.max(peak_each, axis=1)
    spread = jnp.sum(spread_each * jnp.exp(peak_each - peak_logit[:, None, :]), axis=1)
    picked = jnp.sum(picked_each, axis=1)
    scored_rows = lax.dynamic_slice_in_dim(score_flag, lane_index * row_count, row_count, 0).astype(
        jnp.float32
    )
    return (picked - (peak_logit + jnp.log(spread))) * scored_rows[None, :]


def solution(mesh):
    placed = (
        P(None, "req", "tp"),
        P(None, "req", "tp"),
        P(None, "req", None),
        P(None, "req", "tp"),
        P(None, "req", "tp"),
        P(None, None, "tp"),
        P(),
        P(None, "tp"),
        P(None, "tp"),
        P(None, "tp"),
        P(None, "tp"),
        P(),
        P(None, "tp", "req"),
        P(None, "req", None),
        P(None, "req", None, "tp"),
        P(None, "req", None, None),
        P(None, "req", "tp", None),
        P("req", None),
        P("req", None),
        P("req"),
        P("req"),
    )
    return jax.shard_map(
        local, mesh=mesh, in_specs=placed, out_specs=P(None, ("req", "tp")), check_vma=False
    )
```

```python
import jax
import jax.numpy as jnp
from jax import lax
from jax.sharding import PartitionSpec as P

EPSILON = 1e-05
PRECISE = lax.Precision.HIGHEST


def merged_2(part, axis, combine):
    gathered = jax.tree.map(lambda a: lax.all_gather(a, axis), part)

    def take(source):
        return jax.tree.map(lambda a: lax.dynamic_index_in_dim(a, source, 0, False), gathered)

    return lax.fori_loop(
        1, lax.axis_size(axis), lambda source, state: combine(state, take(source)), take(0)
    )


def request_layout(lengths, step_count):
    starts = jnp.cumsum(lengths) - lengths
    time_index = jnp.arange(step_count, dtype=jnp.int32)
    segment = jnp.sum((time_index[:, None] >= starts[None, 1:]).astype(jnp.int32), axis=1)
    member = segment[:, None] == jnp.arange(lengths.shape[0], dtype=jnp.int32)[None, :]
    first_step = jnp.sum(jnp.where(member, starts[None, :], 0), axis=1)
    return (starts, segment, member, time_index - first_step)


def causal_conv(stream, kernel, history, member, offset):
    tap_count = kernel.shape[0]
    history_len = tap_count - 1
    current = stream.astype(jnp.float32)
    member_bf = member.astype(jnp.bfloat16)
    slot_values = [
        jnp.dot(member_bf, history[:, slot_index, :], preferred_element_type=jnp.float32)
        for slot_index in range(history_len)
    ]
    output = kernel[history_len][None, :] * current
    for lag_steps in range(1, tap_count):
        shifted = jnp.concatenate(
            [jnp.zeros((lag_steps, current.shape[1]), current.dtype), current[:-lag_steps]], axis=0
        )
        earlier = jnp.zeros_like(current)
        for slot_index in range(history_len):
            earlier = earlier + jnp.where(
                (offset - lag_steps == slot_index - history_len)[:, None],
                slot_values[slot_index],
                0.0,
            )
        output = output + kernel[history_len - lag_steps][None, :] * jnp.where(
            (offset >= lag_steps)[:, None], shifted, earlier
        )
    return jax.nn.silu(output)


def mixer_block(
    gate_rows,
    mix_rows,
    keys_rows,
    step_raw,
    kernel_mix,
    kernel_keys,
    step_bias,
    decay_rate,
    skip_gain,
    history_mix,
    history_keys,
    start_state,
    lengths,
    continued,
):
    step_count = gate_rows.shape[0]
    head_count = step_raw.shape[1]
    inner_width = mix_rows.shape[1]
    head_size = inner_width // head_count
    states = start_state.shape[2]
    starts, segment, member, offset = request_layout(lengths, step_count)
    keep_state = continued.astype(jnp.bfloat16)
    mixed = causal_conv(
        mix_rows, kernel_mix, history_mix * keep_state[:, None, None], member, offset
    )
    projected = causal_conv(
        keys_rows, kernel_keys, history_keys * keep_state[:, None, None], member, offset
    )
    inject = projected[:, :states]
    readout = projected[:, states:]
    step_size = jax.nn.softplus(step_raw.astype(jnp.float32) + step_bias[None, :])
    log_decay = -step_size * decay_rate[None, :]
    running = jnp.cumsum(log_decay, axis=0)
    time_index = jnp.arange(step_count, dtype=jnp.int32)
    causal = (segment[:, None] == segment[None, :]) & (time_index[:, None] >= time_index[None, :])
    spread = jnp.minimum(running[:, None, :] - running[None, :, :], 0.0)
    transfer = jnp.where(causal[:, :, None], jnp.exp(spread), 0.0)
    intersection = jnp.dot(readout, inject.T, precision=PRECISE)
    kernel_full = transfer * intersection[:, :, None]
    values = mixed.reshape(step_count, head_count, head_size)
    output = jnp.einsum(
        "tsh,shp->thp", kernel_full, step_size[:, :, None] * values, precision=PRECISE
    )
    before = jnp.take(running - log_decay, starts, axis=0)
    member_float = member.astype(jnp.float32)
    entry_level = jnp.dot(member_float, before, precision=PRECISE)
    carried = jnp.exp(jnp.minimum(running - entry_level, 0.0))
    initial = start_state.astype(jnp.float32) * keep_state.astype(jnp.float32)[:, None, None]
    readings = jnp.einsum("tn,rcn->trc", readout, initial, precision=PRECISE)
    chosen = jnp.sum(member_float[:, :, None] * readings, axis=1).reshape(
        step_count, head_count, head_size
    )
    output = output + carried[:, :, None] * chosen + skip_gain[None, :, None] * values
    return output.reshape(step_count, inner_width) * jax.nn.silu(gate_rows.astype(jnp.float32))


def head_scores(head_weight, vocab_start, rows_hidden, rows_target):
    logits = jnp.einsum(
        "mnd,mvd->mnv", rows_hidden, head_weight, preferred_element_type=jnp.float32
    )
    peak_logit = jnp.max(logits, axis=2)
    local_id = rows_target - vocab_start
    matches = jnp.arange(head_weight.shape[1], dtype=jnp.int32)[None, :] == local_id[:, None]
    picked = jnp.sum(jnp.where(matches[None, :, :], logits, 0.0), axis=2)
    return logits, peak_logit, picked


def ring_gather(block, perm_of, count):
    got = {0: block}
    forward = block
    backward = block
    for step in range(1, count // 2 + 1):
        forward = lax.ppermute(forward, "req", perm_of(1))
        got[-step % count] = forward
        if step < count - step:
            backward = lax.ppermute(backward, "req", perm_of(-1))
            got[step] = backward
    return jnp.stack([got[k] for k in range(count)])


DIGIT = 256
CORES = 2
ROWS_X = 4


def local(
    gate_in,
    mix_in,
    keys_in,
    step_in,
    resid_in,
    kernel_mix,
    kernel_keys,
    step_bias,
    decay_rate,
    skip_gain,
    norm_gain,
    final_gain,
    out_weight,
    head_weight,
    history_mix,
    history_keys,
    start_state,
    lengths,
    continued,
    targets,
    score_flag,
):
    groups = lax.axis_size("tp")
    shards = lax.axis_size("req")
    lane_index = lax.axis_index("tp")
    shard_index = lax.axis_index("req")
    models = gate_in.shape[0]
    step_count = gate_in.shape[1]
    row_count = step_count // groups
    chips_z = shards // (ROWS_X * CORES)
    core_index = shard_index % CORES
    x_index = (shard_index // CORES) % ROWS_X
    z_index = shard_index // (CORES * ROWS_X)
    def along_z(shift):
        return [(i, (i + shift * CORES * ROWS_X) % shards) for i in range(shards)]

    def along_x(shift):
        return [
            (i, (i // (CORES * ROWS_X)) * CORES * ROWS_X
             + (((i // CORES) % ROWS_X + shift) % ROWS_X) * CORES + i % CORES)
            for i in range(shards)
        ]

    def along_core(shift):
        return [(i, i ^ 1) for i in range(shards)]

    vocab_part = head_weight.shape[1]
    partner_weight = lax.ppermute(
        head_weight, "req", [(i, i ^ 1) for i in range(shards)]
    )
    gated = jnp.stack(
        [
            mixer_block(
                gate_in[model_index],
                mix_in[model_index],
                keys_in[model_index],
                step_in[model_index],
                kernel_mix[model_index],
                kernel_keys[model_index],
                step_bias[model_index],
                decay_rate[model_index],
                skip_gain[model_index],
                history_mix[model_index],
                history_keys[model_index],
                start_state[model_index],
                lengths[0],
                continued[0],
            )
            for model_index in range(models)
        ]
    )
    squares = lax.psum(jnp.sum(gated * gated, axis=2), "tp")
    inner_width = gated.shape[2] * groups
    normed = (
        gated * lax.rsqrt(squares / inner_width + EPSILON)[:, :, None] * norm_gain[:, None, :]
    ).astype(jnp.bfloat16)
    first_weight = lax.all_gather(out_weight[0], "req", axis=1, tiled=True)
    ring_weight = ring_gather(
        ring_gather(ring_gather(out_weight[1], along_core, CORES), along_z, chips_z),
        along_x,
        ROWS_X,
    )
    ring_weight = jnp.roll(
        jnp.roll(jnp.roll(ring_weight.transpose(1, 0, 2, 3, 4), z_index, axis=0), x_index, axis=1),
        core_index,
        axis=2,
    )
    second_weight = ring_weight.transpose(3, 0, 1, 2, 4).reshape(
        out_weight.shape[1], shards * out_weight.shape[2]
    )
    partial_out = jnp.stack(
        [
            jnp.dot(normed[0], first_weight, preferred_element_type=jnp.float32),
            jnp.dot(normed[1], second_weight, preferred_element_type=jnp.float32),
        ]
    )
    part_width = resid_in.shape[2]
    partial_out = lax.dynamic_update_slice_in_dim(
        partial_out,
        lax.dynamic_slice_in_dim(partial_out, lane_index * part_width, part_width, 2)
        + resid_in.astype(jnp.float32),
        lane_index * part_width,
        2,
    )
    pieces = lax.all_to_all(
        partial_out.reshape(models, groups, row_count, partial_out.shape[2]),
        "tp",
        split_axis=1,
        concat_axis=1,
        tiled=True,
    )
    hidden = jnp.sum(pieces, axis=1).astype(jnp.bfloat16)
    full_width = hidden.shape[2]
    hidden_float = hidden.astype(jnp.float32)
    final_squares = jnp.sum(hidden_float * hidden_float, axis=2)
    final_rows = (
        hidden_float
        * lax.rsqrt(final_squares / full_width + EPSILON)[:, :, None]
        * final_gain[:, None, :]
    ).astype(jnp.bfloat16)
    own_target = lax.dynamic_slice_in_dim(targets, lane_index * row_count, row_count, 0)
    high_digit = (own_target // DIGIT).astype(jnp.bfloat16)
    low_digit = (own_target % DIGIT).astype(jnp.bfloat16)
    target_row = jnp.zeros((1, full_width), jnp.bfloat16)
    target_row = target_row.at[0, :row_count].set(high_digit)
    target_row = target_row.at[0, row_count : 2 * row_count].set(low_digit)
    packet = jnp.concatenate([final_rows.reshape(models * row_count, full_width), target_row], axis=0)

    every = ring_gather(ring_gather(packet, along_z, chips_z), along_x, ROWS_X)
    peers = ROWS_X * chips_z
    every = every.reshape(peers, models * row_count + 1, full_width)
    every_rows = (
        every[:, : models * row_count]
        .reshape(peers, models, row_count, full_width)
        .transpose(1, 0, 2, 3)
        .reshape(models, peers * row_count, full_width)
    )
    every_target = (
        every[:, models * row_count, :row_count].astype(jnp.int32) * DIGIT
        + every[:, models * row_count, row_count : 2 * row_count].astype(jnp.int32)
    ).reshape(peers * row_count)
    own_logits, own_peak, own_picked = head_scores(
        head_weight, shard_index * vocab_part, every_rows, every_target
    )
    other_logits, other_peak, other_picked = head_scores(
        partner_weight, (shard_index ^ 1) * vocab_part, every_rows, every_target
    )
    peak_logit = jnp.maximum(own_peak, other_peak)
    spread = jnp.sum(jnp.exp(own_logits - peak_logit[:, :, None]), axis=2) + jnp.sum(
        jnp.exp(other_logits - peak_logit[:, :, None]), axis=2
    )
    statistics = jnp.stack([peak_logit, spread, own_picked + other_picked])
    statistics = statistics.reshape(3, models, ROWS_X, chips_z, row_count).transpose(0, 1, 3, 2, 4)
    statistics = jnp.roll(jnp.roll(statistics, z_index, axis=2), x_index, axis=3)
    neutral = jnp.stack(
        [
            jnp.full_like(statistics[0], -1e30),
            jnp.zeros_like(statistics[1]),
            jnp.zeros_like(statistics[2]),
        ]
    )
    send = jnp.stack(
        [jnp.where(core_index == c, statistics, neutral) for c in range(CORES)], axis=4
    ).reshape(3, models, shards, row_count)
    received = lax.all_to_all(send, "req", split_axis=2, concat_axis=2, tiled=True)
    peak_each, spread_each, picked_each = received[0], received[1], received[2]
    peak_logit = jnp.max(peak_each, axis=1)
    spread = jnp.sum(spread_each * jnp.exp(peak_each - peak_logit[:, None, :]), axis=1)
    picked = jnp.sum(picked_each, axis=1)
    scored_rows = lax.dynamic_slice_in_dim(score_flag, lane_index * row_count, row_count, 0).astype(
        jnp.float32
    )
    return (picked - (peak_logit + jnp.log(spread))) * scored_rows[None, :]


def solution(mesh):
    placed = (
        P(None, "req", "tp"),
        P(None, "req", "tp"),
        P(None, "req", None),
        P(None, "req", "tp"),
        P(None, "req", "tp"),
        P(None, None, "tp"),
        P(),
        P(None, "tp"),
        P(None, "tp"),
        P(None, "tp"),
        P(None, "tp"),
        P(),
        P(None, "tp", "req"),
        P(None, "req", None),
        P(None, "req", None, "tp"),
        P(None, "req", None, None),
        P(None, "req", "tp", None),
        P("req", None),
        P("req", None),
        P("req"),
        P("req"),
    )
    return jax.shard_map(
        local, mesh=mesh, in_specs=placed, out_specs=P(None, ("req", "tp")), check_vma=False
    )
```

```python
import jax
import jax.numpy as jnp
from jax import lax
from jax.sharding import PartitionSpec as P

EPSILON = 1e-05
PRECISE = lax.Precision.HIGHEST


def merged_2(part, axis, combine):
    gathered = jax.tree.map(lambda a: lax.all_gather(a, axis), part)

    def take(source):
        return jax.tree.map(lambda a: lax.dynamic_index_in_dim(a, source, 0, False), gathered)

    return lax.fori_loop(
        1, lax.axis_size(axis), lambda source, state: combine(state, take(source)), take(0)
    )


def request_layout(lengths, step_count):
    starts = jnp.cumsum(lengths) - lengths
    time_index = jnp.arange(step_count, dtype=jnp.int32)
    segment = jnp.sum((time_index[:, None] >= starts[None, 1:]).astype(jnp.int32), axis=1)
    member = segment[:, None] == jnp.arange(lengths.shape[0], dtype=jnp.int32)[None, :]
    first_step = jnp.sum(jnp.where(member, starts[None, :], 0), axis=1)
    return (starts, segment, member, time_index - first_step)


def causal_conv(stream, kernel, history, member, offset):
    tap_count = kernel.shape[0]
    history_len = tap_count - 1
    current = stream.astype(jnp.float32)
    member_bf = member.astype(jnp.bfloat16)
    slot_values = [
        jnp.dot(member_bf, history[:, slot_index, :], preferred_element_type=jnp.float32)
        for slot_index in range(history_len)
    ]
    output = kernel[history_len][None, :] * current
    for lag_steps in range(1, tap_count):
        shifted = jnp.concatenate(
            [jnp.zeros((lag_steps, current.shape[1]), current.dtype), current[:-lag_steps]], axis=0
        )
        earlier = jnp.zeros_like(current)
        for slot_index in range(history_len):
            earlier = earlier + jnp.where(
                (offset - lag_steps == slot_index - history_len)[:, None],
                slot_values[slot_index],
                0.0,
            )
        output = output + kernel[history_len - lag_steps][None, :] * jnp.where(
            (offset >= lag_steps)[:, None], shifted, earlier
        )
    return jax.nn.silu(output)


def mixer_block(
    gate_rows,
    mix_rows,
    keys_rows,
    step_raw,
    kernel_mix,
    kernel_keys,
    step_bias,
    decay_rate,
    skip_gain,
    history_mix,
    history_keys,
    start_state,
    lengths,
    continued,
):
    step_count = gate_rows.shape[0]
    head_count = step_raw.shape[1]
    inner_width = mix_rows.shape[1]
    head_size = inner_width // head_count
    states = start_state.shape[2]
    starts, segment, member, offset = request_layout(lengths, step_count)
    keep_state = continued.astype(jnp.bfloat16)
    mixed = causal_conv(
        mix_rows, kernel_mix, history_mix * keep_state[:, None, None], member, offset
    )
    projected = causal_conv(
        keys_rows, kernel_keys, history_keys * keep_state[:, None, None], member, offset
    )
    inject = projected[:, :states]
    readout = projected[:, states:]
    step_size = jax.nn.softplus(step_raw.astype(jnp.float32) + step_bias[None, :])
    log_decay = -step_size * decay_rate[None, :]
    running = jnp.cumsum(log_decay, axis=0)
    time_index = jnp.arange(step_count, dtype=jnp.int32)
    causal = (segment[:, None] == segment[None, :]) & (time_index[:, None] >= time_index[None, :])
    spread = jnp.minimum(running[:, None, :] - running[None, :, :], 0.0)
    transfer = jnp.where(causal[:, :, None], jnp.exp(spread), 0.0)
    intersection = jnp.dot(readout, inject.T, precision=PRECISE)
    kernel_full = transfer * intersection[:, :, None]
    values = mixed.reshape(step_count, head_count, head_size)
    output = jnp.einsum(
        "tsh,shp->thp", kernel_full, step_size[:, :, None] * values, precision=PRECISE
    )
    before = jnp.take(running - log_decay, starts, axis=0)
    member_float = member.astype(jnp.float32)
    entry_level = jnp.dot(member_float, before, precision=PRECISE)
    carried = jnp.exp(jnp.minimum(running - entry_level, 0.0))
    initial = start_state.astype(jnp.float32) * keep_state.astype(jnp.float32)[:, None, None]
    readings = jnp.einsum("tn,rcn->trc", readout, initial, precision=PRECISE)
    chosen = jnp.sum(member_float[:, :, None] * readings, axis=1).reshape(
        step_count, head_count, head_size
    )
    output = output + carried[:, :, None] * chosen + skip_gain[None, :, None] * values
    return output.reshape(step_count, inner_width) * jax.nn.silu(gate_rows.astype(jnp.float32))


def head_scores(head_weight, vocab_start, rows_hidden, rows_target):
    logits = jnp.einsum(
        "mnd,mvd->mnv", rows_hidden, head_weight, preferred_element_type=jnp.float32
    )
    peak_logit = jnp.max(logits, axis=2)
    local_id = rows_target - vocab_start
    matches = jnp.arange(head_weight.shape[1], dtype=jnp.int32)[None, :] == local_id[:, None]
    picked = jnp.sum(jnp.where(matches[None, :, :], logits, 0.0), axis=2)
    return logits, peak_logit, picked


def ring_gather(block, perm_of, count):
    got = {0: block}
    forward = block
    backward = block
    for step in range(1, count // 2 + 1):
        forward = lax.ppermute(forward, "req", perm_of(1))
        got[-step % count] = forward
        if step < count - step:
            backward = lax.ppermute(backward, "req", perm_of(-1))
            got[step] = backward
    return jnp.stack([got[k] for k in range(count)])


DIGIT = 256
SQUARE_COLUMNS = 128
CORES = 2
ROWS_X = 4


def local(
    gate_in,
    mix_in,
    keys_in,
    step_in,
    resid_in,
    kernel_mix,
    kernel_keys,
    step_bias,
    decay_rate,
    skip_gain,
    norm_gain,
    final_gain,
    out_weight,
    head_weight,
    history_mix,
    history_keys,
    start_state,
    lengths,
    continued,
    targets,
    score_flag,
):
    groups = lax.axis_size("tp")
    shards = lax.axis_size("req")
    lane_index = lax.axis_index("tp")
    shard_index = lax.axis_index("req")
    models = gate_in.shape[0]
    step_count = gate_in.shape[1]
    row_count = step_count // groups
    chips_z = shards // (ROWS_X * CORES)
    core_index = shard_index % CORES
    x_index = (shard_index // CORES) % ROWS_X
    z_index = shard_index // (CORES * ROWS_X)
    def along_z(shift):
        return [(i, (i + shift * CORES * ROWS_X) % shards) for i in range(shards)]

    def along_x(shift):
        return [
            (i, (i // (CORES * ROWS_X)) * CORES * ROWS_X
             + (((i // CORES) % ROWS_X + shift) % ROWS_X) * CORES + i % CORES)
            for i in range(shards)
        ]

    def along_core(shift):
        return [(i, i ^ 1) for i in range(shards)]

    vocab_part = head_weight.shape[1]
    partner_weight = lax.ppermute(
        head_weight, "req", [(i, i ^ 1) for i in range(shards)]
    )
    gated = jnp.stack(
        [
            mixer_block(
                gate_in[model_index],
                mix_in[model_index],
                keys_in[model_index],
                step_in[model_index],
                kernel_mix[model_index],
                kernel_keys[model_index],
                step_bias[model_index],
                decay_rate[model_index],
                skip_gain[model_index],
                history_mix[model_index],
                history_keys[model_index],
                start_state[model_index],
                lengths[0],
                continued[0],
            )
            for model_index in range(models)
        ]
    )
    inner_width = gated.shape[2] * groups
    squares = jnp.sum(gated * gated, axis=2)
    unscaled = (gated * norm_gain[:, None, :]).astype(jnp.bfloat16)
    ring_weight = ring_gather(
        ring_gather(ring_gather(out_weight, along_z, chips_z), along_x, ROWS_X),
        along_core,
        CORES,
    )
    ring_weight = jnp.roll(
        jnp.roll(jnp.roll(ring_weight.transpose(2, 1, 0, 3, 4, 5), z_index, axis=0), x_index, axis=1),
        core_index,
        axis=2,
    )
    full_weight = ring_weight.transpose(3, 4, 0, 1, 2, 5).reshape(
        models, out_weight.shape[1], shards * out_weight.shape[2]
    )
    partial_out = jnp.einsum(
        "mtc,mcd->mtd", unscaled, full_weight, preferred_element_type=jnp.float32
    )
    full_width = partial_out.shape[2]
    part_width = resid_in.shape[2]
    extra = jnp.zeros(squares.shape + (SQUARE_COLUMNS,), jnp.float32).at[:, :, 0].set(squares)
    payload = jnp.concatenate([partial_out, resid_in.astype(jnp.float32), extra], axis=2)
    pieces = lax.all_to_all(
        payload.reshape(models, groups, row_count, payload.shape[2]),
        "tp",
        split_axis=1,
        concat_axis=1,
        tiled=True,
    )
    update = jnp.sum(pieces[:, :, :, :full_width], axis=1)
    scale = lax.rsqrt(jnp.sum(pieces[:, :, :, full_width + part_width], axis=1) / inner_width + EPSILON)
    resid_rows = (
        pieces[:, :, :, full_width : full_width + part_width]
        .transpose(0, 2, 1, 3)
        .reshape(models, row_count, groups * part_width)
    )
    hidden = (resid_rows + update * scale[:, :, None]).astype(jnp.bfloat16)
    full_width = hidden.shape[2]
    hidden_float = hidden.astype(jnp.float32)
    final_squares = jnp.sum(hidden_float * hidden_float, axis=2)
    final_rows = (
        hidden_float
        * lax.rsqrt(final_squares / full_width + EPSILON)[:, :, None]
        * final_gain[:, None, :]
    ).astype(jnp.bfloat16)
    own_target = lax.dynamic_slice_in_dim(targets, lane_index * row_count, row_count, 0)
    high_digit = (own_target // DIGIT).astype(jnp.bfloat16)
    low_digit = (own_target % DIGIT).astype(jnp.bfloat16)
    target_row = jnp.zeros((1, full_width), jnp.bfloat16)
    target_row = target_row.at[0, :row_count].set(high_digit)
    target_row = target_row.at[0, row_count : 2 * row_count].set(low_digit)
    packet = jnp.concatenate([final_rows.reshape(models * row_count, full_width), target_row], axis=0)

    every = ring_gather(ring_gather(packet, along_z, chips_z), along_x, ROWS_X)
    peers = ROWS_X * chips_z
    every = every.reshape(peers, models * row_count + 1, full_width)
    every_rows = (
        every[:, : models * row_count]
        .reshape(peers, models, row_count, full_width)
        .transpose(1, 0, 2, 3)
        .reshape(models, peers * row_count, full_width)
    )
    every_target = (
        every[:, models * row_count, :row_count].astype(jnp.int32) * DIGIT
        + every[:, models * row_count, row_count : 2 * row_count].astype(jnp.int32)
    ).reshape(peers * row_count)
    own_logits, own_peak, own_picked = head_scores(
        head_weight, shard_index * vocab_part, every_rows, every_target
    )
    other_logits, other_peak, other_picked = head_scores(
        partner_weight, (shard_index ^ 1) * vocab_part, every_rows, every_target
    )
    peak_logit = jnp.maximum(own_peak, other_peak)
    spread = jnp.sum(jnp.exp(own_logits - peak_logit[:, :, None]), axis=2) + jnp.sum(
        jnp.exp(other_logits - peak_logit[:, :, None]), axis=2
    )
    statistics = jnp.stack([peak_logit, spread, own_picked + other_picked])
    statistics = statistics.reshape(3, models, ROWS_X, chips_z, row_count).transpose(0, 1, 3, 2, 4)
    statistics = jnp.roll(jnp.roll(statistics, z_index, axis=2), x_index, axis=3)
    neutral = jnp.stack(
        [
            jnp.full_like(statistics[0], -1e30),
            jnp.zeros_like(statistics[1]),
            jnp.zeros_like(statistics[2]),
        ]
    )
    send = jnp.stack(
        [jnp.where(core_index == c, statistics, neutral) for c in range(CORES)], axis=4
    ).reshape(3, models, shards, row_count)
    received = lax.all_to_all(send, "req", split_axis=2, concat_axis=2, tiled=True)
    peak_each, spread_each, picked_each = received[0], received[1], received[2]
    peak_logit = jnp.max(peak_each, axis=1)
    spread = jnp.sum(spread_each * jnp.exp(peak_each - peak_logit[:, None, :]), axis=1)
    picked = jnp.sum(picked_each, axis=1)
    scored_rows = lax.dynamic_slice_in_dim(score_flag, lane_index * row_count, row_count, 0).astype(
        jnp.float32
    )
    return (picked - (peak_logit + jnp.log(spread))) * scored_rows[None, :]


def solution(mesh):
    placed = (
        P(None, "req", "tp"),
        P(None, "req", "tp"),
        P(None, "req", None),
        P(None, "req", "tp"),
        P(None, "req", "tp"),
        P(None, None, "tp"),
        P(),
        P(None, "tp"),
        P(None, "tp"),
        P(None, "tp"),
        P(None, "tp"),
        P(),
        P(None, "tp", "req"),
        P(None, "req", None),
        P(None, "req", None, "tp"),
        P(None, "req", None, None),
        P(None, "req", "tp", None),
        P("req", None),
        P("req", None),
        P("req"),
        P("req"),
    )
    return jax.shard_map(
        local, mesh=mesh, in_specs=placed, out_specs=P(None, ("req", "tp")), check_vma=False
    )
```

```python
import jax
import jax.numpy as jnp
from jax import lax
from jax.sharding import PartitionSpec as P

EPSILON = 1e-05
PRECISE = lax.Precision.HIGHEST


def merged_2(part, axis, combine):
    gathered = jax.tree.map(lambda a: lax.all_gather(a, axis), part)

    def take(source):
        return jax.tree.map(lambda a: lax.dynamic_index_in_dim(a, source, 0, False), gathered)

    return lax.fori_loop(
        1, lax.axis_size(axis), lambda source, state: combine(state, take(source)), take(0)
    )


def request_layout(lengths, step_count):
    starts = jnp.cumsum(lengths) - lengths
    time_index = jnp.arange(step_count, dtype=jnp.int32)
    segment = jnp.sum((time_index[:, None] >= starts[None, 1:]).astype(jnp.int32), axis=1)
    member = segment[:, None] == jnp.arange(lengths.shape[0], dtype=jnp.int32)[None, :]
    first_step = jnp.sum(jnp.where(member, starts[None, :], 0), axis=1)
    return (starts, segment, member, time_index - first_step)


def causal_conv(stream, kernel, history, member, offset):
    tap_count = kernel.shape[0]
    history_len = tap_count - 1
    current = stream.astype(jnp.float32)
    member_bf = member.astype(jnp.bfloat16)
    slot_values = [
        jnp.dot(member_bf, history[:, slot_index, :], preferred_element_type=jnp.float32)
        for slot_index in range(history_len)
    ]
    output = kernel[history_len][None, :] * current
    for lag_steps in range(1, tap_count):
        shifted = jnp.concatenate(
            [jnp.zeros((lag_steps, current.shape[1]), current.dtype), current[:-lag_steps]], axis=0
        )
        earlier = jnp.zeros_like(current)
        for slot_index in range(history_len):
            earlier = earlier + jnp.where(
                (offset - lag_steps == slot_index - history_len)[:, None],
                slot_values[slot_index],
                0.0,
            )
        output = output + kernel[history_len - lag_steps][None, :] * jnp.where(
            (offset >= lag_steps)[:, None], shifted, earlier
        )
    return jax.nn.silu(output)


def mixer_block(
    gate_rows,
    mix_rows,
    keys_rows,
    step_raw,
    kernel_mix,
    kernel_keys,
    step_bias,
    decay_rate,
    skip_gain,
    history_mix,
    history_keys,
    start_state,
    lengths,
    continued,
):
    step_count = gate_rows.shape[0]
    head_count = step_raw.shape[1]
    inner_width = mix_rows.shape[1]
    head_size = inner_width // head_count
    states = start_state.shape[2]
    starts, segment, member, offset = request_layout(lengths, step_count)
    keep_state = continued.astype(jnp.bfloat16)
    mixed = causal_conv(
        mix_rows, kernel_mix, history_mix * keep_state[:, None, None], member, offset
    )
    projected = causal_conv(
        keys_rows, kernel_keys, history_keys * keep_state[:, None, None], member, offset
    )
    inject = projected[:, :states]
    readout = projected[:, states:]
    step_size = jax.nn.softplus(step_raw.astype(jnp.float32) + step_bias[None, :])
    log_decay = -step_size * decay_rate[None, :]
    running = jnp.cumsum(log_decay, axis=0)
    time_index = jnp.arange(step_count, dtype=jnp.int32)
    causal = (segment[:, None] == segment[None, :]) & (time_index[:, None] >= time_index[None, :])
    spread = jnp.minimum(running[:, None, :] - running[None, :, :], 0.0)
    transfer = jnp.where(causal[:, :, None], jnp.exp(spread), 0.0)
    intersection = jnp.dot(readout, inject.T, precision=PRECISE)
    kernel_full = transfer * intersection[:, :, None]
    values = mixed.reshape(step_count, head_count, head_size)
    output = jnp.einsum(
        "tsh,shp->thp", kernel_full, step_size[:, :, None] * values, precision=PRECISE
    )
    before = jnp.take(running - log_decay, starts, axis=0)
    member_float = member.astype(jnp.float32)
    entry_level = jnp.dot(member_float, before, precision=PRECISE)
    carried = jnp.exp(jnp.minimum(running - entry_level, 0.0))
    initial = start_state.astype(jnp.float32) * keep_state.astype(jnp.float32)[:, None, None]
    readings = jnp.einsum("tn,rcn->trc", readout, initial, precision=PRECISE)
    chosen = jnp.sum(member_float[:, :, None] * readings, axis=1).reshape(
        step_count, head_count, head_size
    )
    output = output + carried[:, :, None] * chosen + skip_gain[None, :, None] * values
    return output.reshape(step_count, inner_width) * jax.nn.silu(gate_rows.astype(jnp.float32))


def head_scores(head_weight, vocab_start, rows_hidden, rows_target):
    logits = jnp.einsum(
        "mnd,mvd->mnv", rows_hidden, head_weight, preferred_element_type=jnp.float32
    )
    peak_logit = jnp.max(logits, axis=2)
    local_id = rows_target - vocab_start
    matches = jnp.arange(head_weight.shape[1], dtype=jnp.int32)[None, :] == local_id[:, None]
    picked = jnp.sum(jnp.where(matches[None, :, :], logits, 0.0), axis=2)
    return logits, peak_logit, picked


def ring_gather(block, perm_of, count):
    got = {0: block}
    forward = block
    backward = block
    for step in range(1, count // 2 + 1):
        forward = lax.ppermute(forward, "req", perm_of(1))
        got[-step % count] = forward
        if step < count - step:
            backward = lax.ppermute(backward, "req", perm_of(-1))
            got[step] = backward
    return jnp.stack([got[k] for k in range(count)])


DIGIT = 256
SQUARE_COLUMNS = 128
CORES = 2
ROWS_X = 4


def local(
    gate_in,
    mix_in,
    keys_in,
    step_in,
    resid_in,
    kernel_mix,
    kernel_keys,
    step_bias,
    decay_rate,
    skip_gain,
    norm_gain,
    final_gain,
    out_weight,
    head_weight,
    history_mix,
    history_keys,
    start_state,
    lengths,
    continued,
    targets,
    score_flag,
):
    groups = lax.axis_size("tp")
    shards = lax.axis_size("req")
    lane_index = lax.axis_index("tp")
    shard_index = lax.axis_index("req")
    models = gate_in.shape[0]
    step_count = gate_in.shape[1]
    row_count = step_count // groups
    chips_z = shards // (ROWS_X * CORES)
    core_index = shard_index % CORES
    x_index = (shard_index // CORES) % ROWS_X
    z_index = shard_index // (CORES * ROWS_X)
    def along_z(shift):
        return [(i, (i + shift * CORES * ROWS_X) % shards) for i in range(shards)]

    def along_x(shift):
        return [
            (i, (i // (CORES * ROWS_X)) * CORES * ROWS_X
             + (((i // CORES) % ROWS_X + shift) % ROWS_X) * CORES + i % CORES)
            for i in range(shards)
        ]

    def along_core(shift):
        return [(i, i ^ 1) for i in range(shards)]

    vocab_part = head_weight.shape[1]
    partner_weight = lax.ppermute(
        head_weight, "req", [(i, i ^ 1) for i in range(shards)]
    )
    gated = jnp.stack(
        [
            mixer_block(
                gate_in[model_index],
                mix_in[model_index],
                keys_in[model_index],
                step_in[model_index],
                kernel_mix[model_index],
                kernel_keys[model_index],
                step_bias[model_index],
                decay_rate[model_index],
                skip_gain[model_index],
                history_mix[model_index],
                history_keys[model_index],
                start_state[model_index],
                lengths[0],
                continued[0],
            )
            for model_index in range(models)
        ]
    )
    inner_width = gated.shape[2] * groups
    squares = jnp.sum(gated * gated, axis=2)
    unscaled = (gated * norm_gain[:, None, :]).astype(jnp.bfloat16)
    ring_weight = ring_gather(
        ring_gather(ring_gather(out_weight, along_z, chips_z), along_x, ROWS_X),
        along_core,
        CORES,
    )
    ring_weight = jnp.roll(
        jnp.roll(jnp.roll(ring_weight.transpose(2, 1, 0, 3, 4, 5), z_index, axis=0), x_index, axis=1),
        core_index,
        axis=2,
    )
    full_weight = ring_weight.transpose(3, 4, 0, 1, 2, 5).reshape(
        models, out_weight.shape[1], shards * out_weight.shape[2]
    )
    partial_out = jnp.einsum(
        "mtc,mcd->mtd", unscaled, full_weight, preferred_element_type=jnp.float32
    )
    full_width = partial_out.shape[2]
    part_width = resid_in.shape[2]
    square_high = squares.astype(jnp.bfloat16)
    square_low = (squares - square_high.astype(jnp.float32)).astype(jnp.bfloat16)
    extra = (
        jnp.zeros(squares.shape + (SQUARE_COLUMNS,), jnp.bfloat16)
        .at[:, :, 0]
        .set(square_high)
        .at[:, :, 1]
        .set(square_low)
    )
    payload = jnp.concatenate([partial_out.astype(jnp.bfloat16), resid_in, extra], axis=2)
    pieces = lax.all_to_all(
        payload.reshape(models, groups, row_count, payload.shape[2]),
        "tp",
        split_axis=1,
        concat_axis=1,
        tiled=True,
    ).astype(jnp.float32)
    update = jnp.sum(pieces[:, :, :, :full_width], axis=1)
    total_squares = jnp.sum(
        pieces[:, :, :, full_width + part_width] + pieces[:, :, :, full_width + part_width + 1],
        axis=1,
    )
    scale = lax.rsqrt(total_squares / inner_width + EPSILON)
    resid_rows = (
        pieces[:, :, :, full_width : full_width + part_width]
        .transpose(0, 2, 1, 3)
        .reshape(models, row_count, groups * part_width)
    )
    hidden = (resid_rows + update * scale[:, :, None]).astype(jnp.bfloat16)
    full_width = hidden.shape[2]
    hidden_float = hidden.astype(jnp.float32)
    final_squares = jnp.sum(hidden_float * hidden_float, axis=2)
    final_rows = (
        hidden_float
        * lax.rsqrt(final_squares / full_width + EPSILON)[:, :, None]
        * final_gain[:, None, :]
    ).astype(jnp.bfloat16)
    own_target = lax.dynamic_slice_in_dim(targets, lane_index * row_count, row_count, 0)
    high_digit = (own_target // DIGIT).astype(jnp.bfloat16)
    low_digit = (own_target % DIGIT).astype(jnp.bfloat16)
    target_row = jnp.zeros((1, full_width), jnp.bfloat16)
    target_row = target_row.at[0, :row_count].set(high_digit)
    target_row = target_row.at[0, row_count : 2 * row_count].set(low_digit)
    packet = jnp.concatenate([final_rows.reshape(models * row_count, full_width), target_row], axis=0)

    every = ring_gather(ring_gather(packet, along_z, chips_z), along_x, ROWS_X)
    peers = ROWS_X * chips_z
    every = every.reshape(peers, models * row_count + 1, full_width)
    every_rows = (
        every[:, : models * row_count]
        .reshape(peers, models, row_count, full_width)
        .transpose(1, 0, 2, 3)
        .reshape(models, peers * row_count, full_width)
    )
    every_target = (
        every[:, models * row_count, :row_count].astype(jnp.int32) * DIGIT
        + every[:, models * row_count, row_count : 2 * row_count].astype(jnp.int32)
    ).reshape(peers * row_count)
    own_logits, own_peak, own_picked = head_scores(
        head_weight, shard_index * vocab_part, every_rows, every_target
    )
    other_logits, other_peak, other_picked = head_scores(
        partner_weight, (shard_index ^ 1) * vocab_part, every_rows, every_target
    )
    peak_logit = jnp.maximum(own_peak, other_peak)
    spread = jnp.sum(jnp.exp(own_logits - peak_logit[:, :, None]), axis=2) + jnp.sum(
        jnp.exp(other_logits - peak_logit[:, :, None]), axis=2
    )
    statistics = jnp.stack([peak_logit, spread, own_picked + other_picked])
    statistics = statistics.reshape(3, models, ROWS_X, chips_z, row_count).transpose(0, 1, 3, 2, 4)
    statistics = jnp.roll(jnp.roll(statistics, z_index, axis=2), x_index, axis=3)
    neutral = jnp.stack(
        [
            jnp.full_like(statistics[0], -1e30),
            jnp.zeros_like(statistics[1]),
            jnp.zeros_like(statistics[2]),
        ]
    )
    send = jnp.stack(
        [jnp.where(core_index == c, statistics, neutral) for c in range(CORES)], axis=4
    ).reshape(3, models, shards, row_count)
    received = lax.all_to_all(send, "req", split_axis=2, concat_axis=2, tiled=True)
    peak_each, spread_each, picked_each = received[0], received[1], received[2]
    peak_logit = jnp.max(peak_each, axis=1)
    spread = jnp.sum(spread_each * jnp.exp(peak_each - peak_logit[:, None, :]), axis=1)
    picked = jnp.sum(picked_each, axis=1)
    scored_rows = lax.dynamic_slice_in_dim(score_flag, lane_index * row_count, row_count, 0).astype(
        jnp.float32
    )
    return (picked - (peak_logit + jnp.log(spread))) * scored_rows[None, :]


def solution(mesh):
    placed = (
        P(None, "req", "tp"),
        P(None, "req", "tp"),
        P(None, "req", None),
        P(None, "req", "tp"),
        P(None, "req", "tp"),
        P(None, None, "tp"),
        P(),
        P(None, "tp"),
        P(None, "tp"),
        P(None, "tp"),
        P(None, "tp"),
        P(),
        P(None, "tp", "req"),
        P(None, "req", None),
        P(None, "req", None, "tp"),
        P(None, "req", None, None),
        P(None, "req", "tp", None),
        P("req", None),
        P("req", None),
        P("req"),
        P("req"),
    )
    return jax.shard_map(
        local, mesh=mesh, in_specs=placed, out_specs=P(None, ("req", "tp")), check_vma=False
    )
```

```python
import jax
import jax.numpy as jnp
from jax import lax
from jax.sharding import PartitionSpec as P

EPSILON = 1e-05
PRECISE = lax.Precision.HIGHEST


def merged_2(part, axis, combine):
    gathered = jax.tree.map(lambda a: lax.all_gather(a, axis), part)

    def take(source):
        return jax.tree.map(lambda a: lax.dynamic_index_in_dim(a, source, 0, False), gathered)

    return lax.fori_loop(
        1, lax.axis_size(axis), lambda source, state: combine(state, take(source)), take(0)
    )


def request_layout(lengths, step_count):
    starts = jnp.cumsum(lengths) - lengths
    time_index = jnp.arange(step_count, dtype=jnp.int32)
    segment = jnp.sum((time_index[:, None] >= starts[None, 1:]).astype(jnp.int32), axis=1)
    member = segment[:, None] == jnp.arange(lengths.shape[0], dtype=jnp.int32)[None, :]
    first_step = jnp.sum(jnp.where(member, starts[None, :], 0), axis=1)
    return (starts, segment, member, time_index - first_step)


def causal_conv(stream, kernel, history, member, offset):
    tap_count = kernel.shape[0]
    history_len = tap_count - 1
    current = stream.astype(jnp.float32)
    member_bf = member.astype(jnp.bfloat16)
    slot_values = [
        jnp.dot(member_bf, history[:, slot_index, :], preferred_element_type=jnp.float32)
        for slot_index in range(history_len)
    ]
    output = kernel[history_len][None, :] * current
    for lag_steps in range(1, tap_count):
        shifted = jnp.concatenate(
            [jnp.zeros((lag_steps, current.shape[1]), current.dtype), current[:-lag_steps]], axis=0
        )
        earlier = jnp.zeros_like(current)
        for slot_index in range(history_len):
            earlier = earlier + jnp.where(
                (offset - lag_steps == slot_index - history_len)[:, None],
                slot_values[slot_index],
                0.0,
            )
        output = output + kernel[history_len - lag_steps][None, :] * jnp.where(
            (offset >= lag_steps)[:, None], shifted, earlier
        )
    return jax.nn.silu(output)


def mixer_block(
    gate_rows,
    mix_rows,
    keys_rows,
    step_raw,
    kernel_mix,
    kernel_keys,
    step_bias,
    decay_rate,
    skip_gain,
    history_mix,
    history_keys,
    start_state,
    lengths,
    continued,
):
    step_count = gate_rows.shape[0]
    head_count = step_raw.shape[1]
    inner_width = mix_rows.shape[1]
    head_size = inner_width // head_count
    states = start_state.shape[2]
    starts, segment, member, offset = request_layout(lengths, step_count)
    keep_state = continued.astype(jnp.bfloat16)
    mixed = causal_conv(
        mix_rows, kernel_mix, history_mix * keep_state[:, None, None], member, offset
    )
    projected = causal_conv(
        keys_rows, kernel_keys, history_keys * keep_state[:, None, None], member, offset
    )
    inject = projected[:, :states]
    readout = projected[:, states:]
    step_size = jax.nn.softplus(step_raw.astype(jnp.float32) + step_bias[None, :])
    log_decay = -step_size * decay_rate[None, :]
    running = jnp.cumsum(log_decay, axis=0)
    time_index = jnp.arange(step_count, dtype=jnp.int32)
    causal = (segment[:, None] == segment[None, :]) & (time_index[:, None] >= time_index[None, :])
    spread = jnp.minimum(running[:, None, :] - running[None, :, :], 0.0)
    transfer = jnp.where(causal[:, :, None], jnp.exp(spread), 0.0)
    intersection = jnp.dot(readout, inject.T, precision=PRECISE)
    kernel_full = transfer * intersection[:, :, None]
    values = mixed.reshape(step_count, head_count, head_size)
    output = jnp.einsum(
        "tsh,shp->thp", kernel_full, step_size[:, :, None] * values, precision=PRECISE
    )
    before = jnp.take(running - log_decay, starts, axis=0)
    member_float = member.astype(jnp.float32)
    entry_level = jnp.dot(member_float, before, precision=PRECISE)
    carried = jnp.exp(jnp.minimum(running - entry_level, 0.0))
    initial = start_state.astype(jnp.float32) * keep_state.astype(jnp.float32)[:, None, None]
    readings = jnp.einsum("tn,rcn->trc", readout, initial, precision=PRECISE)
    chosen = jnp.sum(member_float[:, :, None] * readings, axis=1).reshape(
        step_count, head_count, head_size
    )
    output = output + carried[:, :, None] * chosen + skip_gain[None, :, None] * values
    return output.reshape(step_count, inner_width) * jax.nn.silu(gate_rows.astype(jnp.float32))


def head_scores(head_weight, vocab_start, rows_hidden, rows_target):
    logits = jnp.einsum(
        "mnd,mvd->mnv", rows_hidden, head_weight, preferred_element_type=jnp.float32
    )
    peak_logit = jnp.max(logits, axis=2)
    local_id = rows_target - vocab_start
    matches = jnp.arange(head_weight.shape[1], dtype=jnp.int32)[None, :] == local_id[:, None]
    picked = jnp.sum(jnp.where(matches[None, :, :], logits, 0.0), axis=2)
    return logits, peak_logit, picked


def ring_gather(block, perm_of, count):
    got = {0: block}
    forward = block
    backward = block
    for step in range(1, count // 2 + 1):
        forward = lax.ppermute(forward, "req", perm_of(1))
        got[-step % count] = forward
        if step < count - step:
            backward = lax.ppermute(backward, "req", perm_of(-1))
            got[step] = backward
    return jnp.stack([got[k] for k in range(count)])


def direct_gather(block, perm_of, count):
    got = {0: block}
    for shift in range(1, count):
        got[-shift % count] = lax.ppermute(block, "req", perm_of(shift))
    return jnp.stack([got[k] for k in range(count)])


DIGIT = 256
SQUARE_COLUMNS = 128
CORES = 2
ROWS_X = 4


def local(
    gate_in,
    mix_in,
    keys_in,
    step_in,
    resid_in,
    kernel_mix,
    kernel_keys,
    step_bias,
    decay_rate,
    skip_gain,
    norm_gain,
    final_gain,
    out_weight,
    head_weight,
    history_mix,
    history_keys,
    start_state,
    lengths,
    continued,
    targets,
    score_flag,
):
    groups = lax.axis_size("tp")
    shards = lax.axis_size("req")
    lane_index = lax.axis_index("tp")
    shard_index = lax.axis_index("req")
    models = gate_in.shape[0]
    step_count = gate_in.shape[1]
    row_count = step_count // groups
    chips_z = shards // (ROWS_X * CORES)
    core_index = shard_index % CORES
    x_index = (shard_index // CORES) % ROWS_X
    z_index = shard_index // (CORES * ROWS_X)
    def along_z(shift):
        return [(i, (i + shift * CORES * ROWS_X) % shards) for i in range(shards)]

    def along_x(shift):
        return [
            (i, (i // (CORES * ROWS_X)) * CORES * ROWS_X
             + (((i // CORES) % ROWS_X + shift) % ROWS_X) * CORES + i % CORES)
            for i in range(shards)
        ]

    def along_core(shift):
        return [(i, i ^ 1) for i in range(shards)]

    vocab_part = head_weight.shape[1]
    partner_weight = lax.ppermute(
        head_weight, "req", [(i, i ^ 1) for i in range(shards)]
    )
    gated = jnp.stack(
        [
            mixer_block(
                gate_in[model_index],
                mix_in[model_index],
                keys_in[model_index],
                step_in[model_index],
                kernel_mix[model_index],
                kernel_keys[model_index],
                step_bias[model_index],
                decay_rate[model_index],
                skip_gain[model_index],
                history_mix[model_index],
                history_keys[model_index],
                start_state[model_index],
                lengths[0],
                continued[0],
            )
            for model_index in range(models)
        ]
    )
    inner_width = gated.shape[2] * groups
    squares = jnp.sum(gated * gated, axis=2)
    unscaled = (gated * norm_gain[:, None, :]).astype(jnp.bfloat16)
    ring_weight = ring_gather(
        direct_gather(direct_gather(out_weight, along_z, chips_z), along_x, ROWS_X),
        along_core,
        CORES,
    )
    ring_weight = jnp.roll(
        jnp.roll(jnp.roll(ring_weight.transpose(2, 1, 0, 3, 4, 5), z_index, axis=0), x_index, axis=1),
        core_index,
        axis=2,
    )
    full_weight = ring_weight.transpose(3, 4, 0, 1, 2, 5).reshape(
        models, out_weight.shape[1], shards * out_weight.shape[2]
    )
    partial_out = jnp.einsum(
        "mtc,mcd->mtd", unscaled, full_weight, preferred_element_type=jnp.float32
    )
    full_width = partial_out.shape[2]
    part_width = resid_in.shape[2]
    square_high = squares.astype(jnp.bfloat16)
    square_low = (squares - square_high.astype(jnp.float32)).astype(jnp.bfloat16)
    extra = (
        jnp.zeros(squares.shape + (SQUARE_COLUMNS,), jnp.bfloat16)
        .at[:, :, 0]
        .set(square_high)
        .at[:, :, 1]
        .set(square_low)
    )
    payload = jnp.concatenate([partial_out.astype(jnp.bfloat16), resid_in, extra], axis=2)
    pieces = lax.all_to_all(
        payload.reshape(models, groups, row_count, payload.shape[2]),
        "tp",
        split_axis=1,
        concat_axis=1,
        tiled=True,
    ).astype(jnp.float32)
    update = jnp.sum(pieces[:, :, :, :full_width], axis=1)
    total_squares = jnp.sum(
        pieces[:, :, :, full_width + part_width] + pieces[:, :, :, full_width + part_width + 1],
        axis=1,
    )
    scale = lax.rsqrt(total_squares / inner_width + EPSILON)
    resid_rows = (
        pieces[:, :, :, full_width : full_width + part_width]
        .transpose(0, 2, 1, 3)
        .reshape(models, row_count, groups * part_width)
    )
    hidden = (resid_rows + update * scale[:, :, None]).astype(jnp.bfloat16)
    full_width = hidden.shape[2]
    hidden_float = hidden.astype(jnp.float32)
    final_squares = jnp.sum(hidden_float * hidden_float, axis=2)
    final_rows = (
        hidden_float
        * lax.rsqrt(final_squares / full_width + EPSILON)[:, :, None]
        * final_gain[:, None, :]
    ).astype(jnp.bfloat16)
    own_target = lax.dynamic_slice_in_dim(targets, lane_index * row_count, row_count, 0)
    high_digit = (own_target // DIGIT).astype(jnp.bfloat16)
    low_digit = (own_target % DIGIT).astype(jnp.bfloat16)
    target_row = jnp.zeros((1, full_width), jnp.bfloat16)
    target_row = target_row.at[0, :row_count].set(high_digit)
    target_row = target_row.at[0, row_count : 2 * row_count].set(low_digit)
    packet = jnp.concatenate([final_rows.reshape(models * row_count, full_width), target_row], axis=0)

    every = direct_gather(direct_gather(packet, along_z, chips_z), along_x, ROWS_X)
    peers = ROWS_X * chips_z
    every = every.reshape(peers, models * row_count + 1, full_width)
    every_rows = (
        every[:, : models * row_count]
        .reshape(peers, models, row_count, full_width)
        .transpose(1, 0, 2, 3)
        .reshape(models, peers * row_count, full_width)
    )
    every_target = (
        every[:, models * row_count, :row_count].astype(jnp.int32) * DIGIT
        + every[:, models * row_count, row_count : 2 * row_count].astype(jnp.int32)
    ).reshape(peers * row_count)
    own_logits, own_peak, own_picked = head_scores(
        head_weight, shard_index * vocab_part, every_rows, every_target
    )
    other_logits, other_peak, other_picked = head_scores(
        partner_weight, (shard_index ^ 1) * vocab_part, every_rows, every_target
    )
    peak_logit = jnp.maximum(own_peak, other_peak)
    spread = jnp.sum(jnp.exp(own_logits - peak_logit[:, :, None]), axis=2) + jnp.sum(
        jnp.exp(other_logits - peak_logit[:, :, None]), axis=2
    )
    statistics = jnp.stack([peak_logit, spread, own_picked + other_picked])
    statistics = statistics.reshape(3, models, ROWS_X, chips_z, row_count).transpose(0, 1, 3, 2, 4)
    statistics = jnp.roll(jnp.roll(statistics, z_index, axis=2), x_index, axis=3)
    neutral = jnp.stack(
        [
            jnp.full_like(statistics[0], -1e30),
            jnp.zeros_like(statistics[1]),
            jnp.zeros_like(statistics[2]),
        ]
    )
    send = jnp.stack(
        [jnp.where(core_index == c, statistics, neutral) for c in range(CORES)], axis=4
    ).reshape(3, models, shards, row_count)
    received = lax.all_to_all(send, "req", split_axis=2, concat_axis=2, tiled=True)
    peak_each, spread_each, picked_each = received[0], received[1], received[2]
    peak_logit = jnp.max(peak_each, axis=1)
    spread = jnp.sum(spread_each * jnp.exp(peak_each - peak_logit[:, None, :]), axis=1)
    picked = jnp.sum(picked_each, axis=1)
    scored_rows = lax.dynamic_slice_in_dim(score_flag, lane_index * row_count, row_count, 0).astype(
        jnp.float32
    )
    return (picked - (peak_logit + jnp.log(spread))) * scored_rows[None, :]


def solution(mesh):
    placed = (
        P(None, "req", "tp"),
        P(None, "req", "tp"),
        P(None, "req", None),
        P(None, "req", "tp"),
        P(None, "req", "tp"),
        P(None, None, "tp"),
        P(),
        P(None, "tp"),
        P(None, "tp"),
        P(None, "tp"),
        P(None, "tp"),
        P(),
        P(None, "tp", "req"),
        P(None, "req", None),
        P(None, "req", None, "tp"),
        P(None, "req", None, None),
        P(None, "req", "tp", None),
        P("req", None),
        P("req", None),
        P("req"),
        P("req"),
    )
    return jax.shard_map(
        local, mesh=mesh, in_specs=placed, out_specs=P(None, ("req", "tp")), check_vma=False
    )
```

```python
import jax
import jax.numpy as jnp
from jax import lax
from jax.sharding import PartitionSpec as P

EPSILON = 1e-05
PRECISE = lax.Precision.HIGHEST


def merged_2(part, axis, combine):
    gathered = jax.tree.map(lambda a: lax.all_gather(a, axis), part)

    def take(source):
        return jax.tree.map(lambda a: lax.dynamic_index_in_dim(a, source, 0, False), gathered)

    return lax.fori_loop(
        1, lax.axis_size(axis), lambda source, state: combine(state, take(source)), take(0)
    )


def request_layout(lengths, step_count):
    starts = jnp.cumsum(lengths) - lengths
    time_index = jnp.arange(step_count, dtype=jnp.int32)
    segment = jnp.sum((time_index[:, None] >= starts[None, 1:]).astype(jnp.int32), axis=1)
    member = segment[:, None] == jnp.arange(lengths.shape[0], dtype=jnp.int32)[None, :]
    first_step = jnp.sum(jnp.where(member, starts[None, :], 0), axis=1)
    return (starts, segment, member, time_index - first_step)


def causal_conv(stream, kernel, history, member, offset):
    tap_count = kernel.shape[0]
    history_len = tap_count - 1
    current = stream.astype(jnp.float32)
    member_bf = member.astype(jnp.bfloat16)
    slot_values = [
        jnp.dot(member_bf, history[:, slot_index, :], preferred_element_type=jnp.float32)
        for slot_index in range(history_len)
    ]
    output = kernel[history_len][None, :] * current
    for lag_steps in range(1, tap_count):
        shifted = jnp.concatenate(
            [jnp.zeros((lag_steps, current.shape[1]), current.dtype), current[:-lag_steps]], axis=0
        )
        earlier = jnp.zeros_like(current)
        for slot_index in range(history_len):
            earlier = earlier + jnp.where(
                (offset - lag_steps == slot_index - history_len)[:, None],
                slot_values[slot_index],
                0.0,
            )
        output = output + kernel[history_len - lag_steps][None, :] * jnp.where(
            (offset >= lag_steps)[:, None], shifted, earlier
        )
    return jax.nn.silu(output)


def mixer_block(
    gate_rows,
    mix_rows,
    keys_rows,
    step_raw,
    kernel_mix,
    kernel_keys,
    step_bias,
    decay_rate,
    skip_gain,
    history_mix,
    history_keys,
    start_state,
    lengths,
    continued,
):
    step_count = gate_rows.shape[0]
    head_count = step_raw.shape[1]
    inner_width = mix_rows.shape[1]
    head_size = inner_width // head_count
    states = start_state.shape[2]
    starts, segment, member, offset = request_layout(lengths, step_count)
    keep_state = continued.astype(jnp.bfloat16)
    mixed = causal_conv(
        mix_rows, kernel_mix, history_mix * keep_state[:, None, None], member, offset
    )
    projected = causal_conv(
        keys_rows, kernel_keys, history_keys * keep_state[:, None, None], member, offset
    )
    inject = projected[:, :states]
    readout = projected[:, states:]
    step_size = jax.nn.softplus(step_raw.astype(jnp.float32) + step_bias[None, :])
    log_decay = -step_size * decay_rate[None, :]
    running = jnp.cumsum(log_decay, axis=0)
    time_index = jnp.arange(step_count, dtype=jnp.int32)
    causal = (segment[:, None] == segment[None, :]) & (time_index[:, None] >= time_index[None, :])
    spread = jnp.minimum(running[:, None, :] - running[None, :, :], 0.0)
    transfer = jnp.where(causal[:, :, None], jnp.exp(spread), 0.0)
    intersection = jnp.dot(readout, inject.T, precision=PRECISE)
    kernel_full = transfer * intersection[:, :, None]
    values = mixed.reshape(step_count, head_count, head_size)
    output = jnp.einsum(
        "tsh,shp->thp", kernel_full, step_size[:, :, None] * values, precision=PRECISE
    )
    before = jnp.take(running - log_decay, starts, axis=0)
    member_float = member.astype(jnp.float32)
    entry_level = jnp.dot(member_float, before, precision=PRECISE)
    carried = jnp.exp(jnp.minimum(running - entry_level, 0.0))
    initial = start_state.astype(jnp.float32) * keep_state.astype(jnp.float32)[:, None, None]
    readings = jnp.einsum("tn,rcn->trc", readout, initial, precision=PRECISE)
    chosen = jnp.sum(member_float[:, :, None] * readings, axis=1).reshape(
        step_count, head_count, head_size
    )
    output = output + carried[:, :, None] * chosen + skip_gain[None, :, None] * values
    return output.reshape(step_count, inner_width) * jax.nn.silu(gate_rows.astype(jnp.float32))


def head_scores(head_weight, vocab_start, rows_hidden, rows_target):
    logits = jnp.einsum(
        "mnd,mvd->mnv", rows_hidden, head_weight, preferred_element_type=jnp.float32
    )
    peak_logit = jnp.max(logits, axis=2)
    local_id = rows_target - vocab_start
    matches = jnp.arange(head_weight.shape[1], dtype=jnp.int32)[None, :] == local_id[:, None]
    picked = jnp.sum(jnp.where(matches[None, :, :], logits, 0.0), axis=2)
    return logits, peak_logit, picked


def ring_gather(block, perm_of, count):
    got = {0: block}
    forward = block
    backward = block
    for step in range(1, count // 2 + 1):
        forward = lax.ppermute(forward, "req", perm_of(1))
        got[-step % count] = forward
        if step < count - step:
            backward = lax.ppermute(backward, "req", perm_of(-1))
            got[step] = backward
    return jnp.stack([got[k] for k in range(count)])


def doubling_gather(block, coord, stride, count, shards):
    gathered = block[None]
    distance = 1
    while distance < count:
        theirs = lax.ppermute(
            gathered, "req", [(i, i ^ (distance * stride)) for i in range(shards)]
        )
        upper = (coord // distance) % 2 == 1
        gathered = jnp.where(
            upper,
            jnp.concatenate([theirs, gathered], axis=0),
            jnp.concatenate([gathered, theirs], axis=0),
        )
        distance *= 2
    return gathered


DIGIT = 256
SQUARE_COLUMNS = 128
CORES = 2
ROWS_X = 4


def local(
    gate_in,
    mix_in,
    keys_in,
    step_in,
    resid_in,
    kernel_mix,
    kernel_keys,
    step_bias,
    decay_rate,
    skip_gain,
    norm_gain,
    final_gain,
    out_weight,
    head_weight,
    history_mix,
    history_keys,
    start_state,
    lengths,
    continued,
    targets,
    score_flag,
):
    groups = lax.axis_size("tp")
    shards = lax.axis_size("req")
    lane_index = lax.axis_index("tp")
    shard_index = lax.axis_index("req")
    models = gate_in.shape[0]
    step_count = gate_in.shape[1]
    row_count = step_count // groups
    chips_z = shards // (ROWS_X * CORES)
    core_index = shard_index % CORES
    x_index = (shard_index // CORES) % ROWS_X
    z_index = shard_index // (CORES * ROWS_X)
    def along_z(shift):
        return [(i, (i + shift * CORES * ROWS_X) % shards) for i in range(shards)]

    def along_x(shift):
        return [
            (i, (i // (CORES * ROWS_X)) * CORES * ROWS_X
             + (((i // CORES) % ROWS_X + shift) % ROWS_X) * CORES + i % CORES)
            for i in range(shards)
        ]

    def along_core(shift):
        return [(i, i ^ 1) for i in range(shards)]

    vocab_part = head_weight.shape[1]
    partner_weight = lax.ppermute(
        head_weight, "req", [(i, i ^ 1) for i in range(shards)]
    )
    gated = jnp.stack(
        [
            mixer_block(
                gate_in[model_index],
                mix_in[model_index],
                keys_in[model_index],
                step_in[model_index],
                kernel_mix[model_index],
                kernel_keys[model_index],
                step_bias[model_index],
                decay_rate[model_index],
                skip_gain[model_index],
                history_mix[model_index],
                history_keys[model_index],
                start_state[model_index],
                lengths[0],
                continued[0],
            )
            for model_index in range(models)
        ]
    )
    inner_width = gated.shape[2] * groups
    squares = jnp.sum(gated * gated, axis=2)
    unscaled = (gated * norm_gain[:, None, :]).astype(jnp.bfloat16)
    gathered_weight = doubling_gather(
        doubling_gather(
            doubling_gather(out_weight, z_index, CORES * ROWS_X, chips_z, shards),
            x_index,
            CORES,
            ROWS_X,
            shards,
        ),
        core_index,
        1,
        CORES,
        shards,
    )
    full_weight = gathered_weight.transpose(3, 4, 2, 1, 0, 5).reshape(
        models, out_weight.shape[1], shards * out_weight.shape[2]
    )
    partial_out = jnp.einsum(
        "mtc,mcd->mtd", unscaled, full_weight, preferred_element_type=jnp.float32
    )
    full_width = partial_out.shape[2]
    part_width = resid_in.shape[2]
    square_high = squares.astype(jnp.bfloat16)
    square_low = (squares - square_high.astype(jnp.float32)).astype(jnp.bfloat16)
    extra = (
        jnp.zeros(squares.shape + (SQUARE_COLUMNS,), jnp.bfloat16)
        .at[:, :, 0]
        .set(square_high)
        .at[:, :, 1]
        .set(square_low)
    )
    payload = jnp.concatenate([partial_out.astype(jnp.bfloat16), resid_in, extra], axis=2)
    pieces = lax.all_to_all(
        payload.reshape(models, groups, row_count, payload.shape[2]),
        "tp",
        split_axis=1,
        concat_axis=1,
        tiled=True,
    ).astype(jnp.float32)
    update = jnp.sum(pieces[:, :, :, :full_width], axis=1)
    total_squares = jnp.sum(
        pieces[:, :, :, full_width + part_width] + pieces[:, :, :, full_width + part_width + 1],
        axis=1,
    )
    scale = lax.rsqrt(total_squares / inner_width + EPSILON)
    resid_rows = (
        pieces[:, :, :, full_width : full_width + part_width]
        .transpose(0, 2, 1, 3)
        .reshape(models, row_count, groups * part_width)
    )
    hidden = (resid_rows + update * scale[:, :, None]).astype(jnp.bfloat16)
    full_width = hidden.shape[2]
    hidden_float = hidden.astype(jnp.float32)
    final_squares = jnp.sum(hidden_float * hidden_float, axis=2)
    final_rows = (
        hidden_float
        * lax.rsqrt(final_squares / full_width + EPSILON)[:, :, None]
        * final_gain[:, None, :]
    ).astype(jnp.bfloat16)
    own_target = lax.dynamic_slice_in_dim(targets, lane_index * row_count, row_count, 0)
    high_digit = (own_target // DIGIT).astype(jnp.bfloat16)
    low_digit = (own_target % DIGIT).astype(jnp.bfloat16)
    target_row = jnp.zeros((1, full_width), jnp.bfloat16)
    target_row = target_row.at[0, :row_count].set(high_digit)
    target_row = target_row.at[0, row_count : 2 * row_count].set(low_digit)
    packet = jnp.concatenate([final_rows.reshape(models * row_count, full_width), target_row], axis=0)

    every = doubling_gather(
        doubling_gather(packet, z_index, CORES * ROWS_X, chips_z, shards), x_index, CORES, ROWS_X, shards
    )
    peers = ROWS_X * chips_z
    every = every.reshape(peers, models * row_count + 1, full_width)
    every_rows = (
        every[:, : models * row_count]
        .reshape(peers, models, row_count, full_width)
        .transpose(1, 0, 2, 3)
        .reshape(models, peers * row_count, full_width)
    )
    every_target = (
        every[:, models * row_count, :row_count].astype(jnp.int32) * DIGIT
        + every[:, models * row_count, row_count : 2 * row_count].astype(jnp.int32)
    ).reshape(peers * row_count)
    own_logits, own_peak, own_picked = head_scores(
        head_weight, shard_index * vocab_part, every_rows, every_target
    )
    other_logits, other_peak, other_picked = head_scores(
        partner_weight, (shard_index ^ 1) * vocab_part, every_rows, every_target
    )
    peak_logit = jnp.maximum(own_peak, other_peak)
    spread = jnp.sum(jnp.exp(own_logits - peak_logit[:, :, None]), axis=2) + jnp.sum(
        jnp.exp(other_logits - peak_logit[:, :, None]), axis=2
    )
    statistics = jnp.stack([peak_logit, spread, own_picked + other_picked])
    statistics = statistics.reshape(3, models, ROWS_X, chips_z, row_count).transpose(0, 1, 3, 2, 4)
    neutral = jnp.stack(
        [
            jnp.full_like(statistics[0], -1e30),
            jnp.zeros_like(statistics[1]),
            jnp.zeros_like(statistics[2]),
        ]
    )
    send = jnp.stack(
        [jnp.where(core_index == c, statistics, neutral) for c in range(CORES)], axis=4
    ).reshape(3, models, shards, row_count)
    received = lax.all_to_all(send, "req", split_axis=2, concat_axis=2, tiled=True)
    peak_each, spread_each, picked_each = received[0], received[1], received[2]
    peak_logit = jnp.max(peak_each, axis=1)
    spread = jnp.sum(spread_each * jnp.exp(peak_each - peak_logit[:, None, :]), axis=1)
    picked = jnp.sum(picked_each, axis=1)
    scored_rows = lax.dynamic_slice_in_dim(score_flag, lane_index * row_count, row_count, 0).astype(
        jnp.float32
    )
    return (picked - (peak_logit + jnp.log(spread))) * scored_rows[None, :]


def solution(mesh):
    placed = (
        P(None, "req", "tp"),
        P(None, "req", "tp"),
        P(None, "req", None),
        P(None, "req", "tp"),
        P(None, "req", "tp"),
        P(None, None, "tp"),
        P(),
        P(None, "tp"),
        P(None, "tp"),
        P(None, "tp"),
        P(None, "tp"),
        P(),
        P(None, "tp", "req"),
        P(None, "req", None),
        P(None, "req", None, "tp"),
        P(None, "req", None, None),
        P(None, "req", "tp", None),
        P("req", None),
        P("req", None),
        P("req"),
        P("req"),
    )
    return jax.shard_map(
        local, mesh=mesh, in_specs=placed, out_specs=P(None, ("req", "tp")), check_vma=False
    )
```

```python
import jax
import jax.numpy as jnp
from jax import lax
from jax.sharding import PartitionSpec as P

EPSILON = 1e-05
PRECISE = lax.Precision.HIGHEST


def merged_2(part, axis, combine):
    gathered = jax.tree.map(lambda a: lax.all_gather(a, axis), part)

    def take(source):
        return jax.tree.map(lambda a: lax.dynamic_index_in_dim(a, source, 0, False), gathered)

    return lax.fori_loop(
        1, lax.axis_size(axis), lambda source, state: combine(state, take(source)), take(0)
    )


def request_layout(lengths, step_count):
    starts = jnp.cumsum(lengths) - lengths
    time_index = jnp.arange(step_count, dtype=jnp.int32)
    segment = jnp.sum((time_index[:, None] >= starts[None, 1:]).astype(jnp.int32), axis=1)
    member = segment[:, None] == jnp.arange(lengths.shape[0], dtype=jnp.int32)[None, :]
    first_step = jnp.sum(jnp.where(member, starts[None, :], 0), axis=1)
    return (starts, segment, member, time_index - first_step)


def causal_conv(stream, kernel, history, member, offset):
    tap_count = kernel.shape[0]
    history_len = tap_count - 1
    current = stream.astype(jnp.float32)
    member_bf = member.astype(jnp.bfloat16)
    slot_values = [
        jnp.dot(member_bf, history[:, slot_index, :], preferred_element_type=jnp.float32)
        for slot_index in range(history_len)
    ]
    output = kernel[history_len][None, :] * current
    for lag_steps in range(1, tap_count):
        shifted = jnp.concatenate(
            [jnp.zeros((lag_steps, current.shape[1]), current.dtype), current[:-lag_steps]], axis=0
        )
        earlier = jnp.zeros_like(current)
        for slot_index in range(history_len):
            earlier = earlier + jnp.where(
                (offset - lag_steps == slot_index - history_len)[:, None],
                slot_values[slot_index],
                0.0,
            )
        output = output + kernel[history_len - lag_steps][None, :] * jnp.where(
            (offset >= lag_steps)[:, None], shifted, earlier
        )
    return jax.nn.silu(output)


def mixer_block(
    gate_rows,
    mix_rows,
    keys_rows,
    step_raw,
    kernel_mix,
    kernel_keys,
    step_bias,
    decay_rate,
    skip_gain,
    history_mix,
    history_keys,
    start_state,
    lengths,
    continued,
):
    step_count = gate_rows.shape[0]
    head_count = step_raw.shape[1]
    inner_width = mix_rows.shape[1]
    head_size = inner_width // head_count
    states = start_state.shape[2]
    starts, segment, member, offset = request_layout(lengths, step_count)
    keep_state = continued.astype(jnp.bfloat16)
    mixed = causal_conv(
        mix_rows, kernel_mix, history_mix * keep_state[:, None, None], member, offset
    )
    projected = causal_conv(
        keys_rows, kernel_keys, history_keys * keep_state[:, None, None], member, offset
    )
    inject = projected[:, :states]
    readout = projected[:, states:]
    step_size = jax.nn.softplus(step_raw.astype(jnp.float32) + step_bias[None, :])
    log_decay = -step_size * decay_rate[None, :]
    running = jnp.cumsum(log_decay, axis=0)
    time_index = jnp.arange(step_count, dtype=jnp.int32)
    causal = (segment[:, None] == segment[None, :]) & (time_index[:, None] >= time_index[None, :])
    spread = jnp.minimum(running[:, None, :] - running[None, :, :], 0.0)
    transfer = jnp.where(causal[:, :, None], jnp.exp(spread), 0.0)
    intersection = jnp.dot(readout, inject.T, precision=PRECISE)
    kernel_full = transfer * intersection[:, :, None]
    values = mixed.reshape(step_count, head_count, head_size)
    output = jnp.einsum(
        "tsh,shp->thp", kernel_full, step_size[:, :, None] * values, precision=PRECISE
    )
    before = jnp.take(running - log_decay, starts, axis=0)
    member_float = member.astype(jnp.float32)
    entry_level = jnp.dot(member_float, before, precision=PRECISE)
    carried = jnp.exp(jnp.minimum(running - entry_level, 0.0))
    initial = start_state.astype(jnp.float32) * keep_state.astype(jnp.float32)[:, None, None]
    readings = jnp.einsum("tn,rcn->trc", readout, initial, precision=PRECISE)
    chosen = jnp.sum(member_float[:, :, None] * readings, axis=1).reshape(
        step_count, head_count, head_size
    )
    output = output + carried[:, :, None] * chosen + skip_gain[None, :, None] * values
    return output.reshape(step_count, inner_width) * jax.nn.silu(gate_rows.astype(jnp.float32))


def head_scores(head_weight, vocab_start, rows_hidden, rows_target):
    logits = jnp.einsum(
        "mnd,mvd->mnv", rows_hidden, head_weight, preferred_element_type=jnp.float32
    )
    peak_logit = jnp.max(logits, axis=2)
    local_id = rows_target - vocab_start
    matches = jnp.arange(head_weight.shape[1], dtype=jnp.int32)[None, :] == local_id[:, None]
    picked = jnp.sum(jnp.where(matches[None, :, :], logits, 0.0), axis=2)
    return logits, peak_logit, picked


def ring_gather(block, perm_of, count):
    got = {0: block}
    forward = block
    backward = block
    for step in range(1, count // 2 + 1):
        forward = lax.ppermute(forward, "req", perm_of(1))
        got[-step % count] = forward
        if step < count - step:
            backward = lax.ppermute(backward, "req", perm_of(-1))
            got[step] = backward
    return jnp.stack([got[k] for k in range(count)])


DIGIT = 256
SQUARE_COLUMNS = 128
CORES = 2
ROWS_X = 4


def local(
    gate_in,
    mix_in,
    keys_in,
    step_in,
    resid_in,
    kernel_mix,
    kernel_keys,
    step_bias,
    decay_rate,
    skip_gain,
    norm_gain,
    final_gain,
    out_weight,
    head_weight,
    history_mix,
    history_keys,
    start_state,
    lengths,
    continued,
    targets,
    score_flag,
):
    groups = lax.axis_size("tp")
    shards = lax.axis_size("req")
    lane_index = lax.axis_index("tp")
    shard_index = lax.axis_index("req")
    models = gate_in.shape[0]
    step_count = gate_in.shape[1]
    row_count = step_count // groups
    chips_z = shards // (ROWS_X * CORES)
    core_index = shard_index % CORES
    x_index = (shard_index // CORES) % ROWS_X
    z_index = shard_index // (CORES * ROWS_X)
    def along_z(shift):
        return [(i, (i + shift * CORES * ROWS_X) % shards) for i in range(shards)]

    def along_x(shift):
        return [
            (i, (i // (CORES * ROWS_X)) * CORES * ROWS_X
             + (((i // CORES) % ROWS_X + shift) % ROWS_X) * CORES + i % CORES)
            for i in range(shards)
        ]

    def along_core(shift):
        return [(i, i ^ 1) for i in range(shards)]

    vocab_part = head_weight.shape[1]
    partner_weight = lax.ppermute(
        head_weight, "req", [(i, i ^ 1) for i in range(shards)]
    )
    gated = jnp.stack(
        [
            mixer_block(
                gate_in[model_index],
                mix_in[model_index],
                keys_in[model_index],
                step_in[model_index],
                kernel_mix[model_index],
                kernel_keys[model_index],
                step_bias[model_index],
                decay_rate[model_index],
                skip_gain[model_index],
                history_mix[model_index],
                history_keys[model_index],
                start_state[model_index],
                lengths[0],
                continued[0],
            )
            for model_index in range(models)
        ]
    )
    inner_width = gated.shape[2] * groups
    squares = jnp.sum(gated * gated, axis=2)
    unscaled = (gated * norm_gain[:, None, :]).astype(jnp.bfloat16)
    ring_weight = ring_gather(
        ring_gather(ring_gather(out_weight, along_x, ROWS_X), along_z, chips_z),
        along_core,
        CORES,
    )
    ring_weight = jnp.roll(
        jnp.roll(jnp.roll(ring_weight.transpose(1, 2, 0, 3, 4, 5), z_index, axis=0), x_index, axis=1),
        core_index,
        axis=2,
    )
    full_weight = ring_weight.transpose(3, 4, 0, 1, 2, 5).reshape(
        models, out_weight.shape[1], shards * out_weight.shape[2]
    )
    partial_out = jnp.einsum(
        "mtc,mcd->mtd", unscaled, full_weight, preferred_element_type=jnp.float32
    )
    full_width = partial_out.shape[2]
    part_width = resid_in.shape[2]
    square_high = squares.astype(jnp.bfloat16)
    square_low = (squares - square_high.astype(jnp.float32)).astype(jnp.bfloat16)
    extra = (
        jnp.zeros(squares.shape + (SQUARE_COLUMNS,), jnp.bfloat16)
        .at[:, :, 0]
        .set(square_high)
        .at[:, :, 1]
        .set(square_low)
    )
    payload = jnp.concatenate([partial_out.astype(jnp.bfloat16), resid_in, extra], axis=2)
    pieces = lax.all_to_all(
        payload.reshape(models, groups, row_count, payload.shape[2]),
        "tp",
        split_axis=1,
        concat_axis=1,
        tiled=True,
    ).astype(jnp.float32)
    update = jnp.sum(pieces[:, :, :, :full_width], axis=1)
    total_squares = jnp.sum(
        pieces[:, :, :, full_width + part_width] + pieces[:, :, :, full_width + part_width + 1],
        axis=1,
    )
    scale = lax.rsqrt(total_squares / inner_width + EPSILON)
    resid_rows = (
        pieces[:, :, :, full_width : full_width + part_width]
        .transpose(0, 2, 1, 3)
        .reshape(models, row_count, groups * part_width)
    )
    hidden = (resid_rows + update * scale[:, :, None]).astype(jnp.bfloat16)
    full_width = hidden.shape[2]
    hidden_float = hidden.astype(jnp.float32)
    final_squares = jnp.sum(hidden_float * hidden_float, axis=2)
    final_rows = (
        hidden_float
        * lax.rsqrt(final_squares / full_width + EPSILON)[:, :, None]
        * final_gain[:, None, :]
    ).astype(jnp.bfloat16)
    own_target = lax.dynamic_slice_in_dim(targets, lane_index * row_count, row_count, 0)
    high_digit = (own_target // DIGIT).astype(jnp.bfloat16)
    low_digit = (own_target % DIGIT).astype(jnp.bfloat16)
    target_row = jnp.zeros((1, full_width), jnp.bfloat16)
    target_row = target_row.at[0, :row_count].set(high_digit)
    target_row = target_row.at[0, row_count : 2 * row_count].set(low_digit)
    packet = jnp.concatenate([final_rows.reshape(models * row_count, full_width), target_row], axis=0)

    every = ring_gather(ring_gather(packet, along_x, ROWS_X), along_z, chips_z)
    peers = ROWS_X * chips_z
    every = every.reshape(peers, models * row_count + 1, full_width)
    every_rows = (
        every[:, : models * row_count]
        .reshape(peers, models, row_count, full_width)
        .transpose(1, 0, 2, 3)
        .reshape(models, peers * row_count, full_width)
    )
    every_target = (
        every[:, models * row_count, :row_count].astype(jnp.int32) * DIGIT
        + every[:, models * row_count, row_count : 2 * row_count].astype(jnp.int32)
    ).reshape(peers * row_count)
    own_logits, own_peak, own_picked = head_scores(
        head_weight, shard_index * vocab_part, every_rows, every_target
    )
    other_logits, other_peak, other_picked = head_scores(
        partner_weight, (shard_index ^ 1) * vocab_part, every_rows, every_target
    )
    peak_logit = jnp.maximum(own_peak, other_peak)
    spread = jnp.sum(jnp.exp(own_logits - peak_logit[:, :, None]), axis=2) + jnp.sum(
        jnp.exp(other_logits - peak_logit[:, :, None]), axis=2
    )
    statistics = jnp.stack([peak_logit, spread, own_picked + other_picked])
    statistics = statistics.reshape(3, models, chips_z, ROWS_X, row_count)
    statistics = jnp.roll(jnp.roll(statistics, z_index, axis=2), x_index, axis=3)
    neutral = jnp.stack(
        [
            jnp.full_like(statistics[0], -1e30),
            jnp.zeros_like(statistics[1]),
            jnp.zeros_like(statistics[2]),
        ]
    )
    send = jnp.stack(
        [jnp.where(core_index == c, statistics, neutral) for c in range(CORES)], axis=4
    ).reshape(3, models, shards, row_count)
    received = lax.all_to_all(send, "req", split_axis=2, concat_axis=2, tiled=True)
    peak_each, spread_each, picked_each = received[0], received[1], received[2]
    peak_logit = jnp.max(peak_each, axis=1)
    spread = jnp.sum(spread_each * jnp.exp(peak_each - peak_logit[:, None, :]), axis=1)
    picked = jnp.sum(picked_each, axis=1)
    scored_rows = lax.dynamic_slice_in_dim(score_flag, lane_index * row_count, row_count, 0).astype(
        jnp.float32
    )
    return (picked - (peak_logit + jnp.log(spread))) * scored_rows[None, :]


def solution(mesh):
    placed = (
        P(None, "req", "tp"),
        P(None, "req", "tp"),
        P(None, "req", None),
        P(None, "req", "tp"),
        P(None, "req", "tp"),
        P(None, None, "tp"),
        P(),
        P(None, "tp"),
        P(None, "tp"),
        P(None, "tp"),
        P(None, "tp"),
        P(),
        P(None, "tp", "req"),
        P(None, "req", None),
        P(None, "req", None, "tp"),
        P(None, "req", None, None),
        P(None, "req", "tp", None),
        P("req", None),
        P("req", None),
        P("req"),
        P("req"),
    )
    return jax.shard_map(
        local, mesh=mesh, in_specs=placed, out_specs=P(None, ("req", "tp")), check_vma=False
    )
```

```python
import jax
import jax.numpy as jnp
from jax import lax
from jax.sharding import PartitionSpec as P

EPSILON = 1e-05
PRECISE = lax.Precision.HIGH


def merged_2(part, axis, combine):
    gathered = jax.tree.map(lambda a: lax.all_gather(a, axis), part)

    def take(source):
        return jax.tree.map(lambda a: lax.dynamic_index_in_dim(a, source, 0, False), gathered)

    return lax.fori_loop(
        1, lax.axis_size(axis), lambda source, state: combine(state, take(source)), take(0)
    )


def request_layout(lengths, step_count):
    starts = jnp.cumsum(lengths) - lengths
    time_index = jnp.arange(step_count, dtype=jnp.int32)
    segment = jnp.sum((time_index[:, None] >= starts[None, 1:]).astype(jnp.int32), axis=1)
    member = segment[:, None] == jnp.arange(lengths.shape[0], dtype=jnp.int32)[None, :]
    first_step = jnp.sum(jnp.where(member, starts[None, :], 0), axis=1)
    return (starts, segment, member, time_index - first_step)


def causal_conv(stream, kernel, history, member, offset):
    tap_count = kernel.shape[0]
    history_len = tap_count - 1
    current = stream.astype(jnp.float32)
    member_bf = member.astype(jnp.bfloat16)
    slot_values = [
        jnp.dot(member_bf, history[:, slot_index, :], preferred_element_type=jnp.float32)
        for slot_index in range(history_len)
    ]
    output = kernel[history_len][None, :] * current
    for lag_steps in range(1, tap_count):
        shifted = jnp.concatenate(
            [jnp.zeros((lag_steps, current.shape[1]), current.dtype), current[:-lag_steps]], axis=0
        )
        earlier = jnp.zeros_like(current)
        for slot_index in range(history_len):
            earlier = earlier + jnp.where(
                (offset - lag_steps == slot_index - history_len)[:, None],
                slot_values[slot_index],
                0.0,
            )
        output = output + kernel[history_len - lag_steps][None, :] * jnp.where(
            (offset >= lag_steps)[:, None], shifted, earlier
        )
    return jax.nn.silu(output)


def mixer_block(
    gate_rows,
    mix_rows,
    keys_rows,
    step_raw,
    kernel_mix,
    kernel_keys,
    step_bias,
    decay_rate,
    skip_gain,
    history_mix,
    history_keys,
    start_state,
    lengths,
    continued,
):
    step_count = gate_rows.shape[0]
    head_count = step_raw.shape[1]
    inner_width = mix_rows.shape[1]
    head_size = inner_width // head_count
    states = start_state.shape[2]
    starts, segment, member, offset = request_layout(lengths, step_count)
    keep_state = continued.astype(jnp.bfloat16)
    mixed = causal_conv(
        mix_rows, kernel_mix, history_mix * keep_state[:, None, None], member, offset
    )
    projected = causal_conv(
        keys_rows, kernel_keys, history_keys * keep_state[:, None, None], member, offset
    )
    inject = projected[:, :states]
    readout = projected[:, states:]
    step_size = jax.nn.softplus(step_raw.astype(jnp.float32) + step_bias[None, :])
    log_decay = -step_size * decay_rate[None, :]
    running = jnp.cumsum(log_decay, axis=0)
    time_index = jnp.arange(step_count, dtype=jnp.int32)
    causal = (segment[:, None] == segment[None, :]) & (time_index[:, None] >= time_index[None, :])
    spread = jnp.minimum(running[:, None, :] - running[None, :, :], 0.0)
    transfer = jnp.where(causal[:, :, None], jnp.exp(spread), 0.0)
    intersection = jnp.dot(readout, inject.T, precision=PRECISE)
    kernel_full = transfer * intersection[:, :, None]
    values = mixed.reshape(step_count, head_count, head_size)
    output = jnp.einsum(
        "tsh,shp->thp", kernel_full, step_size[:, :, None] * values, precision=PRECISE
    )
    before = jnp.take(running - log_decay, starts, axis=0)
    member_float = member.astype(jnp.float32)
    entry_level = jnp.dot(member_float, before, precision=PRECISE)
    carried = jnp.exp(jnp.minimum(running - entry_level, 0.0))
    initial = start_state.astype(jnp.float32) * keep_state.astype(jnp.float32)[:, None, None]
    readings = jnp.einsum("tn,rcn->trc", readout, initial, precision=PRECISE)
    chosen = jnp.sum(member_float[:, :, None] * readings, axis=1).reshape(
        step_count, head_count, head_size
    )
    output = output + carried[:, :, None] * chosen + skip_gain[None, :, None] * values
    return output.reshape(step_count, inner_width) * jax.nn.silu(gate_rows.astype(jnp.float32))


def head_scores(head_weight, vocab_start, rows_hidden, rows_target):
    logits = jnp.einsum(
        "mnd,mvd->mnv", rows_hidden, head_weight, preferred_element_type=jnp.float32
    )
    peak_logit = jnp.max(logits, axis=2)
    local_id = rows_target - vocab_start
    matches = jnp.arange(head_weight.shape[1], dtype=jnp.int32)[None, :] == local_id[:, None]
    picked = jnp.sum(jnp.where(matches[None, :, :], logits, 0.0), axis=2)
    return logits, peak_logit, picked


def ring_gather(block, perm_of, count):
    got = {0: block}
    forward = block
    backward = block
    for step in range(1, count // 2 + 1):
        forward = lax.ppermute(forward, "req", perm_of(1))
        got[-step % count] = forward
        if step < count - step:
            backward = lax.ppermute(backward, "req", perm_of(-1))
            got[step] = backward
    return jnp.stack([got[k] for k in range(count)])


DIGIT = 256
SQUARE_COLUMNS = 128
CORES = 2
ROWS_X = 4


def local(
    gate_in,
    mix_in,
    keys_in,
    step_in,
    resid_in,
    kernel_mix,
    kernel_keys,
    step_bias,
    decay_rate,
    skip_gain,
    norm_gain,
    final_gain,
    out_weight,
    head_weight,
    history_mix,
    history_keys,
    start_state,
    lengths,
    continued,
    targets,
    score_flag,
):
    groups = lax.axis_size("tp")
    shards = lax.axis_size("req")
    lane_index = lax.axis_index("tp")
    shard_index = lax.axis_index("req")
    models = gate_in.shape[0]
    step_count = gate_in.shape[1]
    row_count = step_count // groups
    chips_z = shards // (ROWS_X * CORES)
    core_index = shard_index % CORES
    x_index = (shard_index // CORES) % ROWS_X
    z_index = shard_index // (CORES * ROWS_X)
    def along_z(shift):
        return [(i, (i + shift * CORES * ROWS_X) % shards) for i in range(shards)]

    def along_x(shift):
        return [
            (i, (i // (CORES * ROWS_X)) * CORES * ROWS_X
             + (((i // CORES) % ROWS_X + shift) % ROWS_X) * CORES + i % CORES)
            for i in range(shards)
        ]

    def along_core(shift):
        return [(i, i ^ 1) for i in range(shards)]

    vocab_part = head_weight.shape[1]
    partner_weight = lax.ppermute(
        head_weight, "req", [(i, i ^ 1) for i in range(shards)]
    )
    gated = jnp.stack(
        [
            mixer_block(
                gate_in[model_index],
                mix_in[model_index],
                keys_in[model_index],
                step_in[model_index],
                kernel_mix[model_index],
                kernel_keys[model_index],
                step_bias[model_index],
                decay_rate[model_index],
                skip_gain[model_index],
                history_mix[model_index],
                history_keys[model_index],
                start_state[model_index],
                lengths[0],
                continued[0],
            )
            for model_index in range(models)
        ]
    )
    inner_width = gated.shape[2] * groups
    squares = jnp.sum(gated * gated, axis=2)
    unscaled = (gated * norm_gain[:, None, :]).astype(jnp.bfloat16)
    ring_weight = ring_gather(
        ring_gather(ring_gather(out_weight, along_x, ROWS_X), along_z, chips_z),
        along_core,
        CORES,
    )
    ring_weight = jnp.roll(
        jnp.roll(jnp.roll(ring_weight.transpose(1, 2, 0, 3, 4, 5), z_index, axis=0), x_index, axis=1),
        core_index,
        axis=2,
    )
    full_weight = ring_weight.transpose(3, 4, 0, 1, 2, 5).reshape(
        models, out_weight.shape[1], shards * out_weight.shape[2]
    )
    partial_out = jnp.einsum(
        "mtc,mcd->mtd", unscaled, full_weight, preferred_element_type=jnp.float32
    )
    full_width = partial_out.shape[2]
    part_width = resid_in.shape[2]
    square_high = squares.astype(jnp.bfloat16)
    square_low = (squares - square_high.astype(jnp.float32)).astype(jnp.bfloat16)
    extra = (
        jnp.zeros(squares.shape + (SQUARE_COLUMNS,), jnp.bfloat16)
        .at[:, :, 0]
        .set(square_high)
        .at[:, :, 1]
        .set(square_low)
    )
    payload = jnp.concatenate([partial_out.astype(jnp.bfloat16), resid_in, extra], axis=2)
    pieces = lax.all_to_all(
        payload.reshape(models, groups, row_count, payload.shape[2]),
        "tp",
        split_axis=1,
        concat_axis=1,
        tiled=True,
    ).astype(jnp.float32)
    update = jnp.sum(pieces[:, :, :, :full_width], axis=1)
    total_squares = jnp.sum(
        pieces[:, :, :, full_width + part_width] + pieces[:, :, :, full_width + part_width + 1],
        axis=1,
    )
    scale = lax.rsqrt(total_squares / inner_width + EPSILON)
    resid_rows = (
        pieces[:, :, :, full_width : full_width + part_width]
        .transpose(0, 2, 1, 3)
        .reshape(models, row_count, groups * part_width)
    )
    hidden = (resid_rows + update * scale[:, :, None]).astype(jnp.bfloat16)
    full_width = hidden.shape[2]
    hidden_float = hidden.astype(jnp.float32)
    final_squares = jnp.sum(hidden_float * hidden_float, axis=2)
    final_rows = (
        hidden_float
        * lax.rsqrt(final_squares / full_width + EPSILON)[:, :, None]
        * final_gain[:, None, :]
    ).astype(jnp.bfloat16)
    own_target = lax.dynamic_slice_in_dim(targets, lane_index * row_count, row_count, 0)
    high_digit = (own_target // DIGIT).astype(jnp.bfloat16)
    low_digit = (own_target % DIGIT).astype(jnp.bfloat16)
    target_row = jnp.zeros((1, full_width), jnp.bfloat16)
    target_row = target_row.at[0, :row_count].set(high_digit)
    target_row = target_row.at[0, row_count : 2 * row_count].set(low_digit)
    packet = jnp.concatenate([final_rows.reshape(models * row_count, full_width), target_row], axis=0)

    every = ring_gather(ring_gather(packet, along_z, chips_z), along_x, ROWS_X)
    peers = ROWS_X * chips_z
    every = every.reshape(peers, models * row_count + 1, full_width)
    every_rows = (
        every[:, : models * row_count]
        .reshape(peers, models, row_count, full_width)
        .transpose(1, 0, 2, 3)
        .reshape(models, peers * row_count, full_width)
    )
    every_target = (
        every[:, models * row_count, :row_count].astype(jnp.int32) * DIGIT
        + every[:, models * row_count, row_count : 2 * row_count].astype(jnp.int32)
    ).reshape(peers * row_count)
    own_logits, own_peak, own_picked = head_scores(
        head_weight, shard_index * vocab_part, every_rows, every_target
    )
    other_logits, other_peak, other_picked = head_scores(
        partner_weight, (shard_index ^ 1) * vocab_part, every_rows, every_target
    )
    peak_logit = jnp.maximum(own_peak, other_peak)
    spread = jnp.sum(jnp.exp(own_logits - peak_logit[:, :, None]), axis=2) + jnp.sum(
        jnp.exp(other_logits - peak_logit[:, :, None]), axis=2
    )
    statistics = jnp.stack([peak_logit, spread, own_picked + other_picked])
    statistics = statistics.reshape(3, models, ROWS_X, chips_z, row_count).transpose(0, 1, 3, 2, 4)
    statistics = jnp.roll(jnp.roll(statistics, z_index, axis=2), x_index, axis=3)
    neutral = jnp.stack(
        [
            jnp.full_like(statistics[0], -1e30),
            jnp.zeros_like(statistics[1]),
            jnp.zeros_like(statistics[2]),
        ]
    )
    send = jnp.stack(
        [jnp.where(core_index == c, statistics, neutral) for c in range(CORES)], axis=4
    ).reshape(3, models, shards, row_count)
    received = lax.all_to_all(send, "req", split_axis=2, concat_axis=2, tiled=True)
    peak_each, spread_each, picked_each = received[0], received[1], received[2]
    peak_logit = jnp.max(peak_each, axis=1)
    spread = jnp.sum(spread_each * jnp.exp(peak_each - peak_logit[:, None, :]), axis=1)
    picked = jnp.sum(picked_each, axis=1)
    scored_rows = lax.dynamic_slice_in_dim(score_flag, lane_index * row_count, row_count, 0).astype(
        jnp.float32
    )
    return (picked - (peak_logit + jnp.log(spread))) * scored_rows[None, :]


def solution(mesh):
    placed = (
        P(None, "req", "tp"),
        P(None, "req", "tp"),
        P(None, "req", None),
        P(None, "req", "tp"),
        P(None, "req", "tp"),
        P(None, None, "tp"),
        P(),
        P(None, "tp"),
        P(None, "tp"),
        P(None, "tp"),
        P(None, "tp"),
        P(),
        P(None, "tp", "req"),
        P(None, "req", None),
        P(None, "req", None, "tp"),
        P(None, "req", None, None),
        P(None, "req", "tp", None),
        P("req", None),
        P("req", None),
        P("req"),
        P("req"),
    )
    return jax.shard_map(
        local, mesh=mesh, in_specs=placed, out_specs=P(None, ("req", "tp")), check_vma=False
    )
```

```python
import jax
import jax.numpy as jnp
from jax import lax
from jax.sharding import PartitionSpec as P

EPSILON = 1e-05
PRECISE = lax.Precision.HIGHEST


def merged_2(part, axis, combine):
    gathered = jax.tree.map(lambda a: lax.all_gather(a, axis), part)

    def take(source):
        return jax.tree.map(lambda a: lax.dynamic_index_in_dim(a, source, 0, False), gathered)

    return lax.fori_loop(
        1, lax.axis_size(axis), lambda source, state: combine(state, take(source)), take(0)
    )


def request_layout(lengths, step_count):
    starts = jnp.cumsum(lengths) - lengths
    time_index = jnp.arange(step_count, dtype=jnp.int32)
    segment = jnp.sum((time_index[:, None] >= starts[None, 1:]).astype(jnp.int32), axis=1)
    member = segment[:, None] == jnp.arange(lengths.shape[0], dtype=jnp.int32)[None, :]
    first_step = jnp.sum(jnp.where(member, starts[None, :], 0), axis=1)
    return (starts, segment, member, time_index - first_step)


def causal_conv(stream, kernel, history, member, offset):
    tap_count = kernel.shape[0]
    history_len = tap_count - 1
    current = stream.astype(jnp.float32)
    member_bf = member.astype(jnp.bfloat16)
    slot_values = [
        jnp.dot(member_bf, history[:, slot_index, :], preferred_element_type=jnp.float32)
        for slot_index in range(history_len)
    ]
    output = kernel[history_len][None, :] * current
    for lag_steps in range(1, tap_count):
        shifted = jnp.concatenate(
            [jnp.zeros((lag_steps, current.shape[1]), current.dtype), current[:-lag_steps]], axis=0
        )
        earlier = jnp.zeros_like(current)
        for slot_index in range(history_len):
            earlier = earlier + jnp.where(
                (offset - lag_steps == slot_index - history_len)[:, None],
                slot_values[slot_index],
                0.0,
            )
        output = output + kernel[history_len - lag_steps][None, :] * jnp.where(
            (offset >= lag_steps)[:, None], shifted, earlier
        )
    return jax.nn.silu(output)


def mixer_block(
    gate_rows,
    mix_rows,
    keys_rows,
    step_raw,
    kernel_mix,
    kernel_keys,
    step_bias,
    decay_rate,
    skip_gain,
    history_mix,
    history_keys,
    start_state,
    lengths,
    continued,
):
    step_count = gate_rows.shape[0]
    head_count = step_raw.shape[1]
    inner_width = mix_rows.shape[1]
    head_size = inner_width // head_count
    states = start_state.shape[2]
    starts, segment, member, offset = request_layout(lengths, step_count)
    keep_state = continued.astype(jnp.bfloat16)
    mixed = causal_conv(
        mix_rows, kernel_mix, history_mix * keep_state[:, None, None], member, offset
    )
    projected = causal_conv(
        keys_rows, kernel_keys, history_keys * keep_state[:, None, None], member, offset
    )
    inject = projected[:, :states]
    readout = projected[:, states:]
    step_size = jax.nn.softplus(step_raw.astype(jnp.float32) + step_bias[None, :])
    log_decay = -step_size * decay_rate[None, :]
    running = jnp.cumsum(log_decay, axis=0)
    time_index = jnp.arange(step_count, dtype=jnp.int32)
    causal = (segment[:, None] == segment[None, :]) & (time_index[:, None] >= time_index[None, :])
    spread = jnp.minimum(running[:, None, :] - running[None, :, :], 0.0)
    transfer = jnp.where(causal[:, :, None], jnp.exp(spread), 0.0)
    intersection = jnp.dot(readout, inject.T, precision=PRECISE)
    kernel_full = transfer * intersection[:, :, None]
    values = mixed.reshape(step_count, head_count, head_size)
    output = jnp.einsum(
        "tsh,shp->thp", kernel_full, step_size[:, :, None] * values, precision=PRECISE
    )
    before = jnp.take(running - log_decay, starts, axis=0)
    member_float = member.astype(jnp.float32)
    entry_level = jnp.dot(member_float, before, precision=PRECISE)
    carried = jnp.exp(jnp.minimum(running - entry_level, 0.0))
    initial = start_state.astype(jnp.float32) * keep_state.astype(jnp.float32)[:, None, None]
    readings = jnp.einsum("tn,rcn->trc", readout, initial, precision=PRECISE)
    chosen = jnp.sum(member_float[:, :, None] * readings, axis=1).reshape(
        step_count, head_count, head_size
    )
    output = output + carried[:, :, None] * chosen + skip_gain[None, :, None] * values
    return output.reshape(step_count, inner_width) * jax.nn.silu(gate_rows.astype(jnp.float32))


def head_scores(head_weight, vocab_start, rows_hidden, rows_target):
    logits = jnp.einsum(
        "mnd,mvd->mnv", rows_hidden, head_weight, preferred_element_type=jnp.float32
    )
    peak_logit = jnp.max(logits, axis=2)
    local_id = rows_target - vocab_start
    matches = jnp.arange(head_weight.shape[1], dtype=jnp.int32)[None, :] == local_id[:, None]
    picked = jnp.sum(jnp.where(matches[None, :, :], logits, 0.0), axis=2)
    return logits, peak_logit, picked


def ring_gather(block, perm_of, count):
    got = {0: block}
    forward = block
    backward = block
    for step in range(1, count // 2 + 1):
        forward = lax.ppermute(forward, "req", perm_of(1))
        got[-step % count] = forward
        if step < count - step:
            backward = lax.ppermute(backward, "req", perm_of(-1))
            got[step] = backward
    return jnp.stack([got[k] for k in range(count)])


DIGIT = 256
SQUARE_COLUMNS = 128
CORES = 2
ROWS_X = 4


def local(
    gate_in,
    mix_in,
    keys_in,
    step_in,
    resid_in,
    kernel_mix,
    kernel_keys,
    step_bias,
    decay_rate,
    skip_gain,
    norm_gain,
    final_gain,
    out_weight,
    head_weight,
    history_mix,
    history_keys,
    start_state,
    lengths,
    continued,
    targets,
    score_flag,
):
    groups = lax.axis_size("tp")
    shards = lax.axis_size("req")
    lane_index = lax.axis_index("tp")
    shard_index = lax.axis_index("req")
    models = gate_in.shape[0]
    step_count = gate_in.shape[1]
    row_count = step_count // groups
    chips_z = shards // (ROWS_X * CORES)
    core_index = shard_index % CORES
    x_index = (shard_index // CORES) % ROWS_X
    z_index = shard_index // (CORES * ROWS_X)
    def along_z(shift):
        return [(i, (i + shift * CORES * ROWS_X) % shards) for i in range(shards)]

    def along_x(shift):
        return [
            (i, (i // (CORES * ROWS_X)) * CORES * ROWS_X
             + (((i // CORES) % ROWS_X + shift) % ROWS_X) * CORES + i % CORES)
            for i in range(shards)
        ]

    def along_core(shift):
        return [(i, i ^ 1) for i in range(shards)]

    vocab_part = head_weight.shape[1]
    partner_weight = lax.ppermute(
        head_weight, "req", [(i, i ^ 1) for i in range(shards)]
    )
    gated = jnp.stack(
        [
            mixer_block(
                gate_in[model_index],
                mix_in[model_index],
                keys_in[model_index],
                step_in[model_index],
                kernel_mix[model_index],
                kernel_keys[model_index],
                step_bias[model_index],
                decay_rate[model_index],
                skip_gain[model_index],
                history_mix[model_index],
                history_keys[model_index],
                start_state[model_index],
                lengths[0],
                continued[0],
            )
            for model_index in range(models)
        ]
    )
    inner_width = gated.shape[2] * groups
    squares = jnp.sum(gated * gated, axis=2)
    unscaled = (gated * norm_gain[:, None, :]).astype(jnp.bfloat16)
    ring_weight = ring_gather(
        ring_gather(ring_gather(out_weight, along_x, ROWS_X), along_core, CORES),
        along_z,
        chips_z,
    )
    ring_weight = jnp.roll(
        jnp.roll(jnp.roll(ring_weight.transpose(0, 2, 1, 3, 4, 5), z_index, axis=0), x_index, axis=1),
        core_index,
        axis=2,
    )
    full_weight = ring_weight.transpose(3, 4, 0, 1, 2, 5).reshape(
        models, out_weight.shape[1], shards * out_weight.shape[2]
    )
    partial_out = jnp.einsum(
        "mtc,mcd->mtd", unscaled, full_weight, preferred_element_type=jnp.float32
    )
    full_width = partial_out.shape[2]
    part_width = resid_in.shape[2]
    square_high = squares.astype(jnp.bfloat16)
    square_low = (squares - square_high.astype(jnp.float32)).astype(jnp.bfloat16)
    extra = (
        jnp.zeros(squares.shape + (SQUARE_COLUMNS,), jnp.bfloat16)
        .at[:, :, 0]
        .set(square_high)
        .at[:, :, 1]
        .set(square_low)
    )
    payload = jnp.concatenate([partial_out.astype(jnp.bfloat16), resid_in, extra], axis=2)
    pieces = lax.all_to_all(
        payload.reshape(models, groups, row_count, payload.shape[2]),
        "tp",
        split_axis=1,
        concat_axis=1,
        tiled=True,
    ).astype(jnp.float32)
    update = jnp.sum(pieces[:, :, :, :full_width], axis=1)
    total_squares = jnp.sum(
        pieces[:, :, :, full_width + part_width] + pieces[:, :, :, full_width + part_width + 1],
        axis=1,
    )
    scale = lax.rsqrt(total_squares / inner_width + EPSILON)
    resid_rows = (
        pieces[:, :, :, full_width : full_width + part_width]
        .transpose(0, 2, 1, 3)
        .reshape(models, row_count, groups * part_width)
    )
    hidden = (resid_rows + update * scale[:, :, None]).astype(jnp.bfloat16)
    full_width = hidden.shape[2]
    hidden_float = hidden.astype(jnp.float32)
    final_squares = jnp.sum(hidden_float * hidden_float, axis=2)
    final_rows = (
        hidden_float
        * lax.rsqrt(final_squares / full_width + EPSILON)[:, :, None]
        * final_gain[:, None, :]
    ).astype(jnp.bfloat16)
    own_target = lax.dynamic_slice_in_dim(targets, lane_index * row_count, row_count, 0)
    high_digit = (own_target // DIGIT).astype(jnp.bfloat16)
    low_digit = (own_target % DIGIT).astype(jnp.bfloat16)
    target_row = jnp.zeros((1, full_width), jnp.bfloat16)
    target_row = target_row.at[0, :row_count].set(high_digit)
    target_row = target_row.at[0, row_count : 2 * row_count].set(low_digit)
    packet = jnp.concatenate([final_rows.reshape(models * row_count, full_width), target_row], axis=0)

    every = ring_gather(ring_gather(packet, along_z, chips_z), along_x, ROWS_X)
    peers = ROWS_X * chips_z
    every = every.reshape(peers, models * row_count + 1, full_width)
    every_rows = (
        every[:, : models * row_count]
        .reshape(peers, models, row_count, full_width)
        .transpose(1, 0, 2, 3)
        .reshape(models, peers * row_count, full_width)
    )
    every_target = (
        every[:, models * row_count, :row_count].astype(jnp.int32) * DIGIT
        + every[:, models * row_count, row_count : 2 * row_count].astype(jnp.int32)
    ).reshape(peers * row_count)
    own_logits, own_peak, own_picked = head_scores(
        head_weight, shard_index * vocab_part, every_rows, every_target
    )
    other_logits, other_peak, other_picked = head_scores(
        partner_weight, (shard_index ^ 1) * vocab_part, every_rows, every_target
    )
    peak_logit = jnp.maximum(own_peak, other_peak)
    spread = jnp.sum(jnp.exp(own_logits - peak_logit[:, :, None]), axis=2) + jnp.sum(
        jnp.exp(other_logits - peak_logit[:, :, None]), axis=2
    )
    statistics = jnp.stack([peak_logit, spread, own_picked + other_picked])
    statistics = statistics.reshape(3, models, ROWS_X, chips_z, row_count).transpose(0, 1, 3, 2, 4)
    statistics = jnp.roll(jnp.roll(statistics, z_index, axis=2), x_index, axis=3)
    neutral = jnp.stack(
        [
            jnp.full_like(statistics[0], -1e30),
            jnp.zeros_like(statistics[1]),
            jnp.zeros_like(statistics[2]),
        ]
    )
    send = jnp.stack(
        [jnp.where(core_index == c, statistics, neutral) for c in range(CORES)], axis=4
    ).reshape(3, models, shards, row_count)
    received = lax.all_to_all(send, "req", split_axis=2, concat_axis=2, tiled=True)
    peak_each, spread_each, picked_each = received[0], received[1], received[2]
    peak_logit = jnp.max(peak_each, axis=1)
    spread = jnp.sum(spread_each * jnp.exp(peak_each - peak_logit[:, None, :]), axis=1)
    picked = jnp.sum(picked_each, axis=1)
    scored_rows = lax.dynamic_slice_in_dim(score_flag, lane_index * row_count, row_count, 0).astype(
        jnp.float32
    )
    return (picked - (peak_logit + jnp.log(spread))) * scored_rows[None, :]


def solution(mesh):
    placed = (
        P(None, "req", "tp"),
        P(None, "req", "tp"),
        P(None, "req", None),
        P(None, "req", "tp"),
        P(None, "req", "tp"),
        P(None, None, "tp"),
        P(),
        P(None, "tp"),
        P(None, "tp"),
        P(None, "tp"),
        P(None, "tp"),
        P(),
        P(None, "tp", "req"),
        P(None, "req", None),
        P(None, "req", None, "tp"),
        P(None, "req", None, None),
        P(None, "req", "tp", None),
        P("req", None),
        P("req", None),
        P("req"),
        P("req"),
    )
    return jax.shard_map(
        local, mesh=mesh, in_specs=placed, out_specs=P(None, ("req", "tp")), check_vma=False
    )
```

```python
import jax
import jax.numpy as jnp
from jax import lax
from jax.sharding import PartitionSpec as P

EPSILON = 1e-05
PRECISE = lax.Precision.HIGHEST


def merged_2(part, axis, combine):
    gathered = jax.tree.map(lambda a: lax.all_gather(a, axis), part)

    def take(source):
        return jax.tree.map(lambda a: lax.dynamic_index_in_dim(a, source, 0, False), gathered)

    return lax.fori_loop(
        1, lax.axis_size(axis), lambda source, state: combine(state, take(source)), take(0)
    )


def request_layout(lengths, step_count):
    starts = jnp.cumsum(lengths) - lengths
    time_index = jnp.arange(step_count, dtype=jnp.int32)
    segment = jnp.sum((time_index[:, None] >= starts[None, 1:]).astype(jnp.int32), axis=1)
    member = segment[:, None] == jnp.arange(lengths.shape[0], dtype=jnp.int32)[None, :]
    first_step = jnp.sum(jnp.where(member, starts[None, :], 0), axis=1)
    return (starts, segment, member, time_index - first_step)


def causal_conv(stream, kernel, history, member, offset):
    tap_count = kernel.shape[0]
    history_len = tap_count - 1
    current = stream.astype(jnp.float32)
    member_bf = member.astype(jnp.bfloat16)
    slot_values = [
        jnp.dot(member_bf, history[:, slot_index, :], preferred_element_type=jnp.float32)
        for slot_index in range(history_len)
    ]
    output = kernel[history_len][None, :] * current
    for lag_steps in range(1, tap_count):
        shifted = jnp.concatenate(
            [jnp.zeros((lag_steps, current.shape[1]), current.dtype), current[:-lag_steps]], axis=0
        )
        earlier = jnp.zeros_like(current)
        for slot_index in range(history_len):
            earlier = earlier + jnp.where(
                (offset - lag_steps == slot_index - history_len)[:, None],
                slot_values[slot_index],
                0.0,
            )
        output = output + kernel[history_len - lag_steps][None, :] * jnp.where(
            (offset >= lag_steps)[:, None], shifted, earlier
        )
    return jax.nn.silu(output)


def mixer_block(
    gate_rows,
    mix_rows,
    keys_rows,
    step_raw,
    kernel_mix,
    kernel_keys,
    step_bias,
    decay_rate,
    skip_gain,
    history_mix,
    history_keys,
    start_state,
    lengths,
    continued,
):
    step_count = gate_rows.shape[0]
    head_count = step_raw.shape[1]
    inner_width = mix_rows.shape[1]
    head_size = inner_width // head_count
    states = start_state.shape[2]
    starts, segment, member, offset = request_layout(lengths, step_count)
    keep_state = continued.astype(jnp.bfloat16)
    mixed = causal_conv(
        mix_rows, kernel_mix, history_mix * keep_state[:, None, None], member, offset
    )
    projected = causal_conv(
        keys_rows, kernel_keys, history_keys * keep_state[:, None, None], member, offset
    )
    inject = projected[:, :states]
    readout = projected[:, states:]
    step_size = jax.nn.softplus(step_raw.astype(jnp.float32) + step_bias[None, :])
    log_decay = -step_size * decay_rate[None, :]
    running = jnp.cumsum(log_decay, axis=0)
    time_index = jnp.arange(step_count, dtype=jnp.int32)
    causal = (segment[:, None] == segment[None, :]) & (time_index[:, None] >= time_index[None, :])
    spread = jnp.minimum(running[:, None, :] - running[None, :, :], 0.0)
    transfer = jnp.where(causal[:, :, None], jnp.exp(spread), 0.0)
    intersection = jnp.dot(readout, inject.T, precision=PRECISE)
    kernel_full = transfer * intersection[:, :, None]
    values = mixed.reshape(step_count, head_count, head_size)
    output = jnp.einsum(
        "tsh,shp->thp", kernel_full, step_size[:, :, None] * values, precision=PRECISE
    )
    before = jnp.take(running - log_decay, starts, axis=0)
    member_float = member.astype(jnp.float32)
    entry_level = jnp.dot(member_float, before, precision=PRECISE)
    carried = jnp.exp(jnp.minimum(running - entry_level, 0.0))
    initial = start_state.astype(jnp.float32) * keep_state.astype(jnp.float32)[:, None, None]
    readings = jnp.einsum("tn,rcn->trc", readout, initial, precision=PRECISE)
    chosen = jnp.sum(member_float[:, :, None] * readings, axis=1).reshape(
        step_count, head_count, head_size
    )
    output = output + carried[:, :, None] * chosen + skip_gain[None, :, None] * values
    return output.reshape(step_count, inner_width) * jax.nn.silu(gate_rows.astype(jnp.float32))


def head_scores(head_weight, vocab_start, rows_hidden, rows_target):
    logits = jnp.einsum(
        "mnd,mvd->mnv", rows_hidden, head_weight, preferred_element_type=jnp.float32
    )
    peak_logit = jnp.max(logits, axis=2)
    local_id = rows_target - vocab_start
    matches = jnp.arange(head_weight.shape[1], dtype=jnp.int32)[None, :] == local_id[:, None]
    picked = jnp.sum(jnp.where(matches[None, :, :], logits, 0.0), axis=2)
    return logits, peak_logit, picked


def ring_gather(block, perm_of, count):
    got = {0: block}
    forward = block
    backward = block
    for step in range(1, count // 2 + 1):
        forward = lax.ppermute(forward, "req", perm_of(1))
        got[-step % count] = forward
        if step < count - step:
            backward = lax.ppermute(backward, "req", perm_of(-1))
            got[step] = backward
    return jnp.stack([got[k] for k in range(count)])


DIGIT = 256
SQUARE_COLUMNS = 128
CORES = 2
ROWS_X = 4


def local(
    gate_in,
    mix_in,
    keys_in,
    step_in,
    resid_in,
    kernel_mix,
    kernel_keys,
    step_bias,
    decay_rate,
    skip_gain,
    norm_gain,
    final_gain,
    out_weight,
    head_weight,
    history_mix,
    history_keys,
    start_state,
    lengths,
    continued,
    targets,
    score_flag,
):
    groups = lax.axis_size("tp")
    shards = lax.axis_size("req")
    lane_index = lax.axis_index("tp")
    shard_index = lax.axis_index("req")
    models = gate_in.shape[0]
    step_count = gate_in.shape[1]
    row_count = step_count // groups
    chips_z = shards // (ROWS_X * CORES)
    core_index = shard_index % CORES
    x_index = (shard_index // CORES) % ROWS_X
    z_index = shard_index // (CORES * ROWS_X)
    def along_z(shift):
        return [(i, (i + shift * CORES * ROWS_X) % shards) for i in range(shards)]

    def along_x(shift):
        return [
            (i, (i // (CORES * ROWS_X)) * CORES * ROWS_X
             + (((i // CORES) % ROWS_X + shift) % ROWS_X) * CORES + i % CORES)
            for i in range(shards)
        ]

    def along_core(shift):
        return [(i, i ^ 1) for i in range(shards)]

    vocab_part = head_weight.shape[1]
    gated = jnp.stack(
        [
            mixer_block(
                gate_in[model_index],
                mix_in[model_index],
                keys_in[model_index],
                step_in[model_index],
                kernel_mix[model_index],
                kernel_keys[model_index],
                step_bias[model_index],
                decay_rate[model_index],
                skip_gain[model_index],
                history_mix[model_index],
                history_keys[model_index],
                start_state[model_index],
                lengths[0],
                continued[0],
            )
            for model_index in range(models)
        ]
    )
    inner_width = gated.shape[2] * groups
    squares = jnp.sum(gated * gated, axis=2)
    unscaled = (gated * norm_gain[:, None, :]).astype(jnp.bfloat16)
    ring_weight = ring_gather(
        ring_gather(ring_gather(out_weight, along_x, ROWS_X), along_z, chips_z),
        along_core,
        CORES,
    )
    ring_weight = jnp.roll(
        jnp.roll(jnp.roll(ring_weight.transpose(1, 2, 0, 3, 4, 5), z_index, axis=0), x_index, axis=1),
        core_index,
        axis=2,
    )
    full_weight = ring_weight.transpose(3, 4, 0, 1, 2, 5).reshape(
        models, out_weight.shape[1], shards * out_weight.shape[2]
    )
    partial_out = jnp.einsum(
        "mtc,mcd->mtd", unscaled, full_weight, preferred_element_type=jnp.float32
    )
    full_width = partial_out.shape[2]
    part_width = resid_in.shape[2]
    square_high = squares.astype(jnp.bfloat16)
    square_low = (squares - square_high.astype(jnp.float32)).astype(jnp.bfloat16)
    extra = (
        jnp.zeros(squares.shape + (SQUARE_COLUMNS,), jnp.bfloat16)
        .at[:, :, 0]
        .set(square_high)
        .at[:, :, 1]
        .set(square_low)
    )
    payload = jnp.concatenate([partial_out.astype(jnp.bfloat16), resid_in, extra], axis=2)
    pieces = lax.all_to_all(
        payload.reshape(models, groups, row_count, payload.shape[2]),
        "tp",
        split_axis=1,
        concat_axis=1,
        tiled=True,
    ).astype(jnp.float32)
    update = jnp.sum(pieces[:, :, :, :full_width], axis=1)
    total_squares = jnp.sum(
        pieces[:, :, :, full_width + part_width] + pieces[:, :, :, full_width + part_width + 1],
        axis=1,
    )
    scale = lax.rsqrt(total_squares / inner_width + EPSILON)
    resid_rows = (
        pieces[:, :, :, full_width : full_width + part_width]
        .transpose(0, 2, 1, 3)
        .reshape(models, row_count, groups * part_width)
    )
    hidden = (resid_rows + update * scale[:, :, None]).astype(jnp.bfloat16)
    full_width = hidden.shape[2]
    hidden_float = hidden.astype(jnp.float32)
    final_squares = jnp.sum(hidden_float * hidden_float, axis=2)
    final_rows = (
        hidden_float
        * lax.rsqrt(final_squares / full_width + EPSILON)[:, :, None]
        * final_gain[:, None, :]
    ).astype(jnp.bfloat16)
    own_target = lax.dynamic_slice_in_dim(targets, lane_index * row_count, row_count, 0)
    high_digit = (own_target // DIGIT).astype(jnp.bfloat16)
    low_digit = (own_target % DIGIT).astype(jnp.bfloat16)
    target_row = jnp.zeros((1, full_width), jnp.bfloat16)
    target_row = target_row.at[0, :row_count].set(high_digit)
    target_row = target_row.at[0, row_count : 2 * row_count].set(low_digit)
    packet = jnp.concatenate([final_rows.reshape(models * row_count, full_width), target_row], axis=0)

    every = ring_gather(ring_gather(packet, along_z, chips_z), along_x, ROWS_X)
    late_weight, _ = lax.optimization_barrier((head_weight, packet))
    partner_weight = lax.ppermute(
        late_weight, "req", [(i, i ^ 1) for i in range(shards)]
    )
    peers = ROWS_X * chips_z
    every = every.reshape(peers, models * row_count + 1, full_width)
    every_rows = (
        every[:, : models * row_count]
        .reshape(peers, models, row_count, full_width)
        .transpose(1, 0, 2, 3)
        .reshape(models, peers * row_count, full_width)
    )
    every_target = (
        every[:, models * row_count, :row_count].astype(jnp.int32) * DIGIT
        + every[:, models * row_count, row_count : 2 * row_count].astype(jnp.int32)
    ).reshape(peers * row_count)
    own_logits, own_peak, own_picked = head_scores(
        head_weight, shard_index * vocab_part, every_rows, every_target
    )
    other_logits, other_peak, other_picked = head_scores(
        partner_weight, (shard_index ^ 1) * vocab_part, every_rows, every_target
    )
    peak_logit = jnp.maximum(own_peak, other_peak)
    spread = jnp.sum(jnp.exp(own_logits - peak_logit[:, :, None]), axis=2) + jnp.sum(
        jnp.exp(other_logits - peak_logit[:, :, None]), axis=2
    )
    statistics = jnp.stack([peak_logit, spread, own_picked + other_picked])
    statistics = statistics.reshape(3, models, ROWS_X, chips_z, row_count).transpose(0, 1, 3, 2, 4)
    statistics = jnp.roll(jnp.roll(statistics, z_index, axis=2), x_index, axis=3)
    neutral = jnp.stack(
        [
            jnp.full_like(statistics[0], -1e30),
            jnp.zeros_like(statistics[1]),
            jnp.zeros_like(statistics[2]),
        ]
    )
    send = jnp.stack(
        [jnp.where(core_index == c, statistics, neutral) for c in range(CORES)], axis=4
    ).reshape(3, models, shards, row_count)
    received = lax.all_to_all(send, "req", split_axis=2, concat_axis=2, tiled=True)
    peak_each, spread_each, picked_each = received[0], received[1], received[2]
    peak_logit = jnp.max(peak_each, axis=1)
    spread = jnp.sum(spread_each * jnp.exp(peak_each - peak_logit[:, None, :]), axis=1)
    picked = jnp.sum(picked_each, axis=1)
    scored_rows = lax.dynamic_slice_in_dim(score_flag, lane_index * row_count, row_count, 0).astype(
        jnp.float32
    )
    return (picked - (peak_logit + jnp.log(spread))) * scored_rows[None, :]


def solution(mesh):
    placed = (
        P(None, "req", "tp"),
        P(None, "req", "tp"),
        P(None, "req", None),
        P(None, "req", "tp"),
        P(None, "req", "tp"),
        P(None, None, "tp"),
        P(),
        P(None, "tp"),
        P(None, "tp"),
        P(None, "tp"),
        P(None, "tp"),
        P(),
        P(None, "tp", "req"),
        P(None, "req", None),
        P(None, "req", None, "tp"),
        P(None, "req", None, None),
        P(None, "req", "tp", None),
        P("req", None),
        P("req", None),
        P("req"),
        P("req"),
    )
    return jax.shard_map(
        local, mesh=mesh, in_specs=placed, out_specs=P(None, ("req", "tp")), check_vma=False
    )
```

```python
import jax
import jax.numpy as jnp
from jax import lax
from jax.sharding import PartitionSpec as P

EPSILON = 1e-05
PRECISE = lax.Precision.HIGHEST


def merged_2(part, axis, combine):
    gathered = jax.tree.map(lambda a: lax.all_gather(a, axis), part)

    def take(source):
        return jax.tree.map(lambda a: lax.dynamic_index_in_dim(a, source, 0, False), gathered)

    return lax.fori_loop(
        1, lax.axis_size(axis), lambda source, state: combine(state, take(source)), take(0)
    )


def request_layout(lengths, step_count):
    starts = jnp.cumsum(lengths) - lengths
    time_index = jnp.arange(step_count, dtype=jnp.int32)
    segment = jnp.sum((time_index[:, None] >= starts[None, 1:]).astype(jnp.int32), axis=1)
    member = segment[:, None] == jnp.arange(lengths.shape[0], dtype=jnp.int32)[None, :]
    first_step = jnp.sum(jnp.where(member, starts[None, :], 0), axis=1)
    return (starts, segment, member, time_index - first_step)


def causal_conv(stream, kernel, history, member, offset):
    tap_count = kernel.shape[0]
    history_len = tap_count - 1
    current = stream.astype(jnp.float32)
    member_bf = member.astype(jnp.bfloat16)
    slot_values = [
        jnp.dot(member_bf, history[:, slot_index, :], preferred_element_type=jnp.float32)
        for slot_index in range(history_len)
    ]
    output = kernel[history_len][None, :] * current
    for lag_steps in range(1, tap_count):
        shifted = jnp.concatenate(
            [jnp.zeros((lag_steps, current.shape[1]), current.dtype), current[:-lag_steps]], axis=0
        )
        earlier = jnp.zeros_like(current)
        for slot_index in range(history_len):
            earlier = earlier + jnp.where(
                (offset - lag_steps == slot_index - history_len)[:, None],
                slot_values[slot_index],
                0.0,
            )
        output = output + kernel[history_len - lag_steps][None, :] * jnp.where(
            (offset >= lag_steps)[:, None], shifted, earlier
        )
    return jax.nn.silu(output)


def mixer_block(
    gate_rows,
    mix_rows,
    keys_rows,
    step_raw,
    kernel_mix,
    kernel_keys,
    step_bias,
    decay_rate,
    skip_gain,
    history_mix,
    history_keys,
    start_state,
    lengths,
    continued,
):
    step_count = gate_rows.shape[0]
    head_count = step_raw.shape[1]
    inner_width = mix_rows.shape[1]
    head_size = inner_width // head_count
    states = start_state.shape[2]
    starts, segment, member, offset = request_layout(lengths, step_count)
    keep_state = continued.astype(jnp.bfloat16)
    mixed = causal_conv(
        mix_rows, kernel_mix, history_mix * keep_state[:, None, None], member, offset
    )
    projected = causal_conv(
        keys_rows, kernel_keys, history_keys * keep_state[:, None, None], member, offset
    )
    inject = projected[:, :states]
    readout = projected[:, states:]
    step_size = jax.nn.softplus(step_raw.astype(jnp.float32) + step_bias[None, :])
    log_decay = -step_size * decay_rate[None, :]
    running = jnp.cumsum(log_decay, axis=0)
    time_index = jnp.arange(step_count, dtype=jnp.int32)
    causal = (segment[:, None] == segment[None, :]) & (time_index[:, None] >= time_index[None, :])
    spread = jnp.minimum(running[:, None, :] - running[None, :, :], 0.0)
    transfer = jnp.where(causal[:, :, None], jnp.exp(spread), 0.0)
    intersection = jnp.dot(readout, inject.T, precision=PRECISE)
    kernel_full = transfer * intersection[:, :, None]
    values = mixed.reshape(step_count, head_count, head_size)
    output = jnp.einsum(
        "tsh,shp->thp", kernel_full, step_size[:, :, None] * values, precision=PRECISE
    )
    before = jnp.take(running - log_decay, starts, axis=0)
    member_float = member.astype(jnp.float32)
    entry_level = jnp.dot(member_float, before, precision=PRECISE)
    carried = jnp.exp(jnp.minimum(running - entry_level, 0.0))
    initial = start_state.astype(jnp.float32) * keep_state.astype(jnp.float32)[:, None, None]
    readings = jnp.einsum("tn,rcn->trc", readout, initial, precision=PRECISE)
    chosen = jnp.sum(member_float[:, :, None] * readings, axis=1).reshape(
        step_count, head_count, head_size
    )
    output = output + carried[:, :, None] * chosen + skip_gain[None, :, None] * values
    return output.reshape(step_count, inner_width) * jax.nn.silu(gate_rows.astype(jnp.float32))


def head_scores(head_weight, vocab_start, rows_hidden, rows_target):
    logits = jnp.einsum(
        "mnd,mvd->mnv", rows_hidden, head_weight, preferred_element_type=jnp.float32
    )
    peak_logit = jnp.max(logits, axis=2)
    local_id = rows_target - vocab_start
    matches = jnp.arange(head_weight.shape[1], dtype=jnp.int32)[None, :] == local_id[:, None]
    picked = jnp.sum(jnp.where(matches[None, :, :], logits, 0.0), axis=2)
    return logits, peak_logit, picked


def ring_gather(block, perm_of, count):
    got = {0: block}
    forward = block
    backward = block
    for step in range(1, count // 2 + 1):
        forward = lax.ppermute(forward, "req", perm_of(1))
        got[-step % count] = forward
        if step < count - step:
            backward = lax.ppermute(backward, "req", perm_of(-1))
            got[step] = backward
    return jnp.stack([got[k] for k in range(count)])


DIGIT = 256
SQUARE_COLUMNS = 128
CORES = 2
ROWS_X = 4


def local(
    gate_in,
    mix_in,
    keys_in,
    step_in,
    resid_in,
    kernel_mix,
    kernel_keys,
    step_bias,
    decay_rate,
    skip_gain,
    norm_gain,
    final_gain,
    out_weight,
    head_weight,
    history_mix,
    history_keys,
    start_state,
    lengths,
    continued,
    targets,
    score_flag,
):
    groups = lax.axis_size("tp")
    shards = lax.axis_size("req")
    lane_index = lax.axis_index("tp")
    shard_index = lax.axis_index("req")
    models = gate_in.shape[0]
    step_count = gate_in.shape[1]
    row_count = step_count // groups
    chips_z = shards // (ROWS_X * CORES)
    core_index = shard_index % CORES
    x_index = (shard_index // CORES) % ROWS_X
    z_index = shard_index // (CORES * ROWS_X)
    def along_z(shift):
        return [(i, (i + shift * CORES * ROWS_X) % shards) for i in range(shards)]

    def along_x(shift):
        return [
            (i, (i // (CORES * ROWS_X)) * CORES * ROWS_X
             + (((i // CORES) % ROWS_X + shift) % ROWS_X) * CORES + i % CORES)
            for i in range(shards)
        ]

    def along_core(shift):
        return [(i, i ^ 1) for i in range(shards)]

    vocab_part = head_weight.shape[1]
    gated = jnp.stack(
        [
            mixer_block(
                gate_in[model_index],
                mix_in[model_index],
                keys_in[model_index],
                step_in[model_index],
                kernel_mix[model_index],
                kernel_keys[model_index],
                step_bias[model_index],
                decay_rate[model_index],
                skip_gain[model_index],
                history_mix[model_index],
                history_keys[model_index],
                start_state[model_index],
                lengths[0],
                continued[0],
            )
            for model_index in range(models)
        ]
    )
    inner_width = gated.shape[2] * groups
    squares = jnp.sum(gated * gated, axis=2)
    unscaled = (gated * norm_gain[:, None, :]).astype(jnp.bfloat16)
    near_weight = ring_gather(ring_gather(out_weight, along_x, ROWS_X), along_z, chips_z)
    partner_weight, far_weight = lax.ppermute(
        (head_weight, near_weight), "req", [(i, i ^ 1) for i in range(shards)]
    )
    ring_weight = jnp.stack([near_weight, far_weight])
    ring_weight = jnp.roll(
        jnp.roll(jnp.roll(ring_weight.transpose(1, 2, 0, 3, 4, 5), z_index, axis=0), x_index, axis=1),
        core_index,
        axis=2,
    )
    full_weight = ring_weight.transpose(3, 4, 0, 1, 2, 5).reshape(
        models, out_weight.shape[1], shards * out_weight.shape[2]
    )
    partial_out = jnp.einsum(
        "mtc,mcd->mtd", unscaled, full_weight, preferred_element_type=jnp.float32
    )
    full_width = partial_out.shape[2]
    part_width = resid_in.shape[2]
    square_high = squares.astype(jnp.bfloat16)
    square_low = (squares - square_high.astype(jnp.float32)).astype(jnp.bfloat16)
    extra = (
        jnp.zeros(squares.shape + (SQUARE_COLUMNS,), jnp.bfloat16)
        .at[:, :, 0]
        .set(square_high)
        .at[:, :, 1]
        .set(square_low)
    )
    payload = jnp.concatenate([partial_out.astype(jnp.bfloat16), resid_in, extra], axis=2)
    pieces = lax.all_to_all(
        payload.reshape(models, groups, row_count, payload.shape[2]),
        "tp",
        split_axis=1,
        concat_axis=1,
        tiled=True,
    ).astype(jnp.float32)
    update = jnp.sum(pieces[:, :, :, :full_width], axis=1)
    total_squares = jnp.sum(
        pieces[:, :, :, full_width + part_width] + pieces[:, :, :, full_width + part_width + 1],
        axis=1,
    )
    scale = lax.rsqrt(total_squares / inner_width + EPSILON)
    resid_rows = (
        pieces[:, :, :, full_width : full_width + part_width]
        .transpose(0, 2, 1, 3)
        .reshape(models, row_count, groups * part_width)
    )
    hidden = (resid_rows + update * scale[:, :, None]).astype(jnp.bfloat16)
    full_width = hidden.shape[2]
    hidden_float = hidden.astype(jnp.float32)
    final_squares = jnp.sum(hidden_float * hidden_float, axis=2)
    final_rows = (
        hidden_float
        * lax.rsqrt(final_squares / full_width + EPSILON)[:, :, None]
        * final_gain[:, None, :]
    ).astype(jnp.bfloat16)
    own_target = lax.dynamic_slice_in_dim(targets, lane_index * row_count, row_count, 0)
    high_digit = (own_target // DIGIT).astype(jnp.bfloat16)
    low_digit = (own_target % DIGIT).astype(jnp.bfloat16)
    target_row = jnp.zeros((1, full_width), jnp.bfloat16)
    target_row = target_row.at[0, :row_count].set(high_digit)
    target_row = target_row.at[0, row_count : 2 * row_count].set(low_digit)
    packet = jnp.concatenate([final_rows.reshape(models * row_count, full_width), target_row], axis=0)

    every = ring_gather(ring_gather(packet, along_z, chips_z), along_x, ROWS_X)
    peers = ROWS_X * chips_z
    every = every.reshape(peers, models * row_count + 1, full_width)
    every_rows = (
        every[:, : models * row_count]
        .reshape(peers, models, row_count, full_width)
        .transpose(1, 0, 2, 3)
        .reshape(models, peers * row_count, full_width)
    )
    every_target = (
        every[:, models * row_count, :row_count].astype(jnp.int32) * DIGIT
        + every[:, models * row_count, row_count : 2 * row_count].astype(jnp.int32)
    ).reshape(peers * row_count)
    own_logits, own_peak, own_picked = head_scores(
        head_weight, shard_index * vocab_part, every_rows, every_target
    )
    other_logits, other_peak, other_picked = head_scores(
        partner_weight, (shard_index ^ 1) * vocab_part, every_rows, every_target
    )
    peak_logit = jnp.maximum(own_peak, other_peak)
    spread = jnp.sum(jnp.exp(own_logits - peak_logit[:, :, None]), axis=2) + jnp.sum(
        jnp.exp(other_logits - peak_logit[:, :, None]), axis=2
    )
    statistics = jnp.stack([peak_logit, spread, own_picked + other_picked])
    statistics = statistics.reshape(3, models, ROWS_X, chips_z, row_count).transpose(0, 1, 3, 2, 4)
    statistics = jnp.roll(jnp.roll(statistics, z_index, axis=2), x_index, axis=3)
    neutral = jnp.stack(
        [
            jnp.full_like(statistics[0], -1e30),
            jnp.zeros_like(statistics[1]),
            jnp.zeros_like(statistics[2]),
        ]
    )
    send = jnp.stack(
        [jnp.where(core_index == c, statistics, neutral) for c in range(CORES)], axis=4
    ).reshape(3, models, shards, row_count)
    received = lax.all_to_all(send, "req", split_axis=2, concat_axis=2, tiled=True)
    peak_each, spread_each, picked_each = received[0], received[1], received[2]
    peak_logit = jnp.max(peak_each, axis=1)
    spread = jnp.sum(spread_each * jnp.exp(peak_each - peak_logit[:, None, :]), axis=1)
    picked = jnp.sum(picked_each, axis=1)
    scored_rows = lax.dynamic_slice_in_dim(score_flag, lane_index * row_count, row_count, 0).astype(
        jnp.float32
    )
    return (picked - (peak_logit + jnp.log(spread))) * scored_rows[None, :]


def solution(mesh):
    placed = (
        P(None, "req", "tp"),
        P(None, "req", "tp"),
        P(None, "req", None),
        P(None, "req", "tp"),
        P(None, "req", "tp"),
        P(None, None, "tp"),
        P(),
        P(None, "tp"),
        P(None, "tp"),
        P(None, "tp"),
        P(None, "tp"),
        P(),
        P(None, "tp", "req"),
        P(None, "req", None),
        P(None, "req", None, "tp"),
        P(None, "req", None, None),
        P(None, "req", "tp", None),
        P("req", None),
        P("req", None),
        P("req"),
        P("req"),
    )
    return jax.shard_map(
        local, mesh=mesh, in_specs=placed, out_specs=P(None, ("req", "tp")), check_vma=False
    )
```
